32 devices in a mesh: dp: 8 (over y, x, core), tensor: 4 (over z).
Axes of the slice: x: 2, y: 2, z: 4, core: 2. Of those that a mesh axis runs over, the one named last changes fastest.
Arguments:
- tokens: bfloat16 [16384, 768], P(('dp', 'tensor')), may hold values from -6 to 6
- out_grad: bfloat16 [16384, 768], P(('dp', 'tensor')), may hold values from -6 to 6
- lengths: int32 [32], P('dp'), may hold values from 20 to 512, as said below
- qkv_weight: bfloat16 [3, 768, 768], P(None, None, 'tensor'), may hold values from -0.21875 to 0.21875
- qkv_bias: bfloat16 [2, 768], P(None, 'tensor'), may hold values from -3 to 3
- out_weight: bfloat16 [768, 768], P('tensor'), may hold values from -1.75 to 1.75
- out_bias: float32 [768], replicated, may hold values from -3 to 3
- norm1_gain: float32 [768], replicated, may hold values from 0.5 to 1.5
- norm1_shift: float32 [768], replicated, may hold values from -3 to 3
- up_weight: bfloat16 [768, 3072], P(None, 'tensor'), may hold values from -0.21875 to 0.21875
- up_bias: bfloat16 [3072], P('tensor'), may hold values from -3 to 3
- down_weight: bfloat16 [3072, 768], P('tensor'), may hold values from -0.109375 to 0.109375
- down_bias: float32 [768], replicated, may hold values from -3 to 3
- norm2_gain: float32 [768], replicated, may hold values from 0.5 to 1.5
- norm2_shift: float32 [768], replicated, may hold values from -3 to 3
Outputs:
- layer_out: bfloat16 [16384, 768], P(('dp', 'tensor'))
- input_grad: bfloat16 [16384, 768], P(('dp', 'tensor'))
- grad_qkv_weight: float32 [3, 768, 768], P(None, None, 'tensor')
- grad_qkv_bias: float32 [2, 768], P(None, 'tensor')
- grad_out_weight: float32 [768, 768], P('tensor')
- grad_out_bias: float32 [768], replicated
- grad_norm1_gain: float32 [768], replicated
- grad_norm1_shift: float32 [768], replicated
- grad_up_weight: float32 [768, 3072], P(None, 'tensor')
- grad_up_bias: float32 [3072], P('tensor')
- grad_down_weight: float32 [3072, 768], P('tensor')
- grad_down_bias: float32 [768], replicated
- grad_norm2_gain: float32 [768], replicated
- grad_norm2_shift: float32 [768], replicated
The draws below stay inside these ranges and needn't reach their ends.
Inputs may be any that keep to these rules, and one draw needn't show every extreme that they name: Keys at positions lengths[p] and beyond of passage p are padding; some passage has exactly 512 and some exactly 20.
All inputs are finite; a program needn't handle non-finite values.
Results may differ from the reference program's by a relative error of at most 0.02.
Values may be sent and summed in bfloat16 or wider, within the bound.
No kernel may reach another device: no remote copies, remote signals or barrier semaphores. Data moves between devices by JAX's collectives and lax.ppermute only.
A program may use at most 128 MiB of HBM per device.

```python
import jax
import jax.numpy as jnp
from jax import lax

D = 768
HEADS = 12
HD = 64
FF = 3072
LEN = 512
MIN_LEN = 20
PASS_DEV = 4
PASSAGES = 32
TOKENS = 16384


def draw_lengths(key, part):
    key_draw, key_long, key_short = jax.random.split(jax.random.fold_in(key, 17), 3)
    values = jax.random.randint(key_draw, (PASSAGES,), MIN_LEN, LEN + 1)
    longest = jax.random.randint(key_long, (), 0, PASSAGES)
    shortest = (longest + 1 + jax.random.randint(key_short, (), 0, PASSAGES - 1)) % PASSAGES
    values = values.at[longest].set(LEN).at[shortest].set(MIN_LEN)
    return values.astype(jnp.int32)


def level_of(stream_key, dims, cuts, smallest, largest):
    def one(position, shards_of):
        steps = jax.random.uniform(jax.random.fold_in(jax.random.fold_in(stream_key, 6), position), (shards_of,), jnp.float32, smallest / len(cuts), largest / len(cuts))
        return jnp.repeat(jnp.exp(steps), dims[position] // shards_of).reshape((-1,) + (1,) * (len(dims) - position - 1))

    factor_of = one(*cuts[0])
    for cut in cuts[1:]:
        factor_of = factor_of * one(*cut)
    return factor_of


def gaussian(key, dims, deviation, reach, cuts=(), kind=jnp.bfloat16):
    entries = deviation * jax.random.normal(key, dims, jnp.float32)
    if cuts:
        entries = entries * level_of(key, dims, cuts, -0.22, 0.18)
    return jnp.clip(entries, -reach, reach).astype(kind)


def setup_inputs(seed: int = 0) -> dict:
    keys = jax.random.split(jax.random.key(seed), 16)
    return {
        "tokens": gaussian(keys[0], (TOKENS, D), 1.0, 6.0, ((0, 32),)),
        "out_grad": gaussian(keys[1], (TOKENS, D), 1.0, 6.0, ((0, 32),)),
        "lengths": draw_lengths(jax.random.fold_in(keys[15], 71), 0),
        "qkv_weight": gaussian(keys[3], (3, D, D), D ** -0.5, 0.21875, ((2, 4),)),
        "qkv_bias": gaussian(keys[4], (2, D), 0.5, 3.0, ((1, 4),)),
        "out_weight": gaussian(keys[5], (D, D), (max(D * 8 // LEN, 1)) ** -0.5, 1.75, ((0, 4),)),
        "out_bias": gaussian(keys[6], (D,), 0.5, 3.0, (), jnp.float32),
        "norm1_gain": jnp.clip(1.0 + 0.1 * jax.random.normal(keys[7], (D,), jnp.float32), 0.5, 1.5),
        "norm1_shift": gaussian(keys[8], (D,), 0.5, 3.0, (), jnp.float32),
        "up_weight": gaussian(keys[9], (D, FF), D ** -0.5, 0.21875, ((1, 4),)),
        "up_bias": gaussian(keys[10], (FF,), 0.5, 3.0, ((0, 4),)),
        "down_weight": gaussian(keys[11], (FF, D), FF ** -0.5, 0.109375, ((0, 4),)),
        "down_bias": gaussian(keys[12], (D,), 0.5, 3.0, (), jnp.float32),
        "norm2_gain": jnp.clip(1.0 + 0.1 * jax.random.normal(keys[13], (D,), jnp.float32), 0.5, 1.5),
        "norm2_shift": gaussian(keys[14], (D,), 0.5, 3.0, (), jnp.float32),
    }


HIGH = lax.Precision.HIGHEST
EPS = 1e-12
NEG = -1e+30

@jax.custom_vjp
def low(v):
    return lax.optimization_barrier(v.astype(jnp.bfloat16)).astype(jnp.float32)

@jax.custom_vjp
def low_back(v):
    return v

def low_keep(v):
    return (low(v), None)

def low_pass(kept, grad):
    return (grad,)

def back_keep(v):
    return (v, None)

def back_low(kept, grad):
    return (low(grad),)
low.defvjp(low_keep, low_pass)
low_back.defvjp(back_keep, back_low)

def layer_norm(values, gain_vec, shift_vec):
    center = values - lax.optimization_barrier(jnp.mean(values, axis=-1, keepdims=True))
    spread = lax.optimization_barrier(jnp.mean(center * center, axis=-1, keepdims=True))
    return center * lax.rsqrt(spread + EPS) * gain_vec + shift_vec

def gelu_exact(values):
    return jax.nn.gelu(values, approximate=False)

def block_forward(inputs, params, usable):
    qkv_weight, qkv_bias, out_weight, out_bias, norm1_gain, norm1_shift, up_weight, up_bias, down_weight, down_bias, norm2_gain, norm2_shift = params
    row_total = inputs.shape[0]
    projected = jnp.einsum('rd,tde->tre', inputs, qkv_weight, precision=HIGH)
    queries = low_back(low(projected[0] + qkv_bias[0]))
    key_rows = low_back(low(projected[1]))
    value_rows = low_back(low(projected[2] + qkv_bias[1]))
    four_dims = (row_total // LEN, LEN, HEADS, HD)
    scores = jnp.einsum('pqhe,pkhe->phqk', queries.reshape(four_dims), key_rows.reshape(four_dims), precision=HIGH)
    scores = low_back(scores * HD ** (-0.5))
    scores = jnp.where(usable[:, None, None, :], scores, NEG)
    attn_probs = jnp.exp(scores - jax.nn.logsumexp(scores, axis=-1, keepdims=True))
    context = jnp.einsum('phqk,pkhe->pqhe', low(attn_probs), value_rows.reshape(four_dims), precision=HIGH)
    context = low_back(low(context.reshape(row_total, D)))
    attn = low_back(jnp.dot(context, out_weight, precision=HIGH) + out_bias)
    middle = layer_norm(inputs + attn, norm1_gain, norm1_shift)
    pre_act = low_back(jnp.dot(low(middle), up_weight, precision=HIGH) + up_bias)
    hidden = low(gelu_exact(pre_act))
    branch = low_back(jnp.dot(hidden, down_weight, precision=HIGH) + down_bias)
    return layer_norm(middle + branch, norm2_gain, norm2_shift)

def reference(tokens, out_grad, lengths, qkv_weight, qkv_bias, out_weight, out_bias, norm1_gain, norm1_shift, up_weight, up_bias, down_weight, down_bias, norm2_gain, norm2_shift):
    params = tuple((weight_item.astype(jnp.float32) for weight_item in (qkv_weight, qkv_bias, out_weight, out_bias, norm1_gain, norm1_shift, up_weight, up_bias, down_weight, down_bias, norm2_gain, norm2_shift)))
    group_rows = PASS_DEV * LEN
    groups = PASSAGES // PASS_DEV
    token_groups = tokens.astype(jnp.float32).reshape(groups, group_rows, D)
    grad_groups = out_grad.astype(jnp.float32).reshape(groups, group_rows, D)
    usable = jnp.arange(LEN, dtype=jnp.int32)[None, :] < lengths.astype(jnp.int32)[:, None]
    usable = usable.reshape(groups, PASS_DEV, LEN)

    def scan_step(totals, scan_inputs):
        rows_now, cotangent, key_mask = scan_inputs
        result, pullback = jax.vjp(lambda left, right: block_forward(left, right, key_mask), rows_now, params)
        grad_rows, grad_params = pullback(cotangent)
        totals = jax.tree.map(lambda left, right: left + right, totals, grad_params)
        return (totals, (result.astype(jnp.bfloat16), grad_rows.astype(jnp.bfloat16)))
    initial = jax.tree.map(jnp.zeros_like, params)
    summed, (outputs, grad_out_rows) = lax.scan(scan_step, initial, (token_groups, grad_groups, usable))
    return (outputs.reshape(TOKENS, D), grad_out_rows.reshape(TOKENS, D), summed[0], summed[1], summed[2], summed[3], summed[4], summed[5], summed[6], summed[7], summed[8], summed[9], summed[10], summed[11])
```

```python
import jax
import jax.numpy as jnp
from jax import lax
from jax.sharding import PartitionSpec as P

HD = 64
LEN = 512


EPS = 1e-12
NEG = -1e30


def layer_norm(values, gain_vec, shift_vec):
    center = values - jnp.mean(values, axis=-1, keepdims=True)
    spread = jnp.mean(center * center, axis=-1, keepdims=True)
    return center * lax.rsqrt(spread + EPS) * gain_vec + shift_vec


def gelu_exact(values):
    return jax.nn.gelu(values, approximate=False)


def contract(left, right, left_dim, right_dim):
    return lax.dot_general(
        left, right, (((left_dim,), (right_dim,)), ((), ())), preferred_element_type=jnp.float32
    )


def attend_forward(queries, key_rows, value_rows, usable, factor):
    scores = (
        jnp.einsum("pqhe,pkhe->phqk", queries, key_rows, preferred_element_type=jnp.float32)
        * factor
    )
    scores = jnp.where(usable[:, None, None, :], scores, NEG)
    log_total = jax.nn.logsumexp(scores, axis=-1, keepdims=True)
    attn_probs = jnp.exp(scores - log_total)
    context = jnp.einsum(
        "phqk,pkhe->pqhe",
        attn_probs.astype(jnp.bfloat16),
        value_rows,
        preferred_element_type=jnp.float32,
    )
    return context, attn_probs


def attend_backward(queries, key_rows, value_rows, attn_probs, context_grad, factor):
    prob_grad = jnp.einsum(
        "pqhe,pkhe->phqk", context_grad, value_rows, preferred_element_type=jnp.float32
    )
    row_dot = jnp.sum(prob_grad * attn_probs, axis=-1, keepdims=True)
    score_grad = (attn_probs * (prob_grad - row_dot)).astype(jnp.bfloat16)
    query_grad = (
        jnp.einsum("phqk,pkhe->pqhe", score_grad, key_rows, preferred_element_type=jnp.float32)
        * factor
    )
    key_grad = (
        jnp.einsum("phqk,pqhe->pkhe", score_grad, queries, preferred_element_type=jnp.float32)
        * factor
    )
    value_grad = jnp.einsum(
        "phqk,pqhe->pkhe",
        attn_probs.astype(jnp.bfloat16),
        context_grad,
        preferred_element_type=jnp.float32,
    )
    return query_grad, key_grad, value_grad


def dp_pow2(values, dp_size):
    steps = dp_size.bit_length() - 1
    return dp_size == 1 << steps and values.shape[0] % dp_size == 0


def dp_halve(values, dp_size):
    steps = dp_size.bit_length() - 1
    index = lax.axis_index("dp")
    kept = values
    for step in range(steps):
        bit = (index >> step) & 1
        half = kept.shape[0] // 2
        keep = lax.dynamic_slice_in_dim(kept, bit * half, half)
        give = lax.dynamic_slice_in_dim(kept, (1 - bit) * half, half)
        got = lax.ppermute(give, "dp", [(i, i ^ (1 << step)) for i in range(dp_size)])
        kept = keep + got
    return kept


def dp_double(kept, dp_size):
    steps = dp_size.bit_length() - 1
    index = lax.axis_index("dp")
    for step in reversed(range(steps)):
        bit = (index >> step) & 1
        got = lax.ppermute(kept, "dp", [(i, i ^ (1 << step)) for i in range(dp_size)])
        kept = jnp.where(bit == 0, jnp.concatenate([kept, got]), jnp.concatenate([got, kept]))
    return kept


def make_per_device(dp_size):
    def per_device(
        tokens,
        out_grad,
        lengths,
        qkv_weight,
        qkv_bias,
        out_weight,
        out_bias,
        norm1_gain,
        norm1_shift,
        up_weight,
        up_bias,
        down_weight,
        down_bias,
        norm2_gain,
        norm2_shift,
    ):
        rows, width = tokens.shape
        shard = qkv_weight.shape[2]
        groups = width // shard
        passages = rows // LEN
        heads = width // HD
        factor = HD ** (-0.5)

        packed_w = jnp.concatenate(
            [
                qkv_weight.reshape(3 * width, shard),
                out_weight.T,
                qkv_bias,
            ],
            axis=0,
        )
        w_rows = packed_w.shape[0]
        half_rows = -(-w_rows // 16) * 8
        packed_w = jnp.pad(packed_w, ((0, 2 * half_rows - w_rows), (0, 0)))
        dp_index = lax.axis_index("dp")
        parity = dp_index % 2
        mine = lax.dynamic_slice_in_dim(packed_w, parity * half_rows, half_rows)
        mine = lax.all_gather(mine, "tensor", axis=0, tiled=False)
        other = lax.ppermute(mine, "dp", [(i, i ^ 1) for i in range(dp_size)])
        first = jnp.where(parity == 0, mine, other)
        second = jnp.where(parity == 0, other, mine)
        weights_all = jnp.concatenate([first, second], axis=1)[:, :w_rows]
        qkv_blocks = weights_all[:, : 3 * width].reshape(groups, 3, width, shard)
        proj_blocks = weights_all[:, 3 * width : 4 * width]
        bias_full = weights_all[:, 4 * width :].transpose(1, 0, 2).reshape(2, width)

        tensor_index = lax.axis_index("tensor")
        own_lengths = lax.dynamic_slice_in_dim(lengths, tensor_index * passages, passages)
        usable = jnp.arange(LEN, dtype=jnp.int32)[None, :] < own_lengths[:, None]

        own_tokens = tokens.astype(jnp.float32)
        projected = jnp.einsum(
            "rd,gtdj->trgj", tokens, qkv_blocks, preferred_element_type=jnp.float32
        ).reshape(3, rows, width)
        four_dims = (passages, LEN, heads, HD)
        queries = (projected[0] + bias_full[0]).astype(jnp.bfloat16).reshape(four_dims)
        key_rows = projected[1].astype(jnp.bfloat16).reshape(four_dims)
        value_rows = (projected[2] + bias_full[1]).astype(jnp.bfloat16).reshape(four_dims)
        context, attn_probs = attend_forward(queries, key_rows, value_rows, usable, factor)
        context_low = context.reshape(rows, width).astype(jnp.bfloat16)
        attn_out = jnp.einsum(
            "rgj,gcj->rc",
            context_low.reshape(rows, groups, shard),
            proj_blocks,
            preferred_element_type=jnp.float32,
        )
        middle, norm1_back = jax.vjp(
            layer_norm, own_tokens + attn_out + out_bias, norm1_gain, norm1_shift
        )
        middle_low = middle.astype(jnp.bfloat16)
        ffn_rows = lax.all_gather(middle_low, "tensor", axis=0, tiled=True)
        pre_act = jnp.dot(ffn_rows, up_weight, preferred_element_type=jnp.float32) + up_bias
        activated, gelu_back = jax.vjp(gelu_exact, pre_act)
        hidden = activated.astype(jnp.bfloat16)
        ffn_out = lax.psum_scatter(
            jnp.dot(hidden, down_weight, preferred_element_type=jnp.float32).astype(jnp.bfloat16),
            "tensor",
            scatter_dimension=0,
            tiled=True,
        ).astype(jnp.float32)
        layer_out, norm2_back = jax.vjp(
            layer_norm, middle + ffn_out + down_bias, norm2_gain, norm2_shift
        )
        second_grad, grad_norm2_gain, grad_norm2_shift = norm2_back(out_grad.astype(jnp.float32))
        branch_grad = second_grad.astype(jnp.bfloat16)
        grad_down_bias = jnp.sum(branch_grad, axis=0, dtype=jnp.float32)
        branch_rows = lax.all_gather(branch_grad, "tensor", axis=0, tiled=True)
        hidden_grad = contract(branch_rows, down_weight, 1, 1)
        grad_down_weight = contract(hidden, branch_rows, 0, 0)
        pre_grad = gelu_back(hidden_grad)[0].astype(jnp.bfloat16)
        grad_up_bias = jnp.sum(pre_grad, axis=0, dtype=jnp.float32)
        grad_up_weight = contract(ffn_rows, pre_grad, 0, 0)
        ffn_grads = (grad_up_weight, grad_down_weight)
        halved = all(dp_pow2(g, dp_size) for g in ffn_grads)
        if halved:
            ffn_grads = tuple(dp_halve(g, dp_size) for g in ffn_grads)
        else:
            ffn_grads = lax.psum(ffn_grads, "dp")
        middle_part = lax.psum_scatter(
            contract(pre_grad, up_weight, 1, 1).astype(jnp.bfloat16),
            "tensor",
            scatter_dimension=0,
            tiled=True,
        ).astype(jnp.float32)
        norm1_in, ffn_grads = lax.optimization_barrier((second_grad + middle_part, ffn_grads))
        first_grad, grad_norm1_gain, grad_norm1_shift = norm1_back(norm1_in)
        attn_grad = first_grad.astype(jnp.bfloat16)
        grad_out_bias = jnp.sum(attn_grad, axis=0, dtype=jnp.float32)
        context_grad = (
            jnp.einsum("rc,gcj->rgj", attn_grad, proj_blocks, preferred_element_type=jnp.float32)
            .astype(jnp.bfloat16)
            .reshape(four_dims)
        )
        query_grad, key_grad, value_grad = attend_backward(
            queries, key_rows, value_rows, attn_probs, context_grad, factor
        )
        proj_grad = (
            jnp.stack([query_grad, key_grad, value_grad])
            .reshape(3, rows, width)
            .astype(jnp.bfloat16)
        )
        if halved:
            ffn_grads = tuple(dp_double(g, dp_size) for g in ffn_grads)
            proj_grad, ffn_grads = lax.optimization_barrier((proj_grad, ffn_grads))
        grad_up_weight, grad_down_weight = ffn_grads
        grad_bias_full = jnp.sum(proj_grad[0::2], axis=1, dtype=jnp.float32)
        grad_qkv_full = jnp.einsum(
            "rd,tre->tde", tokens, proj_grad, preferred_element_type=jnp.float32
        )
        input_part = jnp.einsum(
            "trgj,gtdj->rd",
            proj_grad.reshape(3, rows, groups, shard),
            qkv_blocks,
            preferred_element_type=jnp.float32,
        )
        input_grad = (first_grad + input_part).astype(jnp.bfloat16)

        small = jnp.stack(
            [
                grad_out_bias,
                grad_norm1_gain,
                grad_norm1_shift,
                grad_down_bias,
                grad_norm2_gain,
                grad_norm2_shift,
            ]
        )
        n_small = small.shape[0]
        small_rep = jnp.tile(small.reshape(n_small, groups, shard), (1, 1, groups)).reshape(
            n_small * groups, width
        )
        up_parts = grad_up_bias.shape[0] // shard
        own_group = (jnp.arange(width) // shard == tensor_index)[None, :]
        up_rep = jnp.where(
            own_group, jnp.tile(grad_up_bias.reshape(up_parts, shard), (1, groups)), 0.0
        )
        tail = jnp.concatenate([grad_bias_full, small_rep, up_rep], axis=0)
        tail_rows = tail.shape[0]
        unit = dp_size * 8
        tail = jnp.pad(tail, ((0, -(-tail_rows // unit) * unit - tail_rows), (0, 0)))
        early = lax.psum_scatter(
            jnp.concatenate([contract(attn_grad, context_low, 0, 0), tail], axis=0),
            "dp",
            scatter_dimension=0,
            tiled=True,
        )
        late = lax.psum_scatter(
            grad_qkv_full.reshape(3 * width, width), "dp", scatter_dimension=0, tiled=True
        )
        joined = jnp.concatenate([late, early], axis=0)
        joined = lax.psum_scatter(
            joined.reshape(joined.shape[0], groups, shard).transpose(1, 0, 2),
            "tensor",
            scatter_dimension=0,
            tiled=True,
        )[0]
        late_rows = late.shape[0]
        joined = lax.all_gather(joined, "dp", axis=0, tiled=False)
        early = joined[:, late_rows:].reshape(-1, shard)
        pieces = [joined[:, :late_rows].reshape(-1, shard), early[:width], early[width:]]
        grad_qkv_weight = pieces[0].reshape(3, width, shard)
        grad_out_weight = pieces[1].T
        tail = pieces[2]
        grad_qkv_bias = tail[:2]
        small_sum = tail[2 : 2 + n_small * groups].reshape(n_small, width)
        grad_up_bias = tail[2 + n_small * groups : 2 + n_small * groups + up_parts].reshape(-1)
        (
            grad_out_bias,
            grad_norm1_gain,
            grad_norm1_shift,
            grad_down_bias,
            grad_norm2_gain,
            grad_norm2_shift,
        ) = [small_sum[i] for i in range(n_small)]
        return (
            layer_out.astype(jnp.bfloat16),
            input_grad,
            grad_qkv_weight,
            grad_qkv_bias,
            grad_out_weight,
            grad_out_bias,
            grad_norm1_gain,
            grad_norm1_shift,
            grad_up_weight,
            grad_up_bias,
            grad_down_weight,
            grad_down_bias,
            grad_norm2_gain,
            grad_norm2_shift,
        )

    return per_device


def solution(mesh):
    placed = (
        P(("dp", "tensor"), None),
        P(("dp", "tensor"), None),
        P("dp"),
        P(None, None, "tensor"),
        P(None, "tensor"),
        P("tensor", None),
        P(),
        P(),
        P(),
        P(None, "tensor"),
        P("tensor"),
        P("tensor", None),
        P(),
        P(),
        P(),
    )
    return jax.shard_map(
        make_per_device(mesh.shape["dp"]),
        mesh=mesh,
        in_specs=placed,
        out_specs=(
            P(("dp", "tensor"), None),
            P(("dp", "tensor"), None),
            P(None, None, "tensor"),
            P(None, "tensor"),
            P("tensor", None),
            P(),
            P(),
            P(),
            P(None, "tensor"),
            P("tensor"),
            P("tensor", None),
            P(),
            P(),
            P(),
        ),
        check_vma=False,
    )
```

```python
import jax
import jax.numpy as jnp
from jax import lax
from jax.sharding import PartitionSpec as P

HD = 64
LEN = 512


EPS = 1e-12
NEG = -1e30


def layer_norm(values, gain_vec, shift_vec):
    center = values - jnp.mean(values, axis=-1, keepdims=True)
    spread = jnp.mean(center * center, axis=-1, keepdims=True)
    return center * lax.rsqrt(spread + EPS) * gain_vec + shift_vec


def gelu_exact(values):
    return jax.nn.gelu(values, approximate=False)


def contract(left, right, left_dim, right_dim):
    return lax.dot_general(
        left, right, (((left_dim,), (right_dim,)), ((), ())), preferred_element_type=jnp.float32
    )


def attend_forward(queries, key_rows, value_rows, usable, factor):
    scores = (
        jnp.einsum("pqhe,pkhe->phqk", queries, key_rows, preferred_element_type=jnp.float32)
        * factor
    )
    scores = jnp.where(usable[:, None, None, :], scores, NEG)
    log_total = jax.nn.logsumexp(scores, axis=-1, keepdims=True)
    attn_probs = jnp.exp(scores - log_total)
    context = jnp.einsum(
        "phqk,pkhe->pqhe",
        attn_probs.astype(jnp.bfloat16),
        value_rows,
        preferred_element_type=jnp.float32,
    )
    return context, attn_probs


def attend_backward(queries, key_rows, value_rows, attn_probs, context_grad, factor):
    prob_grad = jnp.einsum(
        "pqhe,pkhe->phqk", context_grad, value_rows, preferred_element_type=jnp.float32
    )
    row_dot = jnp.sum(prob_grad * attn_probs, axis=-1, keepdims=True)
    score_grad = (attn_probs * (prob_grad - row_dot)).astype(jnp.bfloat16)
    query_grad = (
        jnp.einsum("phqk,pkhe->pqhe", score_grad, key_rows, preferred_element_type=jnp.float32)
        * factor
    )
    key_grad = (
        jnp.einsum("phqk,pqhe->pkhe", score_grad, queries, preferred_element_type=jnp.float32)
        * factor
    )
    value_grad = jnp.einsum(
        "phqk,pqhe->pkhe",
        attn_probs.astype(jnp.bfloat16),
        context_grad,
        preferred_element_type=jnp.float32,
    )
    return query_grad, key_grad, value_grad


def dp_pow2(values, dp_size):
    steps = dp_size.bit_length() - 1
    return dp_size == 1 << steps and values.shape[0] % dp_size == 0


def dp_halve(values, dp_size):
    steps = dp_size.bit_length() - 1
    index = lax.axis_index("dp")
    kept = values
    for step in range(steps):
        bit = (index >> step) & 1
        half = kept.shape[0] // 2
        keep = lax.dynamic_slice_in_dim(kept, bit * half, half)
        give = lax.dynamic_slice_in_dim(kept, (1 - bit) * half, half)
        got = lax.ppermute(give, "dp", [(i, i ^ (1 << step)) for i in range(dp_size)])
        kept = keep + got
    return kept


def dp_double(kept, dp_size):
    steps = dp_size.bit_length() - 1
    index = lax.axis_index("dp")
    for step in reversed(range(steps)):
        bit = (index >> step) & 1
        got = lax.ppermute(kept, "dp", [(i, i ^ (1 << step)) for i in range(dp_size)])
        kept = jnp.where(bit == 0, jnp.concatenate([kept, got]), jnp.concatenate([got, kept]))
    return kept


def make_per_device(dp_size):
    def per_device(
        tokens,
        out_grad,
        lengths,
        qkv_weight,
        qkv_bias,
        out_weight,
        out_bias,
        norm1_gain,
        norm1_shift,
        up_weight,
        up_bias,
        down_weight,
        down_bias,
        norm2_gain,
        norm2_shift,
    ):
        rows, width = tokens.shape
        shard = qkv_weight.shape[2]
        groups = width // shard
        passages = rows // LEN
        heads = width // HD
        factor = HD ** (-0.5)

        packed_w = jnp.concatenate(
            [
                qkv_weight.reshape(3 * width, shard),
                out_weight.T,
                qkv_bias,
            ],
            axis=0,
        )
        w_rows = packed_w.shape[0]
        half_rows = -(-w_rows // 16) * 8
        packed_w = jnp.pad(packed_w, ((0, 2 * half_rows - w_rows), (0, 0)))
        dp_index = lax.axis_index("dp")
        parity = dp_index % 2
        mine = lax.dynamic_slice_in_dim(packed_w, parity * half_rows, half_rows)
        mine = lax.all_gather(mine, "tensor", axis=0, tiled=False)
        other = lax.ppermute(mine, "dp", [(i, i ^ 1) for i in range(dp_size)])
        first = jnp.where(parity == 0, mine, other)
        second = jnp.where(parity == 0, other, mine)
        weights_all = jnp.concatenate([first, second], axis=1)[:, :w_rows]
        qkv_blocks = weights_all[:, : 3 * width].reshape(groups, 3, width, shard)
        proj_blocks = weights_all[:, 3 * width : 4 * width]
        bias_full = weights_all[:, 4 * width :].transpose(1, 0, 2).reshape(2, width)

        tensor_index = lax.axis_index("tensor")
        own_lengths = lax.dynamic_slice_in_dim(lengths, tensor_index * passages, passages)
        usable = jnp.arange(LEN, dtype=jnp.int32)[None, :] < own_lengths[:, None]

        own_tokens = tokens.astype(jnp.float32)
        projected = jnp.einsum(
            "rd,gtdj->trgj", tokens, qkv_blocks, preferred_element_type=jnp.float32
        ).reshape(3, rows, width)
        four_dims = (passages, LEN, heads, HD)
        queries = (projected[0] + bias_full[0]).astype(jnp.bfloat16).reshape(four_dims)
        key_rows = projected[1].astype(jnp.bfloat16).reshape(four_dims)
        value_rows = (projected[2] + bias_full[1]).astype(jnp.bfloat16).reshape(four_dims)
        context, attn_probs = attend_forward(queries, key_rows, value_rows, usable, factor)
        context_low = context.reshape(rows, width).astype(jnp.bfloat16)
        attn_out = jnp.einsum(
            "rgj,gcj->rc",
            context_low.reshape(rows, groups, shard),
            proj_blocks,
            preferred_element_type=jnp.float32,
        )
        middle, norm1_back = jax.vjp(
            layer_norm, own_tokens + attn_out + out_bias, norm1_gain, norm1_shift
        )
        middle_low = middle.astype(jnp.bfloat16)
        ffn_rows = lax.all_gather(middle_low, "tensor", axis=0, tiled=True)
        pre_act = jnp.dot(ffn_rows, up_weight, preferred_element_type=jnp.float32) + up_bias
        activated, gelu_back = jax.vjp(gelu_exact, pre_act)
        hidden = activated.astype(jnp.bfloat16)
        ffn_out = lax.psum_scatter(
            jnp.dot(hidden, down_weight, preferred_element_type=jnp.float32).astype(jnp.bfloat16),
            "tensor",
            scatter_dimension=0,
            tiled=True,
        ).astype(jnp.float32)
        layer_out, norm2_back = jax.vjp(
            layer_norm, middle + ffn_out + down_bias, norm2_gain, norm2_shift
        )
        second_grad, grad_norm2_gain, grad_norm2_shift = norm2_back(out_grad.astype(jnp.float32))
        branch_grad = second_grad.astype(jnp.bfloat16)
        grad_down_bias = jnp.sum(branch_grad, axis=0, dtype=jnp.float32)
        branch_rows = lax.all_gather(branch_grad, "tensor", axis=0, tiled=True)
        hidden_grad = contract(branch_rows, down_weight, 1, 1)
        grad_down_weight = contract(hidden, branch_rows, 0, 0)
        pre_grad = gelu_back(hidden_grad)[0].astype(jnp.bfloat16)
        grad_up_bias = jnp.sum(pre_grad, axis=0, dtype=jnp.float32)
        grad_up_weight = contract(ffn_rows, pre_grad, 0, 0)
        ffn_grads = (grad_up_weight, grad_down_weight)
        halved = all(dp_pow2(g, dp_size) for g in ffn_grads)
        if halved:
            ffn_grads = tuple(dp_halve(g, dp_size) for g in ffn_grads)
        else:
            ffn_grads = lax.psum(ffn_grads, "dp")
        middle_part = lax.psum_scatter(
            contract(pre_grad, up_weight, 1, 1).astype(jnp.bfloat16),
            "tensor",
            scatter_dimension=0,
            tiled=True,
        ).astype(jnp.float32)
        norm1_in, ffn_grads = lax.optimization_barrier((second_grad + middle_part, ffn_grads))
        first_grad, grad_norm1_gain, grad_norm1_shift = norm1_back(norm1_in)
        attn_grad = first_grad.astype(jnp.bfloat16)
        grad_out_bias = jnp.sum(attn_grad, axis=0, dtype=jnp.float32)
        context_grad = (
            jnp.einsum("rc,gcj->rgj", attn_grad, proj_blocks, preferred_element_type=jnp.float32)
            .astype(jnp.bfloat16)
            .reshape(four_dims)
        )
        context_grad, early = lax.optimization_barrier(
            (context_grad, contract(attn_grad, context_low, 0, 0))
        )
        early = lax.psum_scatter(early, "dp", scatter_dimension=0, tiled=True)
        query_grad, key_grad, value_grad = attend_backward(
            queries, key_rows, value_rows, attn_probs, context_grad, factor
        )
        proj_grad = (
            jnp.stack([query_grad, key_grad, value_grad])
            .reshape(3, rows, width)
            .astype(jnp.bfloat16)
        )
        proj_grad, early = lax.optimization_barrier((proj_grad, early))
        grad_bias_full = jnp.sum(proj_grad[0::2], axis=1, dtype=jnp.float32)
        grad_qkv_full = jnp.einsum(
            "rd,tre->tde", tokens, proj_grad, preferred_element_type=jnp.float32
        )
        input_part = jnp.einsum(
            "trgj,gtdj->rd",
            proj_grad.reshape(3, rows, groups, shard),
            qkv_blocks,
            preferred_element_type=jnp.float32,
        )
        input_grad = (first_grad + input_part).astype(jnp.bfloat16)

        small = jnp.stack(
            [
                grad_out_bias,
                grad_norm1_gain,
                grad_norm1_shift,
                grad_down_bias,
                grad_norm2_gain,
                grad_norm2_shift,
            ]
        )
        n_small = small.shape[0]
        small_rep = jnp.tile(small.reshape(n_small, groups, shard), (1, 1, groups)).reshape(
            n_small * groups, width
        )
        up_parts = grad_up_bias.shape[0] // shard
        own_group = (jnp.arange(width) // shard == tensor_index)[None, :]
        up_rep = jnp.where(
            own_group, jnp.tile(grad_up_bias.reshape(up_parts, shard), (1, groups)), 0.0
        )
        tail = jnp.concatenate([grad_bias_full, small_rep, up_rep], axis=0)
        tail_rows = tail.shape[0]
        tail = jnp.pad(tail, ((0, -(-tail_rows // 8) * 8 - tail_rows), (0, 0)))
        late = lax.psum_scatter(
            grad_qkv_full.reshape(3 * width, width), "dp", scatter_dimension=0, tiled=True
        )
        joined = jnp.concatenate([late, early, tail], axis=0)
        if halved:
            ffn_grads = tuple(dp_double(g, dp_size) for g in ffn_grads)
            joined, ffn_grads = lax.optimization_barrier((joined, ffn_grads))
        grad_up_weight, grad_down_weight = ffn_grads
        joined = lax.psum_scatter(
            joined.reshape(joined.shape[0], groups, shard).transpose(1, 0, 2),
            "tensor",
            scatter_dimension=0,
            tiled=True,
        )[0]
        late_rows = late.shape[0]
        early_rows = early.shape[0]
        joined = lax.all_gather(joined, "dp", axis=0, tiled=False)
        pieces = [
            joined[:, :late_rows].reshape(-1, shard),
            joined[:, late_rows : late_rows + early_rows].reshape(-1, shard),
            jnp.sum(joined[:, late_rows + early_rows :], axis=0),
        ]
        grad_qkv_weight = pieces[0].reshape(3, width, shard)
        grad_out_weight = pieces[1].T
        tail = pieces[2]
        grad_qkv_bias = tail[:2]
        small_sum = tail[2 : 2 + n_small * groups].reshape(n_small, width)
        grad_up_bias = tail[2 + n_small * groups : 2 + n_small * groups + up_parts].reshape(-1)
        (
            grad_out_bias,
            grad_norm1_gain,
            grad_norm1_shift,
            grad_down_bias,
            grad_norm2_gain,
            grad_norm2_shift,
        ) = [small_sum[i] for i in range(n_small)]
        return (
            layer_out.astype(jnp.bfloat16),
            input_grad,
            grad_qkv_weight,
            grad_qkv_bias,
            grad_out_weight,
            grad_out_bias,
            grad_norm1_gain,
            grad_norm1_shift,
            grad_up_weight,
            grad_up_bias,
            grad_down_weight,
            grad_down_bias,
            grad_norm2_gain,
            grad_norm2_shift,
        )

    return per_device


def solution(mesh):
    placed = (
        P(("dp", "tensor"), None),
        P(("dp", "tensor"), None),
        P("dp"),
        P(None, None, "tensor"),
        P(None, "tensor"),
        P("tensor", None),
        P(),
        P(),
        P(),
        P(None, "tensor"),
        P("tensor"),
        P("tensor", None),
        P(),
        P(),
        P(),
    )
    return jax.shard_map(
        make_per_device(mesh.shape["dp"]),
        mesh=mesh,
        in_specs=placed,
        out_specs=(
            P(("dp", "tensor"), None),
            P(("dp", "tensor"), None),
            P(None, None, "tensor"),
            P(None, "tensor"),
            P("tensor", None),
            P(),
            P(),
            P(),
            P(None, "tensor"),
            P("tensor"),
            P("tensor", None),
            P(),
            P(),
            P(),
        ),
        check_vma=False,
    )
```

```python
import jax
import jax.numpy as jnp
from jax import lax
from jax.sharding import PartitionSpec as P

HD = 64
LEN = 512


EPS = 1e-12
NEG = -1e30


def layer_norm(values, gain_vec, shift_vec):
    center = values - jnp.mean(values, axis=-1, keepdims=True)
    spread = jnp.mean(center * center, axis=-1, keepdims=True)
    return center * lax.rsqrt(spread + EPS) * gain_vec + shift_vec


def gelu_exact(values):
    return jax.nn.gelu(values, approximate=False)


def contract(left, right, left_dim, right_dim):
    return lax.dot_general(
        left, right, (((left_dim,), (right_dim,)), ((), ())), preferred_element_type=jnp.float32
    )


def attend_forward(queries, key_rows, value_rows, usable, factor):
    scores = (
        jnp.einsum("pqhe,pkhe->phqk", queries, key_rows, preferred_element_type=jnp.float32)
        * factor
    )
    scores = jnp.where(usable[:, None, None, :], scores, NEG)
    log_total = jax.nn.logsumexp(scores, axis=-1, keepdims=True)
    attn_probs = jnp.exp(scores - log_total)
    context = jnp.einsum(
        "phqk,pkhe->pqhe",
        attn_probs.astype(jnp.bfloat16),
        value_rows,
        preferred_element_type=jnp.float32,
    )
    return context, attn_probs


def attend_backward(queries, key_rows, value_rows, attn_probs, context_grad, factor):
    prob_grad = jnp.einsum(
        "pqhe,pkhe->phqk", context_grad, value_rows, preferred_element_type=jnp.float32
    )
    row_dot = jnp.sum(prob_grad * attn_probs, axis=-1, keepdims=True)
    score_grad = (attn_probs * (prob_grad - row_dot)).astype(jnp.bfloat16)
    query_grad = (
        jnp.einsum("phqk,pkhe->pqhe", score_grad, key_rows, preferred_element_type=jnp.float32)
        * factor
    )
    key_grad = (
        jnp.einsum("phqk,pqhe->pkhe", score_grad, queries, preferred_element_type=jnp.float32)
        * factor
    )
    value_grad = jnp.einsum(
        "phqk,pqhe->pkhe",
        attn_probs.astype(jnp.bfloat16),
        context_grad,
        preferred_element_type=jnp.float32,
    )
    return query_grad, key_grad, value_grad


def dp_pow2(values, dp_size):
    steps = dp_size.bit_length() - 1
    return dp_size == 1 << steps and values.shape[0] % dp_size == 0


def dp_halve(values, dp_size):
    steps = dp_size.bit_length() - 1
    index = lax.axis_index("dp")
    kept = values
    for step in range(steps):
        bit = (index >> step) & 1
        half = kept.shape[0] // 2
        keep = lax.dynamic_slice_in_dim(kept, bit * half, half)
        give = lax.dynamic_slice_in_dim(kept, (1 - bit) * half, half)
        got = lax.ppermute(give, "dp", [(i, i ^ (1 << step)) for i in range(dp_size)])
        kept = keep + got
    return kept


def dp_double(kept, dp_size):
    steps = dp_size.bit_length() - 1
    index = lax.axis_index("dp")
    for step in reversed(range(steps)):
        bit = (index >> step) & 1
        got = lax.ppermute(kept, "dp", [(i, i ^ (1 << step)) for i in range(dp_size)])
        kept = jnp.where(bit == 0, jnp.concatenate([kept, got]), jnp.concatenate([got, kept]))
    return kept


def make_per_device(dp_size):
    def per_device(
        tokens,
        out_grad,
        lengths,
        qkv_weight,
        qkv_bias,
        out_weight,
        out_bias,
        norm1_gain,
        norm1_shift,
        up_weight,
        up_bias,
        down_weight,
        down_bias,
        norm2_gain,
        norm2_shift,
    ):
        rows, width = tokens.shape
        shard = qkv_weight.shape[2]
        groups = width // shard
        passages = rows // LEN
        heads = width // HD
        factor = HD ** (-0.5)

        packed_w = jnp.concatenate(
            [
                qkv_weight.reshape(3 * width, shard),
                out_weight.T,
                qkv_bias,
            ],
            axis=0,
        )
        w_rows = packed_w.shape[0]
        half_rows = -(-w_rows // 16) * 8
        packed_w = jnp.pad(packed_w, ((0, 2 * half_rows - w_rows), (0, 0)))
        dp_index = lax.axis_index("dp")
        parity = dp_index % 2
        mine = lax.dynamic_slice_in_dim(packed_w, parity * half_rows, half_rows)
        mine = lax.all_gather(mine, "tensor", axis=0, tiled=False)
        other = lax.ppermute(mine, "dp", [(i, i ^ 1) for i in range(dp_size)])
        first = jnp.where(parity == 0, mine, other)
        second = jnp.where(parity == 0, other, mine)
        weights_all = jnp.concatenate([first, second], axis=1)[:, :w_rows]
        qkv_blocks = weights_all[:, : 3 * width].reshape(groups, 3, width, shard)
        proj_blocks = weights_all[:, 3 * width : 4 * width]
        bias_full = weights_all[:, 4 * width :].transpose(1, 0, 2).reshape(2, width)

        tensor_index = lax.axis_index("tensor")
        own_lengths = lax.dynamic_slice_in_dim(lengths, tensor_index * passages, passages)
        usable = jnp.arange(LEN, dtype=jnp.int32)[None, :] < own_lengths[:, None]

        own_tokens = tokens.astype(jnp.float32)
        projected = jnp.einsum(
            "rd,gtdj->trgj", tokens, qkv_blocks, preferred_element_type=jnp.float32
        ).reshape(3, rows, width)
        four_dims = (passages, LEN, heads, HD)
        queries = (projected[0] + bias_full[0]).astype(jnp.bfloat16).reshape(four_dims)
        key_rows = projected[1].astype(jnp.bfloat16).reshape(four_dims)
        value_rows = (projected[2] + bias_full[1]).astype(jnp.bfloat16).reshape(four_dims)
        context, attn_probs = attend_forward(queries, key_rows, value_rows, usable, factor)
        context_low = context.reshape(rows, width).astype(jnp.bfloat16)
        attn_out = jnp.einsum(
            "rgj,gcj->rc",
            context_low.reshape(rows, groups, shard),
            proj_blocks,
            preferred_element_type=jnp.float32,
        )
        middle, norm1_back = jax.vjp(
            layer_norm, own_tokens + attn_out + out_bias, norm1_gain, norm1_shift
        )
        middle_low = middle.astype(jnp.bfloat16)
        ffn_rows = lax.all_gather(middle_low, "tensor", axis=0, tiled=True)
        pre_act = jnp.dot(ffn_rows, up_weight, preferred_element_type=jnp.float32) + up_bias
        activated, gelu_back = jax.vjp(gelu_exact, pre_act)
        hidden = activated.astype(jnp.bfloat16)
        ffn_out = lax.psum_scatter(
            jnp.dot(hidden, down_weight, preferred_element_type=jnp.float32).astype(jnp.bfloat16),
            "tensor",
            scatter_dimension=0,
            tiled=True,
        ).astype(jnp.float32)
        layer_out, norm2_back = jax.vjp(
            layer_norm, middle + ffn_out + down_bias, norm2_gain, norm2_shift
        )
        second_grad, grad_norm2_gain, grad_norm2_shift = norm2_back(out_grad.astype(jnp.float32))
        branch_grad = second_grad.astype(jnp.bfloat16)
        grad_down_bias = jnp.sum(branch_grad, axis=0, dtype=jnp.float32)
        branch_rows = lax.all_gather(branch_grad, "tensor", axis=0, tiled=True)
        hidden_grad = contract(branch_rows, down_weight, 1, 1)
        grad_down_weight = contract(hidden, branch_rows, 0, 0)
        pre_grad = gelu_back(hidden_grad)[0].astype(jnp.bfloat16)
        grad_up_bias = jnp.sum(pre_grad, axis=0, dtype=jnp.float32)
        grad_up_weight = contract(ffn_rows, pre_grad, 0, 0)
        ffn_grads = (grad_up_weight, grad_down_weight)
        halved = all(dp_pow2(g, dp_size) for g in ffn_grads)
        if halved:
            ffn_grads = tuple(dp_halve(g, dp_size) for g in ffn_grads)
        else:
            ffn_grads = lax.psum(ffn_grads, "dp")
        middle_part = lax.psum_scatter(
            contract(pre_grad, up_weight, 1, 1).astype(jnp.bfloat16),
            "tensor",
            scatter_dimension=0,
            tiled=True,
        ).astype(jnp.float32)
        norm1_in, ffn_grads = lax.optimization_barrier((second_grad + middle_part, ffn_grads))
        first_grad, grad_norm1_gain, grad_norm1_shift = norm1_back(norm1_in)
        attn_grad = first_grad.astype(jnp.bfloat16)
        grad_out_bias = jnp.sum(attn_grad, axis=0, dtype=jnp.float32)
        context_grad = (
            jnp.einsum("rc,gcj->rgj", attn_grad, proj_blocks, preferred_element_type=jnp.float32)
            .astype(jnp.bfloat16)
            .reshape(four_dims)
        )
        context_grad, early = lax.optimization_barrier(
            (context_grad, contract(attn_grad, context_low, 0, 0))
        )
        early = lax.psum_scatter(
            early.astype(jnp.bfloat16), "dp", scatter_dimension=0, tiled=True
        ).astype(jnp.float32)
        query_grad, key_grad, value_grad = attend_backward(
            queries, key_rows, value_rows, attn_probs, context_grad, factor
        )
        proj_grad = (
            jnp.stack([query_grad, key_grad, value_grad])
            .reshape(3, rows, width)
            .astype(jnp.bfloat16)
        )
        proj_grad, early = lax.optimization_barrier((proj_grad, early))
        grad_bias_full = jnp.sum(proj_grad[0::2], axis=1, dtype=jnp.float32)
        grad_qkv_full = jnp.einsum(
            "rd,tre->tde", tokens, proj_grad, preferred_element_type=jnp.float32
        )
        input_part = jnp.einsum(
            "trgj,gtdj->rd",
            proj_grad.reshape(3, rows, groups, shard),
            qkv_blocks,
            preferred_element_type=jnp.float32,
        )
        input_grad = (first_grad + input_part).astype(jnp.bfloat16)

        small = jnp.stack(
            [
                grad_out_bias,
                grad_norm1_gain,
                grad_norm1_shift,
                grad_down_bias,
                grad_norm2_gain,
                grad_norm2_shift,
            ]
        )
        n_small = small.shape[0]
        small_rep = jnp.tile(small.reshape(n_small, groups, shard), (1, 1, groups)).reshape(
            n_small * groups, width
        )
        up_parts = grad_up_bias.shape[0] // shard
        own_group = (jnp.arange(width) // shard == tensor_index)[None, :]
        up_rep = jnp.where(
            own_group, jnp.tile(grad_up_bias.reshape(up_parts, shard), (1, groups)), 0.0
        )
        tail = jnp.concatenate([grad_bias_full, small_rep, up_rep], axis=0)
        tail_rows = tail.shape[0]
        tail = jnp.pad(tail, ((0, -(-tail_rows // 8) * 8 - tail_rows), (0, 0)))
        late = lax.psum_scatter(
            grad_qkv_full.reshape(3 * width, width).astype(jnp.bfloat16),
            "dp",
            scatter_dimension=0,
            tiled=True,
        ).astype(jnp.float32)
        joined = jnp.concatenate([late, early, tail], axis=0)
        if halved:
            ffn_grads = tuple(dp_double(g, dp_size) for g in ffn_grads)
            joined, ffn_grads = lax.optimization_barrier((joined, ffn_grads))
        grad_up_weight, grad_down_weight = ffn_grads
        joined = lax.psum_scatter(
            joined.reshape(joined.shape[0], groups, shard).transpose(1, 0, 2),
            "tensor",
            scatter_dimension=0,
            tiled=True,
        )[0]
        late_rows = late.shape[0]
        early_rows = early.shape[0]
        joined = lax.all_gather(joined, "dp", axis=0, tiled=False)
        pieces = [
            joined[:, :late_rows].reshape(-1, shard),
            joined[:, late_rows : late_rows + early_rows].reshape(-1, shard),
            jnp.sum(joined[:, late_rows + early_rows :], axis=0),
        ]
        grad_qkv_weight = pieces[0].reshape(3, width, shard)
        grad_out_weight = pieces[1].T
        tail = pieces[2]
        grad_qkv_bias = tail[:2]
        small_sum = tail[2 : 2 + n_small * groups].reshape(n_small, width)
        grad_up_bias = tail[2 + n_small * groups : 2 + n_small * groups + up_parts].reshape(-1)
        (
            grad_out_bias,
            grad_norm1_gain,
            grad_norm1_shift,
            grad_down_bias,
            grad_norm2_gain,
            grad_norm2_shift,
        ) = [small_sum[i] for i in range(n_small)]
        return (
            layer_out.astype(jnp.bfloat16),
            input_grad,
            grad_qkv_weight,
            grad_qkv_bias,
            grad_out_weight,
            grad_out_bias,
            grad_norm1_gain,
            grad_norm1_shift,
            grad_up_weight,
            grad_up_bias,
            grad_down_weight,
            grad_down_bias,
            grad_norm2_gain,
            grad_norm2_shift,
        )

    return per_device


def solution(mesh):
    placed = (
        P(("dp", "tensor"), None),
        P(("dp", "tensor"), None),
        P("dp"),
        P(None, None, "tensor"),
        P(None, "tensor"),
        P("tensor", None),
        P(),
        P(),
        P(),
        P(None, "tensor"),
        P("tensor"),
        P("tensor", None),
        P(),
        P(),
        P(),
    )
    return jax.shard_map(
        make_per_device(mesh.shape["dp"]),
        mesh=mesh,
        in_specs=placed,
        out_specs=(
            P(("dp", "tensor"), None),
            P(("dp", "tensor"), None),
            P(None, None, "tensor"),
            P(None, "tensor"),
            P("tensor", None),
            P(),
            P(),
            P(),
            P(None, "tensor"),
            P("tensor"),
            P("tensor", None),
            P(),
            P(),
            P(),
        ),
        check_vma=False,
    )
```

```python
import jax
import jax.numpy as jnp
from jax import lax
from jax.sharding import PartitionSpec as P

HD = 64
LEN = 512


EPS = 1e-12
NEG = -1e30


def layer_norm(values, gain_vec, shift_vec):
    center = values - jnp.mean(values, axis=-1, keepdims=True)
    spread = jnp.mean(center * center, axis=-1, keepdims=True)
    return center * lax.rsqrt(spread + EPS) * gain_vec + shift_vec


def gelu_exact(values):
    return jax.nn.gelu(values, approximate=False)


def contract(left, right, left_dim, right_dim):
    return lax.dot_general(
        left, right, (((left_dim,), (right_dim,)), ((), ())), preferred_element_type=jnp.float32
    )


def attend_forward(queries, key_rows, value_rows, usable, factor):
    scores = (
        jnp.einsum("pqhe,pkhe->phqk", queries, key_rows, preferred_element_type=jnp.float32)
        * factor
    )
    scores = jnp.where(usable[:, None, None, :], scores, NEG)
    log_total = jax.nn.logsumexp(scores, axis=-1, keepdims=True)
    attn_probs = jnp.exp(scores - log_total)
    context = jnp.einsum(
        "phqk,pkhe->pqhe",
        attn_probs.astype(jnp.bfloat16),
        value_rows,
        preferred_element_type=jnp.float32,
    )
    return context, attn_probs


def attend_backward(queries, key_rows, value_rows, attn_probs, context_grad, factor):
    prob_grad = jnp.einsum(
        "pqhe,pkhe->phqk", context_grad, value_rows, preferred_element_type=jnp.float32
    )
    row_dot = jnp.sum(prob_grad * attn_probs, axis=-1, keepdims=True)
    score_grad = (attn_probs * (prob_grad - row_dot)).astype(jnp.bfloat16)
    query_grad = (
        jnp.einsum("phqk,pkhe->pqhe", score_grad, key_rows, preferred_element_type=jnp.float32)
        * factor
    )
    key_grad = (
        jnp.einsum("phqk,pqhe->pkhe", score_grad, queries, preferred_element_type=jnp.float32)
        * factor
    )
    value_grad = jnp.einsum(
        "phqk,pqhe->pkhe",
        attn_probs.astype(jnp.bfloat16),
        context_grad,
        preferred_element_type=jnp.float32,
    )
    return query_grad, key_grad, value_grad


def dp_pow2(values, dp_size):
    steps = dp_size.bit_length() - 1
    return dp_size == 1 << steps and values.shape[0] % dp_size == 0


def dp_halve(values, dp_size):
    steps = dp_size.bit_length() - 1
    index = lax.axis_index("dp")
    kept = values
    for step in range(steps):
        bit = (index >> step) & 1
        half = kept.shape[0] // 2
        keep = lax.dynamic_slice_in_dim(kept, bit * half, half)
        give = lax.dynamic_slice_in_dim(kept, (1 - bit) * half, half)
        got = lax.ppermute(give, "dp", [(i, i ^ (1 << step)) for i in range(dp_size)])
        kept = keep + got
    return kept


def dp_double(kept, dp_size):
    steps = dp_size.bit_length() - 1
    index = lax.axis_index("dp")
    for step in reversed(range(steps)):
        bit = (index >> step) & 1
        got = lax.ppermute(kept, "dp", [(i, i ^ (1 << step)) for i in range(dp_size)])
        kept = jnp.concatenate(
            [jnp.where(bit == 0, kept, got), jnp.where(bit == 0, got, kept)]
        )
    return kept


def make_per_device(dp_size):
    def per_device(
        tokens,
        out_grad,
        lengths,
        qkv_weight,
        qkv_bias,
        out_weight,
        out_bias,
        norm1_gain,
        norm1_shift,
        up_weight,
        up_bias,
        down_weight,
        down_bias,
        norm2_gain,
        norm2_shift,
    ):
        rows, width = tokens.shape
        shard = qkv_weight.shape[2]
        groups = width // shard
        passages = rows // LEN
        heads = width // HD
        factor = HD ** (-0.5)

        packed_w = jnp.concatenate(
            [
                qkv_weight.reshape(3 * width, shard),
                out_weight.T,
                qkv_bias,
            ],
            axis=0,
        )
        w_rows = packed_w.shape[0]
        half_rows = -(-w_rows // 16) * 8
        packed_w = jnp.pad(packed_w, ((0, 2 * half_rows - w_rows), (0, 0)))
        dp_index = lax.axis_index("dp")
        parity = dp_index % 2
        mine = lax.dynamic_slice_in_dim(packed_w, parity * half_rows, half_rows)
        mine = lax.all_gather(mine, "tensor", axis=0, tiled=False)
        other = lax.ppermute(mine, "dp", [(i, i ^ 1) for i in range(dp_size)])
        first = jnp.where(parity == 0, mine, other)
        second = jnp.where(parity == 0, other, mine)
        weights_all = jnp.concatenate([first, second], axis=1)[:, :w_rows]
        qkv_blocks = weights_all[:, : 3 * width].reshape(groups, 3, width, shard)
        proj_blocks = weights_all[:, 3 * width : 4 * width]
        bias_full = weights_all[:, 4 * width :].transpose(1, 0, 2).reshape(2, width)

        tensor_index = lax.axis_index("tensor")
        own_lengths = lax.dynamic_slice_in_dim(lengths, tensor_index * passages, passages)
        usable = jnp.arange(LEN, dtype=jnp.int32)[None, :] < own_lengths[:, None]

        own_tokens = tokens.astype(jnp.float32)
        projected = jnp.einsum(
            "rd,gtdj->trgj", tokens, qkv_blocks, preferred_element_type=jnp.float32
        ).reshape(3, rows, width)
        four_dims = (passages, LEN, heads, HD)
        queries = (projected[0] + bias_full[0]).astype(jnp.bfloat16).reshape(four_dims)
        key_rows = projected[1].astype(jnp.bfloat16).reshape(four_dims)
        value_rows = (projected[2] + bias_full[1]).astype(jnp.bfloat16).reshape(four_dims)
        context, attn_probs = attend_forward(queries, key_rows, value_rows, usable, factor)
        context_low = context.reshape(rows, width).astype(jnp.bfloat16)
        attn_out = jnp.einsum(
            "rgj,gcj->rc",
            context_low.reshape(rows, groups, shard),
            proj_blocks,
            preferred_element_type=jnp.float32,
        )
        middle, norm1_back = jax.vjp(
            layer_norm, own_tokens + attn_out + out_bias, norm1_gain, norm1_shift
        )
        middle_low = middle.astype(jnp.bfloat16)
        ffn_rows = lax.all_gather(middle_low, "tensor", axis=0, tiled=True)
        pre_act = jnp.dot(ffn_rows, up_weight, preferred_element_type=jnp.float32) + up_bias
        activated, gelu_back = jax.vjp(gelu_exact, pre_act)
        hidden = activated.astype(jnp.bfloat16)
        ffn_out = lax.psum_scatter(
            jnp.dot(hidden, down_weight, preferred_element_type=jnp.float32).astype(jnp.bfloat16),
            "tensor",
            scatter_dimension=0,
            tiled=True,
        ).astype(jnp.float32)
        layer_out, norm2_back = jax.vjp(
            layer_norm, middle + ffn_out + down_bias, norm2_gain, norm2_shift
        )
        second_grad, grad_norm2_gain, grad_norm2_shift = norm2_back(out_grad.astype(jnp.float32))
        branch_grad = second_grad.astype(jnp.bfloat16)
        grad_down_bias = jnp.sum(branch_grad, axis=0, dtype=jnp.float32)
        branch_rows = lax.all_gather(branch_grad, "tensor", axis=0, tiled=True)
        hidden_grad = contract(branch_rows, down_weight, 1, 1)
        grad_down_weight = contract(hidden, branch_rows, 0, 0)
        pre_grad = gelu_back(hidden_grad)[0].astype(jnp.bfloat16)
        grad_up_bias = jnp.sum(pre_grad, axis=0, dtype=jnp.float32)
        grad_up_weight = contract(ffn_rows, pre_grad, 0, 0)
        ffn_grads = (grad_up_weight, grad_down_weight)
        halved = all(dp_pow2(g, dp_size) for g in ffn_grads)
        if halved:
            ffn_grads = tuple(dp_halve(g, dp_size) for g in ffn_grads)
        else:
            ffn_grads = lax.psum(ffn_grads, "dp")
        middle_part = lax.psum_scatter(
            contract(pre_grad, up_weight, 1, 1).astype(jnp.bfloat16),
            "tensor",
            scatter_dimension=0,
            tiled=True,
        ).astype(jnp.float32)
        norm1_in, ffn_grads = lax.optimization_barrier((second_grad + middle_part, ffn_grads))
        first_grad, grad_norm1_gain, grad_norm1_shift = norm1_back(norm1_in)
        attn_grad = first_grad.astype(jnp.bfloat16)
        grad_out_bias = jnp.sum(attn_grad, axis=0, dtype=jnp.float32)
        context_grad = (
            jnp.einsum("rc,gcj->rgj", attn_grad, proj_blocks, preferred_element_type=jnp.float32)
            .astype(jnp.bfloat16)
            .reshape(four_dims)
        )
        context_grad, early = lax.optimization_barrier(
            (context_grad, contract(attn_grad, context_low, 0, 0))
        )
        early = lax.psum_scatter(
            early.astype(jnp.bfloat16), "dp", scatter_dimension=0, tiled=True
        ).astype(jnp.float32)
        query_grad, key_grad, value_grad = attend_backward(
            queries, key_rows, value_rows, attn_probs, context_grad, factor
        )
        proj_grad = (
            jnp.stack([query_grad, key_grad, value_grad])
            .reshape(3, rows, width)
            .astype(jnp.bfloat16)
        )
        grad_bias_full = jnp.sum(proj_grad[0::2], axis=1, dtype=jnp.float32)
        grad_qkv_full = jnp.einsum(
            "rd,tre->tde", tokens, proj_grad, preferred_element_type=jnp.float32
        )
        input_part = jnp.einsum(
            "trgj,gtdj->rd",
            proj_grad.reshape(3, rows, groups, shard),
            qkv_blocks,
            preferred_element_type=jnp.float32,
        )
        input_grad = (first_grad + input_part).astype(jnp.bfloat16)

        small = jnp.stack(
            [
                grad_out_bias,
                grad_norm1_gain,
                grad_norm1_shift,
                grad_down_bias,
                grad_norm2_gain,
                grad_norm2_shift,
            ]
        )
        n_small = small.shape[0]
        small_rep = jnp.tile(small.reshape(n_small, groups, shard), (1, 1, groups)).reshape(
            n_small * groups, width
        )
        up_parts = grad_up_bias.shape[0] // shard
        own_group = (jnp.arange(width) // shard == tensor_index)[None, :]
        up_rep = jnp.where(
            own_group, jnp.tile(grad_up_bias.reshape(up_parts, shard), (1, groups)), 0.0
        )
        tail = jnp.concatenate([grad_bias_full, small_rep, up_rep], axis=0)
        tail_rows = tail.shape[0]
        tail = jnp.pad(tail, ((0, -(-tail_rows // 8) * 8 - tail_rows), (0, 0)))
        late = lax.psum_scatter(
            grad_qkv_full.reshape(3 * width, width).astype(jnp.bfloat16),
            "dp",
            scatter_dimension=0,
            tiled=True,
        ).astype(jnp.float32)
        joined = jnp.concatenate([late, early, tail], axis=0)
        joined = lax.psum_scatter(
            joined.reshape(joined.shape[0], groups, shard).transpose(1, 0, 2),
            "tensor",
            scatter_dimension=0,
            tiled=True,
        )[0]
        if halved:
            ffn_grads = tuple(
                dp_double(g.astype(jnp.bfloat16), dp_size).astype(jnp.float32) for g in ffn_grads
            )
            joined, ffn_grads = lax.optimization_barrier((joined, ffn_grads))
        grad_up_weight, grad_down_weight = ffn_grads
        late_rows = late.shape[0]
        early_rows = early.shape[0]
        joined = lax.all_gather(joined, "dp", axis=0, tiled=False)
        pieces = [
            joined[:, :late_rows].reshape(-1, shard),
            joined[:, late_rows : late_rows + early_rows].reshape(-1, shard),
            jnp.sum(joined[:, late_rows + early_rows :], axis=0),
        ]
        grad_qkv_weight = pieces[0].reshape(3, width, shard)
        grad_out_weight = pieces[1].T
        tail = pieces[2]
        grad_qkv_bias = tail[:2]
        small_sum = tail[2 : 2 + n_small * groups].reshape(n_small, width)
        grad_up_bias = tail[2 + n_small * groups : 2 + n_small * groups + up_parts].reshape(-1)
        (
            grad_out_bias,
            grad_norm1_gain,
            grad_norm1_shift,
            grad_down_bias,
            grad_norm2_gain,
            grad_norm2_shift,
        ) = [small_sum[i] for i in range(n_small)]
        return (
            layer_out.astype(jnp.bfloat16),
            input_grad,
            grad_qkv_weight,
            grad_qkv_bias,
            grad_out_weight,
            grad_out_bias,
            grad_norm1_gain,
            grad_norm1_shift,
            grad_up_weight,
            grad_up_bias,
            grad_down_weight,
            grad_down_bias,
            grad_norm2_gain,
            grad_norm2_shift,
        )

    return per_device


def solution(mesh):
    placed = (
        P(("dp", "tensor"), None),
        P(("dp", "tensor"), None),
        P("dp"),
        P(None, None, "tensor"),
        P(None, "tensor"),
        P("tensor", None),
        P(),
        P(),
        P(),
        P(None, "tensor"),
        P("tensor"),
        P("tensor", None),
        P(),
        P(),
        P(),
    )
    return jax.shard_map(
        make_per_device(mesh.shape["dp"]),
        mesh=mesh,
        in_specs=placed,
        out_specs=(
            P(("dp", "tensor"), None),
            P(("dp", "tensor"), None),
            P(None, None, "tensor"),
            P(None, "tensor"),
            P("tensor", None),
            P(),
            P(),
            P(),
            P(None, "tensor"),
            P("tensor"),
            P("tensor", None),
            P(),
            P(),
            P(),
        ),
        check_vma=False,
    )
```

```python
import jax
import jax.numpy as jnp
from jax import lax
from jax.sharding import PartitionSpec as P

HD = 64
LEN = 512


EPS = 1e-12
NEG = -1e30


def layer_norm(values, gain_vec, shift_vec):
    center = values - jnp.mean(values, axis=-1, keepdims=True)
    spread = jnp.mean(center * center, axis=-1, keepdims=True)
    return center * lax.rsqrt(spread + EPS) * gain_vec + shift_vec


def gelu_exact(values):
    return jax.nn.gelu(values, approximate=False)


def contract(left, right, left_dim, right_dim):
    return lax.dot_general(
        left, right, (((left_dim,), (right_dim,)), ((), ())), preferred_element_type=jnp.float32
    )


def attend_forward(queries, key_rows, value_rows, usable, factor):
    scores = (
        jnp.einsum("pqhe,pkhe->phqk", queries, key_rows, preferred_element_type=jnp.float32)
        * factor
    )
    scores = jnp.where(usable[:, None, None, :], scores, NEG)
    log_total = jax.nn.logsumexp(scores, axis=-1, keepdims=True)
    attn_probs = jnp.exp(scores - log_total)
    context = jnp.einsum(
        "phqk,pkhe->pqhe",
        attn_probs.astype(jnp.bfloat16),
        value_rows,
        preferred_element_type=jnp.float32,
    )
    return context, attn_probs


def attend_backward(queries, key_rows, value_rows, attn_probs, context_grad, factor):
    prob_grad = jnp.einsum(
        "pqhe,pkhe->phqk", context_grad, value_rows, preferred_element_type=jnp.float32
    )
    row_dot = jnp.sum(prob_grad * attn_probs, axis=-1, keepdims=True)
    score_grad = (attn_probs * (prob_grad - row_dot)).astype(jnp.bfloat16)
    query_grad = (
        jnp.einsum("phqk,pkhe->pqhe", score_grad, key_rows, preferred_element_type=jnp.float32)
        * factor
    )
    key_grad = (
        jnp.einsum("phqk,pqhe->pkhe", score_grad, queries, preferred_element_type=jnp.float32)
        * factor
    )
    value_grad = jnp.einsum(
        "phqk,pqhe->pkhe",
        attn_probs.astype(jnp.bfloat16),
        context_grad,
        preferred_element_type=jnp.float32,
    )
    return query_grad, key_grad, value_grad


def dp_pow2(values, dp_size):
    steps = dp_size.bit_length() - 1
    return dp_size == 1 << steps and values.shape[0] % dp_size == 0


def dp_halve(values, dp_size, sum_dtype=None):
    steps = dp_size.bit_length() - 1
    index = lax.axis_index("dp")
    link = values.dtype
    kept = values if sum_dtype is None else values.astype(sum_dtype)
    for step in range(steps):
        bit = (index >> step) & 1
        half = kept.shape[0] // 2
        keep = lax.dynamic_slice_in_dim(kept, bit * half, half)
        give = lax.dynamic_slice_in_dim(kept, (1 - bit) * half, half).astype(link)
        got = lax.ppermute(give, "dp", [(i, i ^ (1 << step)) for i in range(dp_size)])
        kept = keep + got.astype(kept.dtype)
    return kept


def bit_reversed(count):
    steps = count.bit_length() - 1
    return [int(format(i, f"0{steps}b")[::-1], 2) if steps else 0 for i in range(count)]


def dp_double(kept, dp_size):
    steps = dp_size.bit_length() - 1
    index = lax.axis_index("dp")
    for step in reversed(range(steps)):
        bit = (index >> step) & 1
        got = lax.ppermute(kept, "dp", [(i, i ^ (1 << step)) for i in range(dp_size)])
        kept = jnp.concatenate(
            [jnp.where(bit == 0, kept, got), jnp.where(bit == 0, got, kept)]
        )
    return kept


def make_per_device(dp_size):
    def per_device(
        tokens,
        out_grad,
        lengths,
        qkv_weight,
        qkv_bias,
        out_weight,
        out_bias,
        norm1_gain,
        norm1_shift,
        up_weight,
        up_bias,
        down_weight,
        down_bias,
        norm2_gain,
        norm2_shift,
    ):
        rows, width = tokens.shape
        shard = qkv_weight.shape[2]
        groups = width // shard
        passages = rows // LEN
        heads = width // HD
        factor = HD ** (-0.5)

        packed_w = jnp.concatenate(
            [
                qkv_weight.reshape(3 * width, shard),
                out_weight.T,
                qkv_bias,
            ],
            axis=0,
        )
        w_rows = packed_w.shape[0]
        half_rows = -(-w_rows // 16) * 8
        packed_w = jnp.pad(packed_w, ((0, 2 * half_rows - w_rows), (0, 0)))
        dp_index = lax.axis_index("dp")
        parity = dp_index % 2
        mine = lax.dynamic_slice_in_dim(packed_w, parity * half_rows, half_rows)
        mine = lax.all_gather(mine, "tensor", axis=0, tiled=False)
        other = lax.ppermute(mine, "dp", [(i, i ^ 1) for i in range(dp_size)])
        first = jnp.where(parity == 0, mine, other)
        second = jnp.where(parity == 0, other, mine)
        weights_all = jnp.concatenate([first, second], axis=1)[:, :w_rows]
        qkv_blocks = weights_all[:, : 3 * width].reshape(groups, 3, width, shard)
        proj_blocks = weights_all[:, 3 * width : 4 * width]
        bias_full = weights_all[:, 4 * width :].transpose(1, 0, 2).reshape(2, width)

        tensor_index = lax.axis_index("tensor")
        own_lengths = lax.dynamic_slice_in_dim(lengths, tensor_index * passages, passages)
        usable = jnp.arange(LEN, dtype=jnp.int32)[None, :] < own_lengths[:, None]

        own_tokens = tokens.astype(jnp.float32)
        projected = jnp.einsum(
            "rd,gtdj->trgj", tokens, qkv_blocks, preferred_element_type=jnp.float32
        ).reshape(3, rows, width)
        four_dims = (passages, LEN, heads, HD)
        queries = (projected[0] + bias_full[0]).astype(jnp.bfloat16).reshape(four_dims)
        key_rows = projected[1].astype(jnp.bfloat16).reshape(four_dims)
        value_rows = (projected[2] + bias_full[1]).astype(jnp.bfloat16).reshape(four_dims)
        context, attn_probs = attend_forward(queries, key_rows, value_rows, usable, factor)
        context_low = context.reshape(rows, width).astype(jnp.bfloat16)
        attn_out = jnp.einsum(
            "rgj,gcj->rc",
            context_low.reshape(rows, groups, shard),
            proj_blocks,
            preferred_element_type=jnp.float32,
        )
        middle, norm1_back = jax.vjp(
            layer_norm, own_tokens + attn_out + out_bias, norm1_gain, norm1_shift
        )
        middle_low = middle.astype(jnp.bfloat16)
        ffn_rows = lax.all_gather(middle_low, "tensor", axis=0, tiled=True)
        pre_act = jnp.dot(ffn_rows, up_weight, preferred_element_type=jnp.float32) + up_bias
        activated, gelu_back = jax.vjp(gelu_exact, pre_act)
        hidden = activated.astype(jnp.bfloat16)
        ffn_out = lax.psum_scatter(
            jnp.dot(hidden, down_weight, preferred_element_type=jnp.float32).astype(jnp.bfloat16),
            "tensor",
            scatter_dimension=0,
            tiled=True,
        ).astype(jnp.float32)
        layer_out, norm2_back = jax.vjp(
            layer_norm, middle + ffn_out + down_bias, norm2_gain, norm2_shift
        )
        second_grad, grad_norm2_gain, grad_norm2_shift = norm2_back(out_grad.astype(jnp.float32))
        branch_grad = second_grad.astype(jnp.bfloat16)
        grad_down_bias = jnp.sum(branch_grad, axis=0, dtype=jnp.float32)
        branch_rows = lax.all_gather(branch_grad, "tensor", axis=0, tiled=True)
        hidden_grad = contract(branch_rows, down_weight, 1, 1)
        grad_down_weight = contract(hidden, branch_rows, 0, 0)
        pre_grad = gelu_back(hidden_grad)[0].astype(jnp.bfloat16)
        grad_up_bias = jnp.sum(pre_grad, axis=0, dtype=jnp.float32)
        grad_up_weight = contract(ffn_rows, pre_grad, 0, 0)
        ffn_grads = (grad_up_weight, grad_down_weight)
        halved = all(dp_pow2(g, dp_size) for g in ffn_grads)
        if halved:
            ffn_grads = tuple(dp_halve(g, dp_size) for g in ffn_grads)
        else:
            ffn_grads = lax.psum(ffn_grads, "dp")
        middle_part = lax.psum_scatter(
            contract(pre_grad, up_weight, 1, 1).astype(jnp.bfloat16),
            "tensor",
            scatter_dimension=0,
            tiled=True,
        ).astype(jnp.float32)
        norm1_in, ffn_grads = lax.optimization_barrier((second_grad + middle_part, ffn_grads))
        first_grad, grad_norm1_gain, grad_norm1_shift = norm1_back(norm1_in)
        attn_grad = first_grad.astype(jnp.bfloat16)
        grad_out_bias = jnp.sum(attn_grad, axis=0, dtype=jnp.float32)
        context_grad = (
            jnp.einsum("rc,gcj->rgj", attn_grad, proj_blocks, preferred_element_type=jnp.float32)
            .astype(jnp.bfloat16)
            .reshape(four_dims)
        )
        early = contract(attn_grad, context_low, 0, 0)
        early_halved = dp_pow2(early, dp_size)
        if early_halved:
            early = dp_halve(early.astype(jnp.bfloat16), dp_size, jnp.float32)
        else:
            early = lax.psum_scatter(early, "dp", scatter_dimension=0, tiled=True)
        query_grad, key_grad, value_grad = attend_backward(
            queries, key_rows, value_rows, attn_probs, context_grad, factor
        )
        proj_grad = (
            jnp.stack([query_grad, key_grad, value_grad])
            .reshape(3, rows, width)
            .astype(jnp.bfloat16)
        )
        grad_bias_full = jnp.sum(proj_grad[0::2], axis=1, dtype=jnp.float32)
        grad_qkv_full = jnp.einsum(
            "rd,tre->tde", tokens, proj_grad, preferred_element_type=jnp.float32
        )
        input_part = jnp.einsum(
            "trgj,gtdj->rd",
            proj_grad.reshape(3, rows, groups, shard),
            qkv_blocks,
            preferred_element_type=jnp.float32,
        )
        input_grad = (first_grad + input_part).astype(jnp.bfloat16)

        small = jnp.stack(
            [
                grad_out_bias,
                grad_norm1_gain,
                grad_norm1_shift,
                grad_down_bias,
                grad_norm2_gain,
                grad_norm2_shift,
            ]
        )
        n_small = small.shape[0]
        small_rep = jnp.tile(small.reshape(n_small, groups, shard), (1, 1, groups)).reshape(
            n_small * groups, width
        )
        up_parts = grad_up_bias.shape[0] // shard
        own_group = (jnp.arange(width) // shard == tensor_index)[None, :]
        up_rep = jnp.where(
            own_group, jnp.tile(grad_up_bias.reshape(up_parts, shard), (1, groups)), 0.0
        )
        tail = jnp.concatenate([grad_bias_full, small_rep, up_rep], axis=0)
        tail_rows = tail.shape[0]
        tail = jnp.pad(tail, ((0, -(-tail_rows // 8) * 8 - tail_rows), (0, 0)))
        late = lax.psum_scatter(
            grad_qkv_full.reshape(3 * width, width).astype(jnp.bfloat16),
            "dp",
            scatter_dimension=0,
            tiled=True,
        ).astype(jnp.float32)
        joined = jnp.concatenate([late, early, tail], axis=0)
        joined = lax.psum_scatter(
            joined.reshape(joined.shape[0], groups, shard).transpose(1, 0, 2),
            "tensor",
            scatter_dimension=0,
            tiled=True,
        )[0]
        if halved:
            ffn_grads = tuple(
                dp_double(g.astype(jnp.bfloat16), dp_size).astype(jnp.float32) for g in ffn_grads
            )
            joined, ffn_grads = lax.optimization_barrier((joined, ffn_grads))
        grad_up_weight, grad_down_weight = ffn_grads
        late_rows = late.shape[0]
        early_rows = early.shape[0]
        joined = lax.all_gather(joined, "dp", axis=0, tiled=False)
        early = joined[:, late_rows : late_rows + early_rows]
        if early_halved:
            order = bit_reversed(dp_size)
            place = [order.index(b) for b in range(dp_size)]
            early = jnp.concatenate([early[p] for p in place], axis=0)
        pieces = [
            joined[:, :late_rows].reshape(-1, shard),
            early.reshape(-1, shard),
            jnp.sum(joined[:, late_rows + early_rows :], axis=0),
        ]
        grad_qkv_weight = pieces[0].reshape(3, width, shard)
        grad_out_weight = pieces[1].T
        tail = pieces[2]
        grad_qkv_bias = tail[:2]
        small_sum = tail[2 : 2 + n_small * groups].reshape(n_small, width)
        grad_up_bias = tail[2 + n_small * groups : 2 + n_small * groups + up_parts].reshape(-1)
        (
            grad_out_bias,
            grad_norm1_gain,
            grad_norm1_shift,
            grad_down_bias,
            grad_norm2_gain,
            grad_norm2_shift,
        ) = [small_sum[i] for i in range(n_small)]
        return (
            layer_out.astype(jnp.bfloat16),
            input_grad,
            grad_qkv_weight,
            grad_qkv_bias,
            grad_out_weight,
            grad_out_bias,
            grad_norm1_gain,
            grad_norm1_shift,
            grad_up_weight,
            grad_up_bias,
            grad_down_weight,
            grad_down_bias,
            grad_norm2_gain,
            grad_norm2_shift,
        )

    return per_device


def solution(mesh):
    placed = (
        P(("dp", "tensor"), None),
        P(("dp", "tensor"), None),
        P("dp"),
        P(None, None, "tensor"),
        P(None, "tensor"),
        P("tensor", None),
        P(),
        P(),
        P(),
        P(None, "tensor"),
        P("tensor"),
        P("tensor", None),
        P(),
        P(),
        P(),
    )
    return jax.shard_map(
        make_per_device(mesh.shape["dp"]),
        mesh=mesh,
        in_specs=placed,
        out_specs=(
            P(("dp", "tensor"), None),
            P(("dp", "tensor"), None),
            P(None, None, "tensor"),
            P(None, "tensor"),
            P("tensor", None),
            P(),
            P(),
            P(),
            P(None, "tensor"),
            P("tensor"),
            P("tensor", None),
            P(),
            P(),
            P(),
        ),
        check_vma=False,
    )
```

```python
import functools

import jax
import jax.numpy as jnp
from jax import lax
from jax.experimental import pallas as pl
from jax.experimental.pallas import tpu as pltpu
from jax.sharding import PartitionSpec as P

HD = 64
LEN = 512


EPS = 1e-12
NEG = -1e30


def layer_norm(values, gain_vec, shift_vec):
    center = values - jnp.mean(values, axis=-1, keepdims=True)
    spread = jnp.mean(center * center, axis=-1, keepdims=True)
    return center * lax.rsqrt(spread + EPS) * gain_vec + shift_vec


def gelu_exact(values):
    return jax.nn.gelu(values, approximate=False)


def contract(left, right, left_dim, right_dim):
    return lax.dot_general(
        left, right, (((left_dim,), (right_dim,)), ((), ())), preferred_element_type=jnp.float32
    )


def _probs(q, k, length, factor):
    scores = lax.dot_general(q, k, (((1,), (1,)), ((), ())), preferred_element_type=jnp.float32) * factor
    col = lax.broadcasted_iota(jnp.int32, scores.shape, 1)
    scores = jnp.where(col < length, scores, NEG)
    top = jnp.max(scores, axis=1, keepdims=True)
    raised = jnp.exp(scores - top)
    return raised / jnp.sum(raised, axis=1, keepdims=True)


def _fwd_kernel(len_ref, qkv_ref, out_ref, *, heads, factor):
    length = len_ref[pl.program_id(0)]
    for h in range(heads):
        cols = slice(h * HD, (h + 1) * HD)
        q = qkv_ref[0, :, cols]
        k = qkv_ref[1, :, cols]
        v = qkv_ref[2, :, cols]
        probs = _probs(q, k, length, factor)
        out_ref[:, cols] = jnp.dot(
            probs.astype(jnp.bfloat16), v, preferred_element_type=jnp.float32
        ).astype(out_ref.dtype)


def _bwd_kernel(len_ref, qkv_ref, grad_ref, out_ref, *, heads, factor):
    length = len_ref[pl.program_id(0)]
    for h in range(heads):
        cols = slice(h * HD, (h + 1) * HD)
        q = qkv_ref[0, :, cols]
        k = qkv_ref[1, :, cols]
        v = qkv_ref[2, :, cols]
        g = grad_ref[:, cols]
        probs = _probs(q, k, length, factor)
        prob_grad = lax.dot_general(g, v, (((1,), (1,)), ((), ())), preferred_element_type=jnp.float32)
        row_dot = jnp.sum(prob_grad * probs, axis=1, keepdims=True)
        score_grad = (probs * (prob_grad - row_dot)).astype(jnp.bfloat16)
        out_ref[0, :, cols] = (
            jnp.dot(score_grad, k, preferred_element_type=jnp.float32) * factor
        ).astype(out_ref.dtype)
        out_ref[1, :, cols] = (
            lax.dot_general(score_grad, q, (((0,), (0,)), ((), ())), preferred_element_type=jnp.float32)
            * factor
        ).astype(out_ref.dtype)
        out_ref[2, :, cols] = lax.dot_general(
            probs.astype(jnp.bfloat16), g, (((0,), (0,)), ((), ())), preferred_element_type=jnp.float32
        ).astype(out_ref.dtype)


def attention_forward(qkv, lengths, factor, pair=2):
    _, rows, width = qkv.shape
    passages = rows // LEN
    block = pair * HD
    grid = (passages, width // block)
    return pl.pallas_call(
        functools.partial(_fwd_kernel, heads=pair, factor=factor),
        out_shape=jax.ShapeDtypeStruct((rows, width), jnp.bfloat16),
        grid_spec=pltpu.PrefetchScalarGridSpec(
            num_scalar_prefetch=1,
            grid=grid,
            in_specs=[pl.BlockSpec((3, LEN, block), lambda p, i, n: (0, p, i))],
            out_specs=pl.BlockSpec((LEN, block), lambda p, i, n: (p, i)),
        ),
        cost_estimate=pl.CostEstimate(
            flops=4 * rows * LEN * width, transcendentals=rows * LEN * width // HD,
            bytes_accessed=4 * rows * width * 2,
        ),
    )(lengths, qkv)


def attention_backward(qkv, context_grad, lengths, factor, pair=2):
    _, rows, width = qkv.shape
    passages = rows // LEN
    block = pair * HD
    grid = (passages, width // block)
    return pl.pallas_call(
        functools.partial(_bwd_kernel, heads=pair, factor=factor),
        out_shape=jax.ShapeDtypeStruct((3, rows, width), jnp.bfloat16),
        grid_spec=pltpu.PrefetchScalarGridSpec(
            num_scalar_prefetch=1,
            grid=grid,
            in_specs=[
                pl.BlockSpec((3, LEN, block), lambda p, i, n: (0, p, i)),
                pl.BlockSpec((LEN, block), lambda p, i, n: (p, i)),
            ],
            out_specs=pl.BlockSpec((3, LEN, block), lambda p, i, n: (0, p, i)),
        ),
        cost_estimate=pl.CostEstimate(
            flops=10 * rows * LEN * width, transcendentals=rows * LEN * width // HD,
            bytes_accessed=8 * rows * width * 2,
        ),
    )(lengths, qkv, context_grad)


def dp_pow2(values, dp_size):
    steps = dp_size.bit_length() - 1
    return dp_size == 1 << steps and values.shape[0] % dp_size == 0


def dp_halve(values, dp_size, sum_dtype=None):
    steps = dp_size.bit_length() - 1
    index = lax.axis_index("dp")
    link = values.dtype
    kept = values if sum_dtype is None else values.astype(sum_dtype)
    for step in range(steps):
        bit = (index >> step) & 1
        half = kept.shape[0] // 2
        keep = lax.dynamic_slice_in_dim(kept, bit * half, half)
        give = lax.dynamic_slice_in_dim(kept, (1 - bit) * half, half).astype(link)
        got = lax.ppermute(give, "dp", [(i, i ^ (1 << step)) for i in range(dp_size)])
        kept = keep + got.astype(kept.dtype)
    return kept


def bit_reversed(count):
    steps = count.bit_length() - 1
    return [int(format(i, f"0{steps}b")[::-1], 2) if steps else 0 for i in range(count)]


def dp_double(kept, dp_size):
    steps = dp_size.bit_length() - 1
    index = lax.axis_index("dp")
    for step in reversed(range(steps)):
        bit = (index >> step) & 1
        got = lax.ppermute(kept, "dp", [(i, i ^ (1 << step)) for i in range(dp_size)])
        kept = jnp.concatenate(
            [jnp.where(bit == 0, kept, got), jnp.where(bit == 0, got, kept)]
        )
    return kept


def make_per_device(dp_size):
    def per_device(
        tokens,
        out_grad,
        lengths,
        qkv_weight,
        qkv_bias,
        out_weight,
        out_bias,
        norm1_gain,
        norm1_shift,
        up_weight,
        up_bias,
        down_weight,
        down_bias,
        norm2_gain,
        norm2_shift,
    ):
        rows, width = tokens.shape
        shard = qkv_weight.shape[2]
        groups = width // shard
        passages = rows // LEN
        factor = HD ** (-0.5)

        packed_w = jnp.concatenate(
            [
                qkv_weight.reshape(3 * width, shard),
                out_weight.T,
                qkv_bias,
            ],
            axis=0,
        )
        w_rows = packed_w.shape[0]
        half_rows = -(-w_rows // 16) * 8
        packed_w = jnp.pad(packed_w, ((0, 2 * half_rows - w_rows), (0, 0)))
        dp_index = lax.axis_index("dp")
        parity = dp_index % 2
        mine = lax.dynamic_slice_in_dim(packed_w, parity * half_rows, half_rows)
        mine = lax.all_gather(mine, "tensor", axis=0, tiled=False)
        other = lax.ppermute(mine, "dp", [(i, i ^ 1) for i in range(dp_size)])
        first = jnp.where(parity == 0, mine, other)
        second = jnp.where(parity == 0, other, mine)
        weights_all = jnp.concatenate([first, second], axis=1)[:, :w_rows]
        qkv_blocks = weights_all[:, : 3 * width].reshape(groups, 3, width, shard)
        proj_blocks = weights_all[:, 3 * width : 4 * width]
        bias_full = weights_all[:, 4 * width :].transpose(1, 0, 2).reshape(2, width)

        tensor_index = lax.axis_index("tensor")
        own_lengths = lax.dynamic_slice_in_dim(lengths, tensor_index * passages, passages)

        own_tokens = tokens.astype(jnp.float32)
        projected = jnp.einsum(
            "rd,gtdj->trgj", tokens, qkv_blocks, preferred_element_type=jnp.float32
        ).reshape(3, rows, width)
        bias3 = jnp.stack([bias_full[0], jnp.zeros_like(bias_full[0]), bias_full[1]])
        qkv_low = (projected + bias3[:, None, :]).astype(jnp.bfloat16)
        context_low = attention_forward(qkv_low, own_lengths, factor)
        attn_out = jnp.einsum(
            "rgj,gcj->rc",
            context_low.reshape(rows, groups, shard),
            proj_blocks,
            preferred_element_type=jnp.float32,
        )
        middle, norm1_back = jax.vjp(
            layer_norm, own_tokens + attn_out + out_bias, norm1_gain, norm1_shift
        )
        middle_low = middle.astype(jnp.bfloat16)
        ffn_rows = lax.all_gather(middle_low, "tensor", axis=0, tiled=True)
        pre_act = jnp.dot(ffn_rows, up_weight, preferred_element_type=jnp.float32) + up_bias
        activated, gelu_back = jax.vjp(gelu_exact, pre_act)
        hidden = activated.astype(jnp.bfloat16)
        ffn_out = lax.psum_scatter(
            jnp.dot(hidden, down_weight, preferred_element_type=jnp.float32).astype(jnp.bfloat16),
            "tensor",
            scatter_dimension=0,
            tiled=True,
        ).astype(jnp.float32)
        layer_out, norm2_back = jax.vjp(
            layer_norm, middle + ffn_out + down_bias, norm2_gain, norm2_shift
        )
        second_grad, grad_norm2_gain, grad_norm2_shift = norm2_back(out_grad.astype(jnp.float32))
        branch_grad = second_grad.astype(jnp.bfloat16)
        grad_down_bias = jnp.sum(branch_grad, axis=0, dtype=jnp.float32)
        branch_rows = lax.all_gather(branch_grad, "tensor", axis=0, tiled=True)
        hidden_grad = contract(branch_rows, down_weight, 1, 1)
        grad_down_weight = contract(hidden, branch_rows, 0, 0)
        pre_grad = gelu_back(hidden_grad)[0].astype(jnp.bfloat16)
        grad_up_bias = jnp.sum(pre_grad, axis=0, dtype=jnp.float32)
        grad_up_weight = contract(ffn_rows, pre_grad, 0, 0)
        ffn_grads = (grad_up_weight, grad_down_weight)
        halved = all(dp_pow2(g, dp_size) for g in ffn_grads)
        if halved:
            ffn_grads = tuple(dp_halve(g, dp_size) for g in ffn_grads)
        else:
            ffn_grads = lax.psum(ffn_grads, "dp")
        middle_part = lax.psum_scatter(
            contract(pre_grad, up_weight, 1, 1).astype(jnp.bfloat16),
            "tensor",
            scatter_dimension=0,
            tiled=True,
        ).astype(jnp.float32)
        norm1_in, ffn_grads = lax.optimization_barrier((second_grad + middle_part, ffn_grads))
        first_grad, grad_norm1_gain, grad_norm1_shift = norm1_back(norm1_in)
        attn_grad = first_grad.astype(jnp.bfloat16)
        grad_out_bias = jnp.sum(attn_grad, axis=0, dtype=jnp.float32)
        context_grad = (
            jnp.einsum("rc,gcj->rgj", attn_grad, proj_blocks, preferred_element_type=jnp.float32)
            .astype(jnp.bfloat16)
            .reshape(rows, width)
        )
        early = contract(attn_grad, context_low, 0, 0)
        early_halved = dp_pow2(early, dp_size)
        if early_halved:
            early = dp_halve(early.astype(jnp.bfloat16), dp_size, jnp.float32)
        else:
            early = lax.psum_scatter(early, "dp", scatter_dimension=0, tiled=True)
        proj_grad = attention_backward(qkv_low, context_grad, own_lengths, factor)
        grad_bias_full = jnp.sum(proj_grad[0::2], axis=1, dtype=jnp.float32)
        grad_qkv_full = jnp.einsum(
            "rd,tre->tde", tokens, proj_grad, preferred_element_type=jnp.float32
        )
        input_part = jnp.einsum(
            "trgj,gtdj->rd",
            proj_grad.reshape(3, rows, groups, shard),
            qkv_blocks,
            preferred_element_type=jnp.float32,
        )
        input_grad = (first_grad + input_part).astype(jnp.bfloat16)

        small = jnp.stack(
            [
                grad_out_bias,
                grad_norm1_gain,
                grad_norm1_shift,
                grad_down_bias,
                grad_norm2_gain,
                grad_norm2_shift,
            ]
        )
        n_small = small.shape[0]
        small_rep = jnp.tile(small.reshape(n_small, groups, shard), (1, 1, groups)).reshape(
            n_small * groups, width
        )
        up_parts = grad_up_bias.shape[0] // shard
        own_group = (jnp.arange(width) // shard == tensor_index)[None, :]
        up_rep = jnp.where(
            own_group, jnp.tile(grad_up_bias.reshape(up_parts, shard), (1, groups)), 0.0
        )
        tail = jnp.concatenate([grad_bias_full, small_rep, up_rep], axis=0)
        tail_rows = tail.shape[0]
        tail = jnp.pad(tail, ((0, -(-tail_rows // 8) * 8 - tail_rows), (0, 0)))
        late = lax.psum_scatter(
            grad_qkv_full.reshape(3 * width, width).astype(jnp.bfloat16),
            "dp",
            scatter_dimension=0,
            tiled=True,
        ).astype(jnp.float32)
        joined = jnp.concatenate([late, early, tail], axis=0)
        joined = lax.psum_scatter(
            joined.reshape(joined.shape[0], groups, shard).transpose(1, 0, 2),
            "tensor",
            scatter_dimension=0,
            tiled=True,
        )[0]
        if halved:
            ffn_grads = tuple(
                dp_double(g.astype(jnp.bfloat16), dp_size).astype(jnp.float32) for g in ffn_grads
            )
            joined, ffn_grads = lax.optimization_barrier((joined, ffn_grads))
        grad_up_weight, grad_down_weight = ffn_grads
        late_rows = late.shape[0]
        early_rows = early.shape[0]
        joined = lax.all_gather(joined, "dp", axis=0, tiled=False)
        early = joined[:, late_rows : late_rows + early_rows]
        if early_halved:
            order = bit_reversed(dp_size)
            place = [order.index(b) for b in range(dp_size)]
            early = jnp.concatenate([early[p] for p in place], axis=0)
        pieces = [
            joined[:, :late_rows].reshape(-1, shard),
            early.reshape(-1, shard),
            jnp.sum(joined[:, late_rows + early_rows :], axis=0),
        ]
        grad_qkv_weight = pieces[0].reshape(3, width, shard)
        grad_out_weight = pieces[1].T
        tail = pieces[2]
        grad_qkv_bias = tail[:2]
        small_sum = tail[2 : 2 + n_small * groups].reshape(n_small, width)
        grad_up_bias = tail[2 + n_small * groups : 2 + n_small * groups + up_parts].reshape(-1)
        (
            grad_out_bias,
            grad_norm1_gain,
            grad_norm1_shift,
            grad_down_bias,
            grad_norm2_gain,
            grad_norm2_shift,
        ) = [small_sum[i] for i in range(n_small)]
        return (
            layer_out.astype(jnp.bfloat16),
            input_grad,
            grad_qkv_weight,
            grad_qkv_bias,
            grad_out_weight,
            grad_out_bias,
            grad_norm1_gain,
            grad_norm1_shift,
            grad_up_weight,
            grad_up_bias,
            grad_down_weight,
            grad_down_bias,
            grad_norm2_gain,
            grad_norm2_shift,
        )

    return per_device


def solution(mesh):
    placed = (
        P(("dp", "tensor"), None),
        P(("dp", "tensor"), None),
        P("dp"),
        P(None, None, "tensor"),
        P(None, "tensor"),
        P("tensor", None),
        P(),
        P(),
        P(),
        P(None, "tensor"),
        P("tensor"),
        P("tensor", None),
        P(),
        P(),
        P(),
    )
    return jax.shard_map(
        make_per_device(mesh.shape["dp"]),
        mesh=mesh,
        in_specs=placed,
        out_specs=(
            P(("dp", "tensor"), None),
            P(("dp", "tensor"), None),
            P(None, None, "tensor"),
            P(None, "tensor"),
            P("tensor", None),
            P(),
            P(),
            P(),
            P(None, "tensor"),
            P("tensor"),
            P("tensor", None),
            P(),
            P(),
            P(),
        ),
        check_vma=False,
    )
```

```python
import functools

import jax
import jax.numpy as jnp
from jax import lax
from jax.experimental import pallas as pl
from jax.experimental.pallas import tpu as pltpu
from jax.sharding import PartitionSpec as P

HD = 64
LEN = 512


EPS = 1e-12
NEG = -1e30


def layer_norm(values, gain_vec, shift_vec):
    center = values - jnp.mean(values, axis=-1, keepdims=True)
    spread = jnp.mean(center * center, axis=-1, keepdims=True)
    return center * lax.rsqrt(spread + EPS) * gain_vec + shift_vec


def gelu_exact(values):
    return jax.nn.gelu(values, approximate=False)


def contract(left, right, left_dim, right_dim):
    return lax.dot_general(
        left, right, (((left_dim,), (right_dim,)), ((), ())), preferred_element_type=jnp.float32
    )


def _probs(q, k, length, factor):
    scores = lax.dot_general(q, k, (((1,), (1,)), ((), ())), preferred_element_type=jnp.float32) * factor
    col = lax.broadcasted_iota(jnp.int32, scores.shape, 1)
    scores = jnp.where(col < length, scores, NEG)
    top = jnp.max(scores, axis=1, keepdims=True)
    raised = jnp.exp(scores - top)
    return raised / jnp.sum(raised, axis=1, keepdims=True)


def _fwd_kernel(len_ref, q_ref, k_ref, v_ref, out_ref, *, heads, factor):
    length = len_ref[pl.program_id(0)]
    for h in range(heads):
        cols = slice(h * HD, (h + 1) * HD)
        v = v_ref[:, cols]
        probs = _probs(q_ref[:, cols], k_ref[:, cols], length, factor)
        out_ref[:, cols] = jnp.dot(
            probs.astype(jnp.bfloat16), v, preferred_element_type=jnp.float32
        ).astype(out_ref.dtype)


def _bwd_kernel(len_ref, q_ref, k_ref, v_ref, grad_ref, out_ref, *, heads, factor):
    length = len_ref[pl.program_id(0)]
    for h in range(heads):
        cols = slice(h * HD, (h + 1) * HD)
        q = q_ref[:, cols]
        k = k_ref[:, cols]
        v = v_ref[:, cols]
        g = grad_ref[:, cols]
        probs = _probs(q, k, length, factor)
        prob_grad = lax.dot_general(g, v, (((1,), (1,)), ((), ())), preferred_element_type=jnp.float32)
        row_dot = jnp.sum(prob_grad * probs, axis=1, keepdims=True)
        score_grad = (probs * (prob_grad - row_dot)).astype(jnp.bfloat16)
        out_ref[0, :, cols] = (
            jnp.dot(score_grad, k, preferred_element_type=jnp.float32) * factor
        ).astype(out_ref.dtype)
        out_ref[1, :, cols] = (
            lax.dot_general(score_grad, q, (((0,), (0,)), ((), ())), preferred_element_type=jnp.float32)
            * factor
        ).astype(out_ref.dtype)
        out_ref[2, :, cols] = lax.dot_general(
            probs.astype(jnp.bfloat16), g, (((0,), (0,)), ((), ())), preferred_element_type=jnp.float32
        ).astype(out_ref.dtype)


def _row_block(pair):
    return pl.BlockSpec((LEN, pair * HD), lambda p, i, n: (p, i))


def attention_forward(queries, keys, values, lengths, factor, pair=2):
    rows, width = queries.shape
    grid = (rows // LEN, width // (pair * HD))
    return pl.pallas_call(
        functools.partial(_fwd_kernel, heads=pair, factor=factor),
        out_shape=jax.ShapeDtypeStruct((rows, width), jnp.bfloat16),
        grid_spec=pltpu.PrefetchScalarGridSpec(
            num_scalar_prefetch=1,
            grid=grid,
            in_specs=[_row_block(pair)] * 3,
            out_specs=_row_block(pair),
        ),
        cost_estimate=pl.CostEstimate(
            flops=4 * rows * LEN * width,
            transcendentals=rows * LEN * width // HD,
            bytes_accessed=4 * rows * width * 2,
        ),
    )(lengths, queries, keys, values)


def attention_backward(queries, keys, values, context_grad, lengths, factor, pair=2):
    rows, width = queries.shape
    grid = (rows // LEN, width // (pair * HD))
    return pl.pallas_call(
        functools.partial(_bwd_kernel, heads=pair, factor=factor),
        out_shape=jax.ShapeDtypeStruct((3, rows, width), jnp.bfloat16),
        grid_spec=pltpu.PrefetchScalarGridSpec(
            num_scalar_prefetch=1,
            grid=grid,
            in_specs=[_row_block(pair)] * 4,
            out_specs=pl.BlockSpec((3, LEN, pair * HD), lambda p, i, n: (0, p, i)),
        ),
        cost_estimate=pl.CostEstimate(
            flops=10 * rows * LEN * width,
            transcendentals=rows * LEN * width // HD,
            bytes_accessed=7 * rows * width * 2,
        ),
    )(lengths, queries, keys, values, context_grad)


def dp_pow2(values, dp_size):
    steps = dp_size.bit_length() - 1
    return dp_size == 1 << steps and values.shape[0] % dp_size == 0


def dp_halve(values, dp_size, sum_dtype=None):
    steps = dp_size.bit_length() - 1
    index = lax.axis_index("dp")
    link = values.dtype
    kept = values if sum_dtype is None else values.astype(sum_dtype)
    for step in range(steps):
        bit = (index >> step) & 1
        half = kept.shape[0] // 2
        keep = lax.dynamic_slice_in_dim(kept, bit * half, half)
        give = lax.dynamic_slice_in_dim(kept, (1 - bit) * half, half).astype(link)
        got = lax.ppermute(give, "dp", [(i, i ^ (1 << step)) for i in range(dp_size)])
        kept = keep + got.astype(kept.dtype)
    return kept


def bit_reversed(count):
    steps = count.bit_length() - 1
    return [int(format(i, f"0{steps}b")[::-1], 2) if steps else 0 for i in range(count)]


def dp_double(kept, dp_size):
    steps = dp_size.bit_length() - 1
    index = lax.axis_index("dp")
    for step in reversed(range(steps)):
        bit = (index >> step) & 1
        got = lax.ppermute(kept, "dp", [(i, i ^ (1 << step)) for i in range(dp_size)])
        kept = jnp.concatenate(
            [jnp.where(bit == 0, kept, got), jnp.where(bit == 0, got, kept)]
        )
    return kept


def make_per_device(dp_size):
    def per_device(
        tokens,
        out_grad,
        lengths,
        qkv_weight,
        qkv_bias,
        out_weight,
        out_bias,
        norm1_gain,
        norm1_shift,
        up_weight,
        up_bias,
        down_weight,
        down_bias,
        norm2_gain,
        norm2_shift,
    ):
        rows, width = tokens.shape
        shard = qkv_weight.shape[2]
        groups = width // shard
        passages = rows // LEN
        factor = HD ** (-0.5)

        half_rows = -(-(2 * width + 2) // 8) * 8
        first_half = jnp.pad(
            jnp.concatenate([qkv_weight[0], qkv_weight[1], qkv_bias], axis=0),
            ((0, half_rows - 2 * width - 2), (0, 0)),
        )
        second_half = jnp.pad(
            jnp.concatenate([qkv_weight[2], out_weight.T], axis=0),
            ((0, half_rows - 2 * width), (0, 0)),
        )
        dp_index = lax.axis_index("dp")
        parity = dp_index % 2
        mine = jnp.where(parity == 0, first_half, second_half)
        mine = lax.all_gather(mine, "tensor", axis=1, tiled=False).reshape(half_rows, width)
        other = lax.ppermute(mine, "dp", [(i, i ^ 1) for i in range(dp_size)])
        first_half = jnp.where(parity == 0, mine, other)
        second_half = jnp.where(parity == 0, other, mine)
        query_weight = first_half[:width]
        key_weight = first_half[width : 2 * width]
        query_bias = first_half[2 * width]
        value_bias = first_half[2 * width + 1]
        value_weight = second_half[:width]
        proj_t = second_half[width : 2 * width]

        tensor_index = lax.axis_index("tensor")
        own_lengths = lax.dynamic_slice_in_dim(lengths, tensor_index * passages, passages)

        own_tokens = tokens.astype(jnp.float32)
        def project(weight, bias=None):
            out = jnp.dot(tokens, weight, preferred_element_type=jnp.float32)
            return (out if bias is None else out + bias).astype(jnp.bfloat16)

        query_low = project(query_weight, query_bias)
        key_low = project(key_weight)
        value_low = project(value_weight, value_bias)
        context_low = attention_forward(query_low, key_low, value_low, own_lengths, factor)
        attn_out = contract(context_low, proj_t, 1, 1)
        middle, norm1_back = jax.vjp(
            layer_norm, own_tokens + attn_out + out_bias, norm1_gain, norm1_shift
        )
        middle_low = middle.astype(jnp.bfloat16)
        ffn_rows = lax.all_gather(middle_low, "tensor", axis=0, tiled=True)
        pre_act = jnp.dot(ffn_rows, up_weight, preferred_element_type=jnp.float32) + up_bias
        activated, gelu_back = jax.vjp(gelu_exact, pre_act)
        hidden = activated.astype(jnp.bfloat16)
        ffn_out = lax.psum_scatter(
            jnp.dot(hidden, down_weight, preferred_element_type=jnp.float32).astype(jnp.bfloat16),
            "tensor",
            scatter_dimension=0,
            tiled=True,
        ).astype(jnp.float32)
        layer_out, norm2_back = jax.vjp(
            layer_norm, middle + ffn_out + down_bias, norm2_gain, norm2_shift
        )
        second_grad, grad_norm2_gain, grad_norm2_shift = norm2_back(out_grad.astype(jnp.float32))
        branch_grad = second_grad.astype(jnp.bfloat16)
        grad_down_bias = jnp.sum(branch_grad, axis=0, dtype=jnp.float32)
        branch_rows = lax.all_gather(branch_grad, "tensor", axis=0, tiled=True)
        hidden_grad = contract(branch_rows, down_weight, 1, 1)
        grad_down_weight = contract(hidden, branch_rows, 0, 0)
        pre_grad = gelu_back(hidden_grad)[0].astype(jnp.bfloat16)
        grad_up_bias = jnp.sum(pre_grad, axis=0, dtype=jnp.float32)
        grad_up_weight = contract(ffn_rows, pre_grad, 0, 0)
        ffn_grads = (grad_up_weight, grad_down_weight)
        halved = all(dp_pow2(g, dp_size) for g in ffn_grads)
        if halved:
            ffn_grads = tuple(dp_halve(g, dp_size) for g in ffn_grads)
        else:
            ffn_grads = lax.psum(ffn_grads, "dp")
        middle_part = lax.psum_scatter(
            contract(pre_grad, up_weight, 1, 1).astype(jnp.bfloat16),
            "tensor",
            scatter_dimension=0,
            tiled=True,
        ).astype(jnp.float32)
        norm1_in, ffn_grads = lax.optimization_barrier((second_grad + middle_part, ffn_grads))
        first_grad, grad_norm1_gain, grad_norm1_shift = norm1_back(norm1_in)
        attn_grad = first_grad.astype(jnp.bfloat16)
        grad_out_bias = jnp.sum(attn_grad, axis=0, dtype=jnp.float32)
        context_grad = jnp.dot(attn_grad, proj_t, preferred_element_type=jnp.float32).astype(
            jnp.bfloat16
        )
        early = contract(attn_grad, context_low, 0, 0)
        early_halved = dp_pow2(early, dp_size)
        if early_halved:
            early = dp_halve(early.astype(jnp.bfloat16), dp_size, jnp.float32)
        else:
            early = lax.psum_scatter(early, "dp", scatter_dimension=0, tiled=True)
        proj_grad = attention_backward(
            query_low, key_low, value_low, context_grad, own_lengths, factor
        )
        grad_bias_full = jnp.sum(proj_grad[0::2], axis=1, dtype=jnp.float32)
        grad_qkv_full = jnp.einsum(
            "rd,tre->tde", tokens, proj_grad, preferred_element_type=jnp.float32
        )
        input_part = (
            contract(proj_grad[0], query_weight, 1, 1)
            + contract(proj_grad[1], key_weight, 1, 1)
            + contract(proj_grad[2], value_weight, 1, 1)
        )
        input_grad = (first_grad + input_part).astype(jnp.bfloat16)

        small = jnp.stack(
            [
                grad_out_bias,
                grad_norm1_gain,
                grad_norm1_shift,
                grad_down_bias,
                grad_norm2_gain,
                grad_norm2_shift,
            ]
        )
        n_small = small.shape[0]
        small_rep = jnp.tile(small.reshape(n_small, groups, shard), (1, 1, groups)).reshape(
            n_small * groups, width
        )
        up_parts = grad_up_bias.shape[0] // shard
        own_group = (jnp.arange(width) // shard == tensor_index)[None, :]
        up_rep = jnp.where(
            own_group, jnp.tile(grad_up_bias.reshape(up_parts, shard), (1, groups)), 0.0
        )
        tail = jnp.concatenate([grad_bias_full, small_rep, up_rep], axis=0)
        tail_rows = tail.shape[0]
        tail = jnp.pad(tail, ((0, -(-tail_rows // 8) * 8 - tail_rows), (0, 0)))
        late = lax.psum_scatter(
            grad_qkv_full.reshape(3 * width, width).astype(jnp.bfloat16),
            "dp",
            scatter_dimension=0,
            tiled=True,
        ).astype(jnp.float32)
        joined = jnp.concatenate([late, early, tail], axis=0)
        joined = lax.psum_scatter(
            joined.reshape(joined.shape[0], groups, shard).transpose(1, 0, 2),
            "tensor",
            scatter_dimension=0,
            tiled=True,
        )[0]
        if halved:
            ffn_grads = tuple(
                dp_double(g.astype(jnp.bfloat16), dp_size).astype(jnp.float32) for g in ffn_grads
            )
            joined, ffn_grads = lax.optimization_barrier((joined, ffn_grads))
        grad_up_weight, grad_down_weight = ffn_grads
        late_rows = late.shape[0]
        early_rows = early.shape[0]
        joined = lax.all_gather(joined, "dp", axis=0, tiled=False)
        early = joined[:, late_rows : late_rows + early_rows]
        if early_halved:
            order = bit_reversed(dp_size)
            place = [order.index(b) for b in range(dp_size)]
            early = jnp.concatenate([early[p] for p in place], axis=0)
        pieces = [
            joined[:, :late_rows].reshape(-1, shard),
            early.reshape(-1, shard),
            jnp.sum(joined[:, late_rows + early_rows :], axis=0),
        ]
        grad_qkv_weight = pieces[0].reshape(3, width, shard)
        grad_out_weight = pieces[1].T
        tail = pieces[2]
        grad_qkv_bias = tail[:2]
        small_sum = tail[2 : 2 + n_small * groups].reshape(n_small, width)
        grad_up_bias = tail[2 + n_small * groups : 2 + n_small * groups + up_parts].reshape(-1)
        (
            grad_out_bias,
            grad_norm1_gain,
            grad_norm1_shift,
            grad_down_bias,
            grad_norm2_gain,
            grad_norm2_shift,
        ) = [small_sum[i] for i in range(n_small)]
        return (
            layer_out.astype(jnp.bfloat16),
            input_grad,
            grad_qkv_weight,
            grad_qkv_bias,
            grad_out_weight,
            grad_out_bias,
            grad_norm1_gain,
            grad_norm1_shift,
            grad_up_weight,
            grad_up_bias,
            grad_down_weight,
            grad_down_bias,
            grad_norm2_gain,
            grad_norm2_shift,
        )

    return per_device


def solution(mesh):
    placed = (
        P(("dp", "tensor"), None),
        P(("dp", "tensor"), None),
        P("dp"),
        P(None, None, "tensor"),
        P(None, "tensor"),
        P("tensor", None),
        P(),
        P(),
        P(),
        P(None, "tensor"),
        P("tensor"),
        P("tensor", None),
        P(),
        P(),
        P(),
    )
    return jax.shard_map(
        make_per_device(mesh.shape["dp"]),
        mesh=mesh,
        in_specs=placed,
        out_specs=(
            P(("dp", "tensor"), None),
            P(("dp", "tensor"), None),
            P(None, None, "tensor"),
            P(None, "tensor"),
            P("tensor", None),
            P(),
            P(),
            P(),
            P(None, "tensor"),
            P("tensor"),
            P("tensor", None),
            P(),
            P(),
            P(),
        ),
        check_vma=False,
    )
```

```python
import functools

import jax
import jax.numpy as jnp
from jax import lax
from jax.experimental import pallas as pl
from jax.experimental.pallas import tpu as pltpu
from jax.sharding import PartitionSpec as P

HD = 64
LEN = 512


EPS = 1e-12
NEG = -1e30


def layer_norm(values, gain_vec, shift_vec):
    center = values - jnp.mean(values, axis=-1, keepdims=True)
    spread = jnp.mean(center * center, axis=-1, keepdims=True)
    return center * lax.rsqrt(spread + EPS) * gain_vec + shift_vec


def gelu_and_slope(values):
    cdf = 0.5 * (1.0 + lax.erf(values * (2.0 ** -0.5)))
    density = jnp.exp(-0.5 * values * values) * ((2.0 * jnp.pi) ** -0.5)
    return values * cdf, cdf + values * density


def contract(left, right, left_dim, right_dim):
    return lax.dot_general(
        left, right, (((left_dim,), (right_dim,)), ((), ())), preferred_element_type=jnp.float32
    )


def _probs(q, k, length, factor):
    scores = lax.dot_general(q, k, (((1,), (1,)), ((), ())), preferred_element_type=jnp.float32) * factor
    col = lax.broadcasted_iota(jnp.int32, scores.shape, 1)
    scores = jnp.where(col < length, scores, NEG)
    top = jnp.max(scores, axis=1, keepdims=True)
    raised = jnp.exp(scores - top)
    return raised / jnp.sum(raised, axis=1, keepdims=True)


def _fwd_kernel(len_ref, q_ref, k_ref, v_ref, out_ref, *, heads, factor):
    length = len_ref[pl.program_id(0)]
    for h in range(heads):
        cols = slice(h * HD, (h + 1) * HD)
        v = v_ref[:, cols]
        probs = _probs(q_ref[:, cols], k_ref[:, cols], length, factor)
        out_ref[:, cols] = jnp.dot(
            probs.astype(jnp.bfloat16), v, preferred_element_type=jnp.float32
        ).astype(out_ref.dtype)


def _bwd_kernel(len_ref, q_ref, k_ref, v_ref, grad_ref, out_ref, *, heads, factor):
    length = len_ref[pl.program_id(0)]
    for h in range(heads):
        cols = slice(h * HD, (h + 1) * HD)
        q = q_ref[:, cols]
        k = k_ref[:, cols]
        v = v_ref[:, cols]
        g = grad_ref[:, cols]
        probs = _probs(q, k, length, factor)
        prob_grad = lax.dot_general(g, v, (((1,), (1,)), ((), ())), preferred_element_type=jnp.float32)
        row_dot = jnp.sum(prob_grad * probs, axis=1, keepdims=True)
        score_grad = (probs * (prob_grad - row_dot)).astype(jnp.bfloat16)
        out_ref[0, :, cols] = (
            jnp.dot(score_grad, k, preferred_element_type=jnp.float32) * factor
        ).astype(out_ref.dtype)
        out_ref[1, :, cols] = (
            lax.dot_general(score_grad, q, (((0,), (0,)), ((), ())), preferred_element_type=jnp.float32)
            * factor
        ).astype(out_ref.dtype)
        out_ref[2, :, cols] = lax.dot_general(
            probs.astype(jnp.bfloat16), g, (((0,), (0,)), ((), ())), preferred_element_type=jnp.float32
        ).astype(out_ref.dtype)


def _row_block(pair):
    return pl.BlockSpec((LEN, pair * HD), lambda p, i, n: (p, i))


def attention_forward(queries, keys, values, lengths, factor, pair=2):
    rows, width = queries.shape
    grid = (rows // LEN, width // (pair * HD))
    return pl.pallas_call(
        functools.partial(_fwd_kernel, heads=pair, factor=factor),
        out_shape=jax.ShapeDtypeStruct((rows, width), jnp.bfloat16),
        grid_spec=pltpu.PrefetchScalarGridSpec(
            num_scalar_prefetch=1,
            grid=grid,
            in_specs=[_row_block(pair)] * 3,
            out_specs=_row_block(pair),
        ),
        cost_estimate=pl.CostEstimate(
            flops=4 * rows * LEN * width,
            transcendentals=rows * LEN * width // HD,
            bytes_accessed=4 * rows * width * 2,
        ),
    )(lengths, queries, keys, values)


def attention_backward(queries, keys, values, context_grad, lengths, factor, pair=2):
    rows, width = queries.shape
    grid = (rows // LEN, width // (pair * HD))
    return pl.pallas_call(
        functools.partial(_bwd_kernel, heads=pair, factor=factor),
        out_shape=jax.ShapeDtypeStruct((3, rows, width), jnp.bfloat16),
        grid_spec=pltpu.PrefetchScalarGridSpec(
            num_scalar_prefetch=1,
            grid=grid,
            in_specs=[_row_block(pair)] * 4,
            out_specs=pl.BlockSpec((3, LEN, pair * HD), lambda p, i, n: (0, p, i)),
        ),
        cost_estimate=pl.CostEstimate(
            flops=10 * rows * LEN * width,
            transcendentals=rows * LEN * width // HD,
            bytes_accessed=7 * rows * width * 2,
        ),
    )(lengths, queries, keys, values, context_grad)


def dp_pow2(values, dp_size):
    steps = dp_size.bit_length() - 1
    return dp_size == 1 << steps and values.shape[0] % dp_size == 0


def dp_halve(values, dp_size, sum_dtype=None):
    steps = dp_size.bit_length() - 1
    index = lax.axis_index("dp")
    link = values.dtype
    kept = values if sum_dtype is None else values.astype(sum_dtype)
    for step in range(steps):
        bit = (index >> step) & 1
        half = kept.shape[0] // 2
        keep = lax.dynamic_slice_in_dim(kept, bit * half, half)
        give = lax.dynamic_slice_in_dim(kept, (1 - bit) * half, half).astype(link)
        got = lax.ppermute(give, "dp", [(i, i ^ (1 << step)) for i in range(dp_size)])
        kept = keep + got.astype(kept.dtype)
    return kept


def bit_reversed(count):
    steps = count.bit_length() - 1
    return [int(format(i, f"0{steps}b")[::-1], 2) if steps else 0 for i in range(count)]


def dp_double(kept, dp_size):
    steps = dp_size.bit_length() - 1
    index = lax.axis_index("dp")
    for step in reversed(range(steps)):
        bit = (index >> step) & 1
        got = lax.ppermute(kept, "dp", [(i, i ^ (1 << step)) for i in range(dp_size)])
        kept = jnp.concatenate(
            [jnp.where(bit == 0, kept, got), jnp.where(bit == 0, got, kept)]
        )
    return kept


def make_per_device(dp_size):
    def per_device(
        tokens,
        out_grad,
        lengths,
        qkv_weight,
        qkv_bias,
        out_weight,
        out_bias,
        norm1_gain,
        norm1_shift,
        up_weight,
        up_bias,
        down_weight,
        down_bias,
        norm2_gain,
        norm2_shift,
    ):
        rows, width = tokens.shape
        shard = qkv_weight.shape[2]
        groups = width // shard
        passages = rows // LEN
        factor = HD ** (-0.5)

        half_rows = -(-(2 * width + 2) // 8) * 8
        first_half = jnp.pad(
            jnp.concatenate([qkv_weight[0], qkv_weight[1], qkv_bias], axis=0),
            ((0, half_rows - 2 * width - 2), (0, 0)),
        )
        second_half = jnp.pad(
            jnp.concatenate([qkv_weight[2], out_weight.T], axis=0),
            ((0, half_rows - 2 * width), (0, 0)),
        )
        dp_index = lax.axis_index("dp")
        parity = dp_index % 2
        mine = jnp.where(parity == 0, first_half, second_half)
        mine = lax.all_gather(mine, "tensor", axis=1, tiled=False).reshape(half_rows, width)
        other = lax.ppermute(mine, "dp", [(i, i ^ 1) for i in range(dp_size)])
        first_half = jnp.where(parity == 0, mine, other)
        second_half = jnp.where(parity == 0, other, mine)
        query_weight = first_half[:width]
        key_weight = first_half[width : 2 * width]
        query_bias = first_half[2 * width]
        value_bias = first_half[2 * width + 1]
        value_weight = second_half[:width]
        proj_t = second_half[width : 2 * width]

        tensor_index = lax.axis_index("tensor")
        own_lengths = lax.dynamic_slice_in_dim(lengths, tensor_index * passages, passages)

        own_tokens = tokens.astype(jnp.float32)
        def project(weight, bias=None):
            out = jnp.dot(tokens, weight, preferred_element_type=jnp.float32)
            return (out if bias is None else out + bias).astype(jnp.bfloat16)

        query_low = project(query_weight, query_bias)
        key_low = project(key_weight)
        value_low = project(value_weight, value_bias)
        context_low = attention_forward(query_low, key_low, value_low, own_lengths, factor)
        attn_out = contract(context_low, proj_t, 1, 1)
        middle, norm1_back = jax.vjp(
            layer_norm, own_tokens + attn_out + out_bias, norm1_gain, norm1_shift
        )
        middle_low = middle.astype(jnp.bfloat16)
        ffn_rows = lax.all_gather(middle_low, "tensor", axis=0, tiled=True)
        pre_act = jnp.dot(ffn_rows, up_weight, preferred_element_type=jnp.float32) + up_bias
        activated, gelu_slope = gelu_and_slope(pre_act)
        hidden = activated.astype(jnp.bfloat16)
        ffn_out = lax.psum_scatter(
            jnp.dot(hidden, down_weight, preferred_element_type=jnp.float32).astype(jnp.bfloat16),
            "tensor",
            scatter_dimension=0,
            tiled=True,
        ).astype(jnp.float32)
        layer_out, norm2_back = jax.vjp(
            layer_norm, middle + ffn_out + down_bias, norm2_gain, norm2_shift
        )
        second_grad, grad_norm2_gain, grad_norm2_shift = norm2_back(out_grad.astype(jnp.float32))
        branch_grad = second_grad.astype(jnp.bfloat16)
        grad_down_bias = jnp.sum(branch_grad, axis=0, dtype=jnp.float32)
        branch_rows = lax.all_gather(branch_grad, "tensor", axis=0, tiled=True)
        hidden_grad = contract(branch_rows, down_weight, 1, 1)
        grad_down_weight = contract(hidden, branch_rows, 0, 0)
        pre_grad = (hidden_grad * gelu_slope).astype(jnp.bfloat16)
        grad_up_bias = jnp.sum(pre_grad, axis=0, dtype=jnp.float32)
        grad_up_weight = contract(ffn_rows, pre_grad, 0, 0)
        ffn_grads = (grad_up_weight, grad_down_weight)
        halved = all(dp_pow2(g, dp_size) for g in ffn_grads)
        if halved:
            ffn_grads = tuple(dp_halve(g, dp_size) for g in ffn_grads)
        else:
            ffn_grads = lax.psum(ffn_grads, "dp")
        middle_part = lax.psum_scatter(
            contract(pre_grad, up_weight, 1, 1).astype(jnp.bfloat16),
            "tensor",
            scatter_dimension=0,
            tiled=True,
        ).astype(jnp.float32)
        norm1_in, ffn_grads = lax.optimization_barrier((second_grad + middle_part, ffn_grads))
        first_grad, grad_norm1_gain, grad_norm1_shift = norm1_back(norm1_in)
        attn_grad = first_grad.astype(jnp.bfloat16)
        grad_out_bias = jnp.sum(attn_grad, axis=0, dtype=jnp.float32)
        context_grad = jnp.dot(attn_grad, proj_t, preferred_element_type=jnp.float32).astype(
            jnp.bfloat16
        )
        early = contract(attn_grad, context_low, 0, 0)
        early_halved = dp_pow2(early, dp_size)
        if early_halved:
            early = dp_halve(early.astype(jnp.bfloat16), dp_size, jnp.float32)
        else:
            early = lax.psum_scatter(early, "dp", scatter_dimension=0, tiled=True)
        proj_grad = attention_backward(
            query_low, key_low, value_low, context_grad, own_lengths, factor
        )
        grad_bias_full = jnp.sum(proj_grad[0::2], axis=1, dtype=jnp.float32)
        grad_qkv_full = jnp.einsum(
            "rd,tre->tde", tokens, proj_grad, preferred_element_type=jnp.float32
        )
        input_part = (
            contract(proj_grad[0], query_weight, 1, 1)
            + contract(proj_grad[1], key_weight, 1, 1)
            + contract(proj_grad[2], value_weight, 1, 1)
        )
        input_grad = (first_grad + input_part).astype(jnp.bfloat16)

        small = jnp.stack(
            [
                grad_out_bias,
                grad_norm1_gain,
                grad_norm1_shift,
                grad_down_bias,
                grad_norm2_gain,
                grad_norm2_shift,
            ]
        )
        n_small = small.shape[0]
        small_rep = jnp.tile(small.reshape(n_small, groups, shard), (1, 1, groups)).reshape(
            n_small * groups, width
        )
        up_parts = grad_up_bias.shape[0] // shard
        own_group = (jnp.arange(width) // shard == tensor_index)[None, :]
        up_rep = jnp.where(
            own_group, jnp.tile(grad_up_bias.reshape(up_parts, shard), (1, groups)), 0.0
        )
        tail = jnp.concatenate([grad_bias_full, small_rep, up_rep], axis=0)
        tail_rows = tail.shape[0]
        tail = jnp.pad(tail, ((0, -(-tail_rows // 8) * 8 - tail_rows), (0, 0)))
        late = lax.psum_scatter(
            grad_qkv_full.reshape(3 * width, width).astype(jnp.bfloat16),
            "dp",
            scatter_dimension=0,
            tiled=True,
        ).astype(jnp.float32)
        joined = jnp.concatenate([late, early, tail], axis=0)
        joined = lax.psum_scatter(
            joined.reshape(joined.shape[0], groups, shard).transpose(1, 0, 2),
            "tensor",
            scatter_dimension=0,
            tiled=True,
        )[0]
        if halved:
            ffn_grads = tuple(
                dp_double(g.astype(jnp.bfloat16), dp_size).astype(jnp.float32) for g in ffn_grads
            )
            joined, ffn_grads = lax.optimization_barrier((joined, ffn_grads))
        grad_up_weight, grad_down_weight = ffn_grads
        late_rows = late.shape[0]
        early_rows = early.shape[0]
        joined = lax.all_gather(joined, "dp", axis=0, tiled=False)
        early = joined[:, late_rows : late_rows + early_rows]
        if early_halved:
            order = bit_reversed(dp_size)
            place = [order.index(b) for b in range(dp_size)]
            early = jnp.concatenate([early[p] for p in place], axis=0)
        pieces = [
            joined[:, :late_rows].reshape(-1, shard),
            early.reshape(-1, shard),
            jnp.sum(joined[:, late_rows + early_rows :], axis=0),
        ]
        grad_qkv_weight = pieces[0].reshape(3, width, shard)
        grad_out_weight = pieces[1].T
        tail = pieces[2]
        grad_qkv_bias = tail[:2]
        small_sum = tail[2 : 2 + n_small * groups].reshape(n_small, width)
        grad_up_bias = tail[2 + n_small * groups : 2 + n_small * groups + up_parts].reshape(-1)
        (
            grad_out_bias,
            grad_norm1_gain,
            grad_norm1_shift,
            grad_down_bias,
            grad_norm2_gain,
            grad_norm2_shift,
        ) = [small_sum[i] for i in range(n_small)]
        return (
            layer_out.astype(jnp.bfloat16),
            input_grad,
            grad_qkv_weight,
            grad_qkv_bias,
            grad_out_weight,
            grad_out_bias,
            grad_norm1_gain,
            grad_norm1_shift,
            grad_up_weight,
            grad_up_bias,
            grad_down_weight,
            grad_down_bias,
            grad_norm2_gain,
            grad_norm2_shift,
        )

    return per_device


def solution(mesh):
    placed = (
        P(("dp", "tensor"), None),
        P(("dp", "tensor"), None),
        P("dp"),
        P(None, None, "tensor"),
        P(None, "tensor"),
        P("tensor", None),
        P(),
        P(),
        P(),
        P(None, "tensor"),
        P("tensor"),
        P("tensor", None),
        P(),
        P(),
        P(),
    )
    return jax.shard_map(
        make_per_device(mesh.shape["dp"]),
        mesh=mesh,
        in_specs=placed,
        out_specs=(
            P(("dp", "tensor"), None),
            P(("dp", "tensor"), None),
            P(None, None, "tensor"),
            P(None, "tensor"),
            P("tensor", None),
            P(),
            P(),
            P(),
            P(None, "tensor"),
            P("tensor"),
            P("tensor", None),
            P(),
            P(),
            P(),
        ),
        check_vma=False,
    )
```

```python
import functools

import jax
import jax.numpy as jnp
from jax import lax
from jax.experimental import pallas as pl
from jax.experimental.pallas import tpu as pltpu
from jax.sharding import PartitionSpec as P

HD = 64
LEN = 512


EPS = 1e-12
NEG = -1e30


def layer_norm(values, gain_vec, shift_vec):
    center = values - jnp.mean(values, axis=-1, keepdims=True)
    spread = jnp.mean(center * center, axis=-1, keepdims=True)
    return center * lax.rsqrt(spread + EPS) * gain_vec + shift_vec


def gelu_and_slope(values):
    cdf = 0.5 * (1.0 + lax.erf(values * (2.0 ** -0.5)))
    density = jnp.exp(-0.5 * values * values) * ((2.0 * jnp.pi) ** -0.5)
    return values * cdf, cdf + values * density


def contract(left, right, left_dim, right_dim):
    return lax.dot_general(
        left, right, (((left_dim,), (right_dim,)), ((), ())), preferred_element_type=jnp.float32
    )


def _probs(q, k, length, factor):
    scores = lax.dot_general(q, k, (((1,), (1,)), ((), ())), preferred_element_type=jnp.float32) * factor
    col = lax.broadcasted_iota(jnp.int32, scores.shape, 1)
    scores = jnp.where(col < length, scores, NEG)
    top = jnp.max(scores, axis=1, keepdims=True)
    raised = jnp.exp(scores - top)
    return raised / jnp.sum(raised, axis=1, keepdims=True)


def _fwd_kernel(len_ref, q_ref, k_ref, v_ref, out_ref, *, heads, factor):
    length = len_ref[pl.program_id(0)]
    for h in range(heads):
        cols = slice(h * HD, (h + 1) * HD)
        v = v_ref[:, cols]
        probs = _probs(q_ref[:, cols], k_ref[:, cols], length, factor)
        out_ref[:, cols] = jnp.dot(
            probs.astype(jnp.bfloat16), v, preferred_element_type=jnp.float32
        ).astype(out_ref.dtype)


def _bwd_kernel(len_ref, q_ref, k_ref, v_ref, grad_ref, out_ref, *, heads, factor):
    length = len_ref[pl.program_id(0)]
    for h in range(heads):
        cols = slice(h * HD, (h + 1) * HD)
        q = q_ref[:, cols]
        k = k_ref[:, cols]
        v = v_ref[:, cols]
        g = grad_ref[:, cols]
        probs = _probs(q, k, length, factor)
        prob_grad = lax.dot_general(g, v, (((1,), (1,)), ((), ())), preferred_element_type=jnp.float32)
        row_dot = jnp.sum(prob_grad * probs, axis=1, keepdims=True)
        score_grad = (probs * (prob_grad - row_dot)).astype(jnp.bfloat16)
        out_ref[0, :, cols] = (
            jnp.dot(score_grad, k, preferred_element_type=jnp.float32) * factor
        ).astype(out_ref.dtype)
        out_ref[1, :, cols] = (
            lax.dot_general(score_grad, q, (((0,), (0,)), ((), ())), preferred_element_type=jnp.float32)
            * factor
        ).astype(out_ref.dtype)
        out_ref[2, :, cols] = lax.dot_general(
            probs.astype(jnp.bfloat16), g, (((0,), (0,)), ((), ())), preferred_element_type=jnp.float32
        ).astype(out_ref.dtype)


def _group_block(shard):
    return pl.BlockSpec((None, LEN, shard), lambda p, g, n: (g, p, 0))


def attention_forward(queries, keys, values, lengths, factor):
    groups, rows, shard = queries.shape
    grid = (rows // LEN, groups)
    return pl.pallas_call(
        functools.partial(_fwd_kernel, heads=shard // HD, factor=factor),
        out_shape=jax.ShapeDtypeStruct((groups, rows, shard), jnp.bfloat16),
        grid_spec=pltpu.PrefetchScalarGridSpec(
            num_scalar_prefetch=1,
            grid=grid,
            in_specs=[_group_block(shard)] * 3,
            out_specs=_group_block(shard),
        ),
        cost_estimate=pl.CostEstimate(
            flops=4 * rows * LEN * groups * shard,
            transcendentals=rows * LEN * groups * shard // HD,
            bytes_accessed=4 * rows * groups * shard * 2,
        ),
    )(lengths, queries, keys, values)


def attention_backward(queries, keys, values, context_grad, lengths, factor):
    groups, rows, shard = queries.shape
    grid = (rows // LEN, groups)
    return pl.pallas_call(
        functools.partial(_bwd_kernel, heads=shard // HD, factor=factor),
        out_shape=jax.ShapeDtypeStruct((3, groups, rows, shard), jnp.bfloat16),
        grid_spec=pltpu.PrefetchScalarGridSpec(
            num_scalar_prefetch=1,
            grid=grid,
            in_specs=[_group_block(shard)] * 4,
            out_specs=pl.BlockSpec((3, None, LEN, shard), lambda p, g, n: (0, g, p, 0)),
        ),
        cost_estimate=pl.CostEstimate(
            flops=10 * rows * LEN * groups * shard,
            transcendentals=rows * LEN * groups * shard // HD,
            bytes_accessed=7 * rows * groups * shard * 2,
        ),
    )(lengths, queries, keys, values, context_grad)


def dp_pow2(values, dp_size):
    steps = dp_size.bit_length() - 1
    return dp_size == 1 << steps and values.shape[0] % dp_size == 0


def dp_halve(values, dp_size, sum_dtype=None):
    steps = dp_size.bit_length() - 1
    index = lax.axis_index("dp")
    link = values.dtype
    kept = values if sum_dtype is None else values.astype(sum_dtype)
    for step in range(steps):
        bit = (index >> step) & 1
        half = kept.shape[0] // 2
        keep = lax.dynamic_slice_in_dim(kept, bit * half, half)
        give = lax.dynamic_slice_in_dim(kept, (1 - bit) * half, half).astype(link)
        got = lax.ppermute(give, "dp", [(i, i ^ (1 << step)) for i in range(dp_size)])
        kept = keep + got.astype(kept.dtype)
    return kept


def bit_reversed(count):
    steps = count.bit_length() - 1
    return [int(format(i, f"0{steps}b")[::-1], 2) if steps else 0 for i in range(count)]


def dp_double(kept, dp_size):
    steps = dp_size.bit_length() - 1
    index = lax.axis_index("dp")
    for step in reversed(range(steps)):
        bit = (index >> step) & 1
        got = lax.ppermute(kept, "dp", [(i, i ^ (1 << step)) for i in range(dp_size)])
        kept = jnp.concatenate(
            [jnp.where(bit == 0, kept, got), jnp.where(bit == 0, got, kept)]
        )
    return kept


def make_per_device(dp_size):
    def per_device(
        tokens,
        out_grad,
        lengths,
        qkv_weight,
        qkv_bias,
        out_weight,
        out_bias,
        norm1_gain,
        norm1_shift,
        up_weight,
        up_bias,
        down_weight,
        down_bias,
        norm2_gain,
        norm2_shift,
    ):
        rows, width = tokens.shape
        shard = qkv_weight.shape[2]
        groups = width // shard
        passages = rows // LEN
        factor = HD ** (-0.5)

        half_rows = -(-(2 * width + 2) // 8) * 8
        first_half = jnp.pad(
            jnp.concatenate([qkv_weight[0], qkv_weight[1], qkv_bias], axis=0),
            ((0, half_rows - 2 * width - 2), (0, 0)),
        )
        second_half = jnp.pad(
            jnp.concatenate([qkv_weight[2], out_weight.T], axis=0),
            ((0, half_rows - 2 * width), (0, 0)),
        )
        dp_index = lax.axis_index("dp")
        parity = dp_index % 2
        mine = jnp.where(parity == 0, first_half, second_half)
        mine = lax.all_gather(mine, "tensor", axis=0, tiled=False)
        other = lax.ppermute(mine, "dp", [(i, i ^ 1) for i in range(dp_size)])
        first_half = jnp.where(parity == 0, mine, other)
        second_half = jnp.where(parity == 0, other, mine)
        query_weight = first_half[:, :width]
        key_weight = first_half[:, width : 2 * width]
        query_bias = first_half[:, 2 * width]
        value_bias = first_half[:, 2 * width + 1]
        value_weight = second_half[:, :width]
        proj_blocks = second_half[:, width : 2 * width]

        tensor_index = lax.axis_index("tensor")
        own_lengths = lax.dynamic_slice_in_dim(lengths, tensor_index * passages, passages)

        own_tokens = tokens.astype(jnp.float32)
        def project(weight, bias=None):
            out = jnp.einsum("rd,gdj->grj", tokens, weight, preferred_element_type=jnp.float32)
            return (out if bias is None else out + bias[:, None, :]).astype(jnp.bfloat16)

        query_low = project(query_weight, query_bias)
        key_low = project(key_weight)
        value_low = project(value_weight, value_bias)
        context_low = attention_forward(query_low, key_low, value_low, own_lengths, factor)
        attn_out = jnp.einsum(
            "grj,gcj->rc", context_low, proj_blocks, preferred_element_type=jnp.float32
        )
        middle, norm1_back = jax.vjp(
            layer_norm, own_tokens + attn_out + out_bias, norm1_gain, norm1_shift
        )
        middle_low = middle.astype(jnp.bfloat16)
        ffn_rows = lax.all_gather(middle_low, "tensor", axis=0, tiled=True)
        pre_act = jnp.dot(ffn_rows, up_weight, preferred_element_type=jnp.float32) + up_bias
        activated, gelu_slope = gelu_and_slope(pre_act)
        hidden = activated.astype(jnp.bfloat16)
        ffn_out = lax.psum_scatter(
            jnp.dot(hidden, down_weight, preferred_element_type=jnp.float32).astype(jnp.bfloat16),
            "tensor",
            scatter_dimension=0,
            tiled=True,
        ).astype(jnp.float32)
        layer_out, norm2_back = jax.vjp(
            layer_norm, middle + ffn_out + down_bias, norm2_gain, norm2_shift
        )
        second_grad, grad_norm2_gain, grad_norm2_shift = norm2_back(out_grad.astype(jnp.float32))
        branch_grad = second_grad.astype(jnp.bfloat16)
        grad_down_bias = jnp.sum(branch_grad, axis=0, dtype=jnp.float32)
        branch_rows = lax.all_gather(branch_grad, "tensor", axis=0, tiled=True)
        hidden_grad = contract(branch_rows, down_weight, 1, 1)
        grad_down_weight = contract(hidden, branch_rows, 0, 0)
        pre_grad = (hidden_grad * gelu_slope).astype(jnp.bfloat16)
        grad_up_bias = jnp.sum(pre_grad, axis=0, dtype=jnp.float32)
        grad_up_weight = contract(ffn_rows, pre_grad, 0, 0)
        ffn_grads = (grad_up_weight, grad_down_weight)
        halved = all(dp_pow2(g, dp_size) for g in ffn_grads)
        if halved:
            ffn_grads = tuple(dp_halve(g, dp_size) for g in ffn_grads)
        else:
            ffn_grads = lax.psum(ffn_grads, "dp")
        middle_part = lax.psum_scatter(
            contract(pre_grad, up_weight, 1, 1).astype(jnp.bfloat16),
            "tensor",
            scatter_dimension=0,
            tiled=True,
        ).astype(jnp.float32)
        norm1_in, ffn_grads = lax.optimization_barrier((second_grad + middle_part, ffn_grads))
        first_grad, grad_norm1_gain, grad_norm1_shift = norm1_back(norm1_in)
        attn_grad = first_grad.astype(jnp.bfloat16)
        grad_out_bias = jnp.sum(attn_grad, axis=0, dtype=jnp.float32)
        context_grad = jnp.einsum(
            "rc,gcj->grj", attn_grad, proj_blocks, preferred_element_type=jnp.float32
        ).astype(jnp.bfloat16)
        early = jnp.einsum(
            "rc,grj->cgj", attn_grad, context_low, preferred_element_type=jnp.float32
        ).reshape(width, width)
        early_halved = dp_pow2(early, dp_size)
        if early_halved:
            early = dp_halve(early.astype(jnp.bfloat16), dp_size, jnp.float32)
        else:
            early = lax.psum_scatter(early, "dp", scatter_dimension=0, tiled=True)
        proj_grad = attention_backward(
            query_low, key_low, value_low, context_grad, own_lengths, factor
        )
        grad_bias_full = jnp.sum(proj_grad[0::2], axis=2, dtype=jnp.float32).reshape(2, width)
        grad_qkv_full = jnp.einsum(
            "rd,kgrj->kdgj", tokens, proj_grad, preferred_element_type=jnp.float32
        )
        input_part = (
            jnp.einsum("grj,gdj->rd", proj_grad[0], query_weight, preferred_element_type=jnp.float32)
            + jnp.einsum("grj,gdj->rd", proj_grad[1], key_weight, preferred_element_type=jnp.float32)
            + jnp.einsum(
                "grj,gdj->rd", proj_grad[2], value_weight, preferred_element_type=jnp.float32
            )
        )
        input_grad = (first_grad + input_part).astype(jnp.bfloat16)

        small = jnp.stack(
            [
                grad_out_bias,
                grad_norm1_gain,
                grad_norm1_shift,
                grad_down_bias,
                grad_norm2_gain,
                grad_norm2_shift,
            ]
        )
        n_small = small.shape[0]
        small_rep = jnp.tile(small.reshape(n_small, groups, shard), (1, 1, groups)).reshape(
            n_small * groups, width
        )
        up_parts = grad_up_bias.shape[0] // shard
        own_group = (jnp.arange(width) // shard == tensor_index)[None, :]
        up_rep = jnp.where(
            own_group, jnp.tile(grad_up_bias.reshape(up_parts, shard), (1, groups)), 0.0
        )
        tail = jnp.concatenate([grad_bias_full, small_rep, up_rep], axis=0)
        tail_rows = tail.shape[0]
        tail = jnp.pad(tail, ((0, -(-tail_rows // 8) * 8 - tail_rows), (0, 0)))
        late = lax.psum_scatter(
            grad_qkv_full.reshape(3 * width, width).astype(jnp.bfloat16),
            "dp",
            scatter_dimension=0,
            tiled=True,
        ).astype(jnp.float32)
        joined = jnp.concatenate([late, early, tail], axis=0)
        joined = lax.psum_scatter(
            joined.reshape(joined.shape[0], groups, shard).transpose(1, 0, 2),
            "tensor",
            scatter_dimension=0,
            tiled=True,
        )[0]
        if halved:
            ffn_grads = tuple(
                dp_double(g.astype(jnp.bfloat16), dp_size).astype(jnp.float32) for g in ffn_grads
            )
            joined, ffn_grads = lax.optimization_barrier((joined, ffn_grads))
        grad_up_weight, grad_down_weight = ffn_grads
        late_rows = late.shape[0]
        early_rows = early.shape[0]
        joined = lax.all_gather(joined, "dp", axis=0, tiled=False)
        early = joined[:, late_rows : late_rows + early_rows]
        if early_halved:
            order = bit_reversed(dp_size)
            place = [order.index(b) for b in range(dp_size)]
            early = jnp.concatenate([early[p] for p in place], axis=0)
        pieces = [
            joined[:, :late_rows].reshape(-1, shard),
            early.reshape(-1, shard),
            jnp.sum(joined[:, late_rows + early_rows :], axis=0),
        ]
        grad_qkv_weight = pieces[0].reshape(3, width, shard)
        grad_out_weight = pieces[1].T
        tail = pieces[2]
        grad_qkv_bias = tail[:2]
        small_sum = tail[2 : 2 + n_small * groups].reshape(n_small, width)
        grad_up_bias = tail[2 + n_small * groups : 2 + n_small * groups + up_parts].reshape(-1)
        (
            grad_out_bias,
            grad_norm1_gain,
            grad_norm1_shift,
            grad_down_bias,
            grad_norm2_gain,
            grad_norm2_shift,
        ) = [small_sum[i] for i in range(n_small)]
        return (
            layer_out.astype(jnp.bfloat16),
            input_grad,
            grad_qkv_weight,
            grad_qkv_bias,
            grad_out_weight,
            grad_out_bias,
            grad_norm1_gain,
            grad_norm1_shift,
            grad_up_weight,
            grad_up_bias,
            grad_down_weight,
            grad_down_bias,
            grad_norm2_gain,
            grad_norm2_shift,
        )

    return per_device


def solution(mesh):
    placed = (
        P(("dp", "tensor"), None),
        P(("dp", "tensor"), None),
        P("dp"),
        P(None, None, "tensor"),
        P(None, "tensor"),
        P("tensor", None),
        P(),
        P(),
        P(),
        P(None, "tensor"),
        P("tensor"),
        P("tensor", None),
        P(),
        P(),
        P(),
    )
    return jax.shard_map(
        make_per_device(mesh.shape["dp"]),
        mesh=mesh,
        in_specs=placed,
        out_specs=(
            P(("dp", "tensor"), None),
            P(("dp", "tensor"), None),
            P(None, None, "tensor"),
            P(None, "tensor"),
            P("tensor", None),
            P(),
            P(),
            P(),
            P(None, "tensor"),
            P("tensor"),
            P("tensor", None),
            P(),
            P(),
            P(),
        ),
        check_vma=False,
    )
```

```python
import functools

import jax
import jax.numpy as jnp
from jax import lax
from jax.experimental import pallas as pl
from jax.experimental.pallas import tpu as pltpu
from jax.sharding import PartitionSpec as P

HD = 64
LEN = 512


EPS = 1e-12
NEG = -1e30


def layer_norm(values, gain_vec, shift_vec):
    center = values - jnp.mean(values, axis=-1, keepdims=True)
    spread = jnp.mean(center * center, axis=-1, keepdims=True)
    return center * lax.rsqrt(spread + EPS) * gain_vec + shift_vec


def gelu_and_slope(values):
    cdf = 0.5 * (1.0 + lax.erf(values * (2.0 ** -0.5)))
    density = jnp.exp(-0.5 * values * values) * ((2.0 * jnp.pi) ** -0.5)
    return values * cdf, cdf + values * density


def contract(left, right, left_dim, right_dim):
    return lax.dot_general(
        left, right, (((left_dim,), (right_dim,)), ((), ())), preferred_element_type=jnp.float32
    )


def _probs(q, k, length, factor):
    scores = lax.dot_general(q, k, (((1,), (1,)), ((), ())), preferred_element_type=jnp.float32) * factor
    col = lax.broadcasted_iota(jnp.int32, scores.shape, 1)
    scores = jnp.where(col < length, scores, NEG)
    top = jnp.max(scores, axis=1, keepdims=True)
    raised = jnp.exp(scores - top)
    return raised / jnp.sum(raised, axis=1, keepdims=True)


def _fwd_kernel(len_ref, q_ref, k_ref, v_ref, out_ref, *, heads, factor):
    length = len_ref[pl.program_id(0)]
    for h in range(heads):
        cols = slice(h * HD, (h + 1) * HD)
        v = v_ref[:, cols]
        probs = _probs(q_ref[:, cols], k_ref[:, cols], length, factor)
        out_ref[:, cols] = jnp.dot(
            probs.astype(jnp.bfloat16), v, preferred_element_type=jnp.float32
        ).astype(out_ref.dtype)


def _bwd_kernel(len_ref, q_ref, k_ref, v_ref, grad_ref, out_ref, *, factor):
    length = len_ref[pl.program_id(0)]
    groups, _, shard = q_ref.shape
    for group in range(groups):
        for h in range(shard // HD):
            cols = slice(h * HD, (h + 1) * HD)
            wide = slice(group * shard + h * HD, group * shard + (h + 1) * HD)
            q = q_ref[group, :, cols]
            k = k_ref[group, :, cols]
            v = v_ref[group, :, cols]
            g = grad_ref[group, :, cols]
            probs = _probs(q, k, length, factor)
            prob_grad = lax.dot_general(
                g, v, (((1,), (1,)), ((), ())), preferred_element_type=jnp.float32
            )
            row_dot = jnp.sum(prob_grad * probs, axis=1, keepdims=True)
            score_grad = (probs * (prob_grad - row_dot)).astype(jnp.bfloat16)
            out_ref[0, :, wide] = (
                jnp.dot(score_grad, k, preferred_element_type=jnp.float32) * factor
            ).astype(out_ref.dtype)
            out_ref[1, :, wide] = (
                lax.dot_general(
                    score_grad, q, (((0,), (0,)), ((), ())), preferred_element_type=jnp.float32
                )
                * factor
            ).astype(out_ref.dtype)
            out_ref[2, :, wide] = lax.dot_general(
                probs.astype(jnp.bfloat16),
                g,
                (((0,), (0,)), ((), ())),
                preferred_element_type=jnp.float32,
            ).astype(out_ref.dtype)


def _group_block(shard):
    return pl.BlockSpec((None, LEN, shard), lambda p, g, n: (g, p, 0))


def attention_forward(queries, keys, values, lengths, factor):
    groups, rows, shard = queries.shape
    grid = (rows // LEN, groups)
    return pl.pallas_call(
        functools.partial(_fwd_kernel, heads=shard // HD, factor=factor),
        out_shape=jax.ShapeDtypeStruct((groups, rows, shard), jnp.bfloat16),
        grid_spec=pltpu.PrefetchScalarGridSpec(
            num_scalar_prefetch=1,
            grid=grid,
            in_specs=[_group_block(shard)] * 3,
            out_specs=_group_block(shard),
        ),
        cost_estimate=pl.CostEstimate(
            flops=4 * rows * LEN * groups * shard,
            transcendentals=rows * LEN * groups * shard // HD,
            bytes_accessed=4 * rows * groups * shard * 2,
        ),
    )(lengths, queries, keys, values)


def attention_backward(queries, keys, values, context_grad, lengths, factor):
    groups, rows, shard = queries.shape
    width = groups * shard
    whole = pl.BlockSpec((groups, LEN, shard), lambda p, n: (0, p, 0))
    return pl.pallas_call(
        functools.partial(_bwd_kernel, factor=factor),
        out_shape=jax.ShapeDtypeStruct((3, rows, width), jnp.bfloat16),
        grid_spec=pltpu.PrefetchScalarGridSpec(
            num_scalar_prefetch=1,
            grid=(rows // LEN,),
            in_specs=[whole] * 4,
            out_specs=pl.BlockSpec((3, LEN, width), lambda p, n: (0, p, 0)),
        ),
        cost_estimate=pl.CostEstimate(
            flops=10 * rows * LEN * width,
            transcendentals=rows * LEN * width // HD,
            bytes_accessed=7 * rows * width * 2,
        ),
    )(lengths, queries, keys, values, context_grad)


def dp_pow2(values, dp_size):
    steps = dp_size.bit_length() - 1
    return dp_size == 1 << steps and values.shape[0] % dp_size == 0


def dp_halve(values, dp_size, sum_dtype=None):
    steps = dp_size.bit_length() - 1
    index = lax.axis_index("dp")
    link = values.dtype
    kept = values if sum_dtype is None else values.astype(sum_dtype)
    for step in range(steps):
        bit = (index >> step) & 1
        half = kept.shape[0] // 2
        keep = lax.dynamic_slice_in_dim(kept, bit * half, half)
        give = lax.dynamic_slice_in_dim(kept, (1 - bit) * half, half).astype(link)
        got = lax.ppermute(give, "dp", [(i, i ^ (1 << step)) for i in range(dp_size)])
        kept = keep + got.astype(kept.dtype)
    return kept


def bit_reversed(count):
    steps = count.bit_length() - 1
    return [int(format(i, f"0{steps}b")[::-1], 2) if steps else 0 for i in range(count)]


def dp_double(kept, dp_size):
    steps = dp_size.bit_length() - 1
    index = lax.axis_index("dp")
    for step in reversed(range(steps)):
        bit = (index >> step) & 1
        got = lax.ppermute(kept, "dp", [(i, i ^ (1 << step)) for i in range(dp_size)])
        kept = jnp.concatenate(
            [jnp.where(bit == 0, kept, got), jnp.where(bit == 0, got, kept)]
        )
    return kept


def make_per_device(dp_size):
    def per_device(
        tokens,
        out_grad,
        lengths,
        qkv_weight,
        qkv_bias,
        out_weight,
        out_bias,
        norm1_gain,
        norm1_shift,
        up_weight,
        up_bias,
        down_weight,
        down_bias,
        norm2_gain,
        norm2_shift,
    ):
        rows, width = tokens.shape
        shard = qkv_weight.shape[2]
        groups = width // shard
        passages = rows // LEN
        factor = HD ** (-0.5)

        half_rows = -(-(2 * width + 2) // 8) * 8
        first_half = jnp.pad(
            jnp.concatenate([qkv_weight[0], qkv_weight[1], qkv_bias], axis=0),
            ((0, half_rows - 2 * width - 2), (0, 0)),
        )
        second_half = jnp.pad(
            jnp.concatenate([qkv_weight[2], out_weight.T], axis=0),
            ((0, half_rows - 2 * width), (0, 0)),
        )
        dp_index = lax.axis_index("dp")
        parity = dp_index % 2
        mine = jnp.where(parity == 0, first_half, second_half)
        mine = lax.all_gather(mine, "tensor", axis=0, tiled=False)
        other = lax.ppermute(mine, "dp", [(i, i ^ 1) for i in range(dp_size)])
        first_half = jnp.where(parity == 0, mine, other)
        second_half = jnp.where(parity == 0, other, mine)
        query_weight = first_half[:, :width]
        key_weight = first_half[:, width : 2 * width]
        query_bias = first_half[:, 2 * width]
        value_bias = first_half[:, 2 * width + 1]
        value_weight = second_half[:, :width]
        proj_blocks = second_half[:, width : 2 * width]

        tensor_index = lax.axis_index("tensor")
        own_lengths = lax.dynamic_slice_in_dim(lengths, tensor_index * passages, passages)

        own_tokens = tokens.astype(jnp.float32)
        def project(weight, bias=None):
            out = jnp.einsum("rd,gdj->grj", tokens, weight, preferred_element_type=jnp.float32)
            return (out if bias is None else out + bias[:, None, :]).astype(jnp.bfloat16)

        query_low = project(query_weight, query_bias)
        key_low = project(key_weight)
        value_low = project(value_weight, value_bias)
        context_low = attention_forward(query_low, key_low, value_low, own_lengths, factor)
        attn_out = jnp.einsum(
            "grj,gcj->rc", context_low, proj_blocks, preferred_element_type=jnp.float32
        )
        middle, norm1_back = jax.vjp(
            layer_norm, own_tokens + attn_out + out_bias, norm1_gain, norm1_shift
        )
        middle_low = middle.astype(jnp.bfloat16)
        ffn_rows = lax.all_gather(middle_low, "tensor", axis=0, tiled=True)
        pre_act = jnp.dot(ffn_rows, up_weight, preferred_element_type=jnp.float32) + up_bias
        activated, gelu_slope = gelu_and_slope(pre_act)
        hidden = activated.astype(jnp.bfloat16)
        ffn_out = lax.psum_scatter(
            jnp.dot(hidden, down_weight, preferred_element_type=jnp.float32).astype(jnp.bfloat16),
            "tensor",
            scatter_dimension=0,
            tiled=True,
        ).astype(jnp.float32)
        layer_out, norm2_back = jax.vjp(
            layer_norm, middle + ffn_out + down_bias, norm2_gain, norm2_shift
        )
        second_grad, grad_norm2_gain, grad_norm2_shift = norm2_back(out_grad.astype(jnp.float32))
        branch_grad = second_grad.astype(jnp.bfloat16)
        grad_down_bias = jnp.sum(branch_grad, axis=0, dtype=jnp.float32)
        branch_rows = lax.all_gather(branch_grad, "tensor", axis=0, tiled=True)
        hidden_grad = contract(branch_rows, down_weight, 1, 1)
        grad_down_weight = contract(hidden, branch_rows, 0, 0)
        pre_grad = (hidden_grad * gelu_slope).astype(jnp.bfloat16)
        grad_up_bias = jnp.sum(pre_grad, axis=0, dtype=jnp.float32)
        grad_up_weight = contract(ffn_rows, pre_grad, 0, 0)
        ffn_grads = (grad_up_weight, grad_down_weight)
        halved = all(dp_pow2(g, dp_size) for g in ffn_grads)
        if halved:
            ffn_grads = tuple(dp_halve(g, dp_size) for g in ffn_grads)
        else:
            ffn_grads = lax.psum(ffn_grads, "dp")
        middle_part = lax.psum_scatter(
            contract(pre_grad, up_weight, 1, 1).astype(jnp.bfloat16),
            "tensor",
            scatter_dimension=0,
            tiled=True,
        ).astype(jnp.float32)
        norm1_in, ffn_grads = lax.optimization_barrier((second_grad + middle_part, ffn_grads))
        first_grad, grad_norm1_gain, grad_norm1_shift = norm1_back(norm1_in)
        attn_grad = first_grad.astype(jnp.bfloat16)
        grad_out_bias = jnp.sum(attn_grad, axis=0, dtype=jnp.float32)
        context_grad = jnp.einsum(
            "rc,gcj->grj", attn_grad, proj_blocks, preferred_element_type=jnp.float32
        ).astype(jnp.bfloat16)
        early = jnp.einsum(
            "rc,grj->cgj", attn_grad, context_low, preferred_element_type=jnp.float32
        ).reshape(width, width)
        early_halved = dp_pow2(early, dp_size)
        if early_halved:
            early = dp_halve(early.astype(jnp.bfloat16), dp_size, jnp.float32)
        else:
            early = lax.psum_scatter(early, "dp", scatter_dimension=0, tiled=True)
        proj_grad = attention_backward(
            query_low, key_low, value_low, context_grad, own_lengths, factor
        )
        grad_bias_full = jnp.sum(proj_grad[0::2], axis=1, dtype=jnp.float32)
        grad_qkv_full = jnp.einsum(
            "rd,kre->kde", tokens, proj_grad, preferred_element_type=jnp.float32
        )

        def back_project(grad, weight):
            return jnp.einsum(
                "rgj,gdj->rd",
                grad.reshape(rows, groups, shard),
                weight,
                preferred_element_type=jnp.float32,
            )

        input_part = (
            back_project(proj_grad[0], query_weight)
            + back_project(proj_grad[1], key_weight)
            + back_project(proj_grad[2], value_weight)
        )
        input_grad = (first_grad + input_part).astype(jnp.bfloat16)

        small = jnp.stack(
            [
                grad_out_bias,
                grad_norm1_gain,
                grad_norm1_shift,
                grad_down_bias,
                grad_norm2_gain,
                grad_norm2_shift,
            ]
        )
        n_small = small.shape[0]
        small_rep = jnp.tile(small.reshape(n_small, groups, shard), (1, 1, groups)).reshape(
            n_small * groups, width
        )
        up_parts = grad_up_bias.shape[0] // shard
        own_group = (jnp.arange(width) // shard == tensor_index)[None, :]
        up_rep = jnp.where(
            own_group, jnp.tile(grad_up_bias.reshape(up_parts, shard), (1, groups)), 0.0
        )
        tail = jnp.concatenate([grad_bias_full, small_rep, up_rep], axis=0)
        tail_rows = tail.shape[0]
        tail = jnp.pad(tail, ((0, -(-tail_rows // 8) * 8 - tail_rows), (0, 0)))
        late = lax.psum_scatter(
            grad_qkv_full.reshape(3 * width, width).astype(jnp.bfloat16),
            "dp",
            scatter_dimension=0,
            tiled=True,
        ).astype(jnp.float32)
        joined = jnp.concatenate([late, early, tail], axis=0)
        joined = lax.psum_scatter(
            joined.reshape(joined.shape[0], groups, shard).transpose(1, 0, 2),
            "tensor",
            scatter_dimension=0,
            tiled=True,
        )[0]
        if halved:
            ffn_grads = tuple(
                dp_double(g.astype(jnp.bfloat16), dp_size).astype(jnp.float32) for g in ffn_grads
            )
            joined, ffn_grads = lax.optimization_barrier((joined, ffn_grads))
        grad_up_weight, grad_down_weight = ffn_grads
        late_rows = late.shape[0]
        early_rows = early.shape[0]
        joined = lax.all_gather(joined, "dp", axis=0, tiled=False)
        early = joined[:, late_rows : late_rows + early_rows]
        if early_halved:
            order = bit_reversed(dp_size)
            place = [order.index(b) for b in range(dp_size)]
            early = jnp.concatenate([early[p] for p in place], axis=0)
        pieces = [
            joined[:, :late_rows].reshape(-1, shard),
            early.reshape(-1, shard),
            jnp.sum(joined[:, late_rows + early_rows :], axis=0),
        ]
        grad_qkv_weight = pieces[0].reshape(3, width, shard)
        grad_out_weight = pieces[1].T
        tail = pieces[2]
        grad_qkv_bias = tail[:2]
        small_sum = tail[2 : 2 + n_small * groups].reshape(n_small, width)
        grad_up_bias = tail[2 + n_small * groups : 2 + n_small * groups + up_parts].reshape(-1)
        (
            grad_out_bias,
            grad_norm1_gain,
            grad_norm1_shift,
            grad_down_bias,
            grad_norm2_gain,
            grad_norm2_shift,
        ) = [small_sum[i] for i in range(n_small)]
        return (
            layer_out.astype(jnp.bfloat16),
            input_grad,
            grad_qkv_weight,
            grad_qkv_bias,
            grad_out_weight,
            grad_out_bias,
            grad_norm1_gain,
            grad_norm1_shift,
            grad_up_weight,
            grad_up_bias,
            grad_down_weight,
            grad_down_bias,
            grad_norm2_gain,
            grad_norm2_shift,
        )

    return per_device


def solution(mesh):
    placed = (
        P(("dp", "tensor"), None),
        P(("dp", "tensor"), None),
        P("dp"),
        P(None, None, "tensor"),
        P(None, "tensor"),
        P("tensor", None),
        P(),
        P(),
        P(),
        P(None, "tensor"),
        P("tensor"),
        P("tensor", None),
        P(),
        P(),
        P(),
    )
    return jax.shard_map(
        make_per_device(mesh.shape["dp"]),
        mesh=mesh,
        in_specs=placed,
        out_specs=(
            P(("dp", "tensor"), None),
            P(("dp", "tensor"), None),
            P(None, None, "tensor"),
            P(None, "tensor"),
            P("tensor", None),
            P(),
            P(),
            P(),
            P(None, "tensor"),
            P("tensor"),
            P("tensor", None),
            P(),
            P(),
            P(),
        ),
        check_vma=False,
    )
```

```python
import functools

import jax
import jax.numpy as jnp
from jax import lax
from jax.experimental import pallas as pl
from jax.experimental.pallas import tpu as pltpu
from jax.sharding import PartitionSpec as P

HD = 64
LEN = 512


EPS = 1e-12
NEG = -1e30


def layer_norm(values, gain_vec, shift_vec):
    center = values - jnp.mean(values, axis=-1, keepdims=True)
    spread = jnp.mean(center * center, axis=-1, keepdims=True)
    return center * lax.rsqrt(spread + EPS) * gain_vec + shift_vec


def gelu_and_slope(values):
    cdf = 0.5 * (1.0 + lax.erf(values * (2.0 ** -0.5)))
    density = jnp.exp(-0.5 * values * values) * ((2.0 * jnp.pi) ** -0.5)
    return values * cdf, cdf + values * density


def contract(left, right, left_dim, right_dim):
    return lax.dot_general(
        left, right, (((left_dim,), (right_dim,)), ((), ())), preferred_element_type=jnp.float32
    )


def _probs(q, k, length, factor):
    scores = lax.dot_general(q, k, (((1,), (1,)), ((), ())), preferred_element_type=jnp.float32) * factor
    col = lax.broadcasted_iota(jnp.int32, scores.shape, 1)
    scores = jnp.where(col < length, scores, NEG)
    top = jnp.max(scores, axis=1, keepdims=True)
    raised = jnp.exp(scores - top)
    return raised / jnp.sum(raised, axis=1, keepdims=True)


def _fwd_kernel(len_ref, q_ref, k_ref, v_ref, out_ref, *, heads, factor):
    length = len_ref[pl.program_id(0)]
    for h in range(heads):
        cols = slice(h * HD, (h + 1) * HD)
        probs = _probs(q_ref[:, cols], k_ref[:, cols], length, factor)
        out_ref[:, cols] = jnp.dot(
            probs.astype(jnp.bfloat16), v_ref[:, cols], preferred_element_type=jnp.float32
        ).astype(out_ref.dtype)


def _bwd_kernel(len_ref, q_ref, k_ref, v_ref, grad_ref, out_ref, *, heads, factor):
    length = len_ref[pl.program_id(0)]
    for h in range(heads):
        cols = slice(h * HD, (h + 1) * HD)
        q = q_ref[:, cols]
        k = k_ref[:, cols]
        v = v_ref[:, cols]
        g = grad_ref[:, cols]
        probs = _probs(q, k, length, factor)
        prob_grad = lax.dot_general(g, v, (((1,), (1,)), ((), ())), preferred_element_type=jnp.float32)
        row_dot = jnp.sum(prob_grad * probs, axis=1, keepdims=True)
        score_grad = (probs * (prob_grad - row_dot)).astype(jnp.bfloat16)
        out_ref[0, :, cols] = (
            jnp.dot(score_grad, k, preferred_element_type=jnp.float32) * factor
        ).astype(out_ref.dtype)
        out_ref[1, :, cols] = (
            lax.dot_general(score_grad, q, (((0,), (0,)), ((), ())), preferred_element_type=jnp.float32)
            * factor
        ).astype(out_ref.dtype)
        out_ref[2, :, cols] = lax.dot_general(
            probs.astype(jnp.bfloat16), g, (((0,), (0,)), ((), ())), preferred_element_type=jnp.float32
        ).astype(out_ref.dtype)


def attention_forward(queries, keys, values, lengths, factor, pair=2):
    rows, width = queries.shape
    block = pl.BlockSpec((LEN, pair * HD), lambda p, i, n: (p, i))
    return pl.pallas_call(
        functools.partial(_fwd_kernel, heads=pair, factor=factor),
        out_shape=jax.ShapeDtypeStruct((rows, width), jnp.bfloat16),
        grid_spec=pltpu.PrefetchScalarGridSpec(
            num_scalar_prefetch=1,
            grid=(rows // LEN, width // (pair * HD)),
            in_specs=[block] * 3,
            out_specs=block,
        ),
        cost_estimate=pl.CostEstimate(
            flops=4 * rows * LEN * width,
            transcendentals=rows * LEN * width // HD,
            bytes_accessed=4 * rows * width * 2,
        ),
    )(lengths, queries, keys, values)


def attention_backward(queries, keys, values, context_grad, lengths, factor, pair=2):
    rows, width = queries.shape
    block = pl.BlockSpec((LEN, pair * HD), lambda p, i, n: (p, i))
    return pl.pallas_call(
        functools.partial(_bwd_kernel, heads=pair, factor=factor),
        out_shape=jax.ShapeDtypeStruct((3, rows, width), jnp.bfloat16),
        grid_spec=pltpu.PrefetchScalarGridSpec(
            num_scalar_prefetch=1,
            grid=(rows // LEN, width // (pair * HD)),
            in_specs=[block] * 4,
            out_specs=pl.BlockSpec((3, LEN, pair * HD), lambda p, i, n: (0, p, i)),
        ),
        cost_estimate=pl.CostEstimate(
            flops=10 * rows * LEN * width,
            transcendentals=rows * LEN * width // HD,
            bytes_accessed=7 * rows * width * 2,
        ),
    )(lengths, queries, keys, values, context_grad)


def dp_pow2(values, dp_size):
    steps = dp_size.bit_length() - 1
    return dp_size == 1 << steps and values.shape[0] % dp_size == 0


def dp_halve(values, dp_size, sum_dtype=None):
    steps = dp_size.bit_length() - 1
    index = lax.axis_index("dp")
    link = values.dtype
    kept = values if sum_dtype is None else values.astype(sum_dtype)
    for step in range(steps):
        bit = (index >> step) & 1
        half = kept.shape[0] // 2
        keep = lax.dynamic_slice_in_dim(kept, bit * half, half)
        give = lax.dynamic_slice_in_dim(kept, (1 - bit) * half, half).astype(link)
        got = lax.ppermute(give, "dp", [(i, i ^ (1 << step)) for i in range(dp_size)])
        kept = keep + got.astype(kept.dtype)
    return kept


def bit_reversed(count):
    steps = count.bit_length() - 1
    return [int(format(i, f"0{steps}b")[::-1], 2) if steps else 0 for i in range(count)]


def dp_double(kept, dp_size):
    steps = dp_size.bit_length() - 1
    index = lax.axis_index("dp")
    for step in reversed(range(steps)):
        bit = (index >> step) & 1
        got = lax.ppermute(kept, "dp", [(i, i ^ (1 << step)) for i in range(dp_size)])
        kept = jnp.concatenate(
            [jnp.where(bit == 0, kept, got), jnp.where(bit == 0, got, kept)]
        )
    return kept


def make_per_device(dp_size):
    def per_device(
        tokens,
        out_grad,
        lengths,
        qkv_weight,
        qkv_bias,
        out_weight,
        out_bias,
        norm1_gain,
        norm1_shift,
        up_weight,
        up_bias,
        down_weight,
        down_bias,
        norm2_gain,
        norm2_shift,
    ):
        rows, width = tokens.shape
        shard = qkv_weight.shape[2]
        groups = width // shard
        passages = rows // LEN
        factor = HD ** (-0.5)

        half_rows = -(-(2 * width + 2) // 8) * 8
        first_half = jnp.pad(
            jnp.concatenate([qkv_weight[0], qkv_weight[1], qkv_bias], axis=0),
            ((0, half_rows - 2 * width - 2), (0, 0)),
        )
        second_half = jnp.pad(
            jnp.concatenate([qkv_weight[2], out_weight.T], axis=0),
            ((0, half_rows - 2 * width), (0, 0)),
        )
        dp_index = lax.axis_index("dp")
        parity = dp_index % 2
        mine = jnp.where(parity == 0, first_half, second_half)
        mine = lax.all_gather(mine, "tensor", axis=0, tiled=False)
        other = lax.ppermute(mine, "dp", [(i, i ^ 1) for i in range(dp_size)])
        first_half = jnp.where(parity == 0, mine, other)
        second_half = jnp.where(parity == 0, other, mine)
        query_weight = first_half[:, :width]
        key_weight = first_half[:, width : 2 * width]
        query_bias = first_half[:, 2 * width]
        value_bias = first_half[:, 2 * width + 1]
        value_weight = second_half[:, :width]
        proj_blocks = second_half[:, width : 2 * width]

        tensor_index = lax.axis_index("tensor")
        own_lengths = lax.dynamic_slice_in_dim(lengths, tensor_index * passages, passages)

        own_tokens = tokens.astype(jnp.float32)
        def project(weight, bias=None):
            out = jnp.einsum("rd,gdj->rgj", tokens, weight, preferred_element_type=jnp.float32)
            out = out if bias is None else out + bias
            return out.astype(jnp.bfloat16).reshape(rows, width)

        query_low = project(query_weight, query_bias)
        key_low = project(key_weight)
        value_low = project(value_weight, value_bias)
        context_low = attention_forward(query_low, key_low, value_low, own_lengths, factor)
        attn_out = jnp.einsum(
            "rgj,gcj->rc",
            context_low.reshape(rows, groups, shard),
            proj_blocks,
            preferred_element_type=jnp.float32,
        )
        middle, norm1_back = jax.vjp(
            layer_norm, own_tokens + attn_out + out_bias, norm1_gain, norm1_shift
        )
        middle_low = middle.astype(jnp.bfloat16)
        ffn_rows = lax.all_gather(middle_low, "tensor", axis=0, tiled=True)
        pre_act = jnp.dot(ffn_rows, up_weight, preferred_element_type=jnp.float32) + up_bias
        activated, gelu_slope = gelu_and_slope(pre_act)
        hidden = activated.astype(jnp.bfloat16)
        ffn_out = lax.psum_scatter(
            jnp.dot(hidden, down_weight, preferred_element_type=jnp.float32).astype(jnp.bfloat16),
            "tensor",
            scatter_dimension=0,
            tiled=True,
        ).astype(jnp.float32)
        layer_out, norm2_back = jax.vjp(
            layer_norm, middle + ffn_out + down_bias, norm2_gain, norm2_shift
        )
        second_grad, grad_norm2_gain, grad_norm2_shift = norm2_back(out_grad.astype(jnp.float32))
        branch_grad = second_grad.astype(jnp.bfloat16)
        grad_down_bias = jnp.sum(branch_grad, axis=0, dtype=jnp.float32)
        branch_rows = lax.all_gather(branch_grad, "tensor", axis=0, tiled=True)
        hidden_grad = contract(branch_rows, down_weight, 1, 1)
        grad_down_weight = contract(hidden, branch_rows, 0, 0)
        pre_grad = (hidden_grad * gelu_slope).astype(jnp.bfloat16)
        grad_up_bias = jnp.sum(pre_grad, axis=0, dtype=jnp.float32)
        grad_up_weight = contract(ffn_rows, pre_grad, 0, 0)
        ffn_grads = (grad_up_weight, grad_down_weight)
        halved = all(dp_pow2(g, dp_size) for g in ffn_grads)
        if halved:
            ffn_grads = tuple(dp_halve(g, dp_size) for g in ffn_grads)
        else:
            ffn_grads = lax.psum(ffn_grads, "dp")
        middle_part = lax.psum_scatter(
            contract(pre_grad, up_weight, 1, 1).astype(jnp.bfloat16),
            "tensor",
            scatter_dimension=0,
            tiled=True,
        ).astype(jnp.float32)
        norm1_in, ffn_grads = lax.optimization_barrier((second_grad + middle_part, ffn_grads))
        first_grad, grad_norm1_gain, grad_norm1_shift = norm1_back(norm1_in)
        attn_grad = first_grad.astype(jnp.bfloat16)
        grad_out_bias = jnp.sum(attn_grad, axis=0, dtype=jnp.float32)
        context_grad = (
            jnp.einsum("rc,gcj->rgj", attn_grad, proj_blocks, preferred_element_type=jnp.float32)
            .astype(jnp.bfloat16)
            .reshape(rows, width)
        )
        early = contract(attn_grad, context_low, 0, 0)
        early_halved = dp_pow2(early, dp_size)
        if early_halved:
            early = dp_halve(early.astype(jnp.bfloat16), dp_size, jnp.float32)
        else:
            early = lax.psum_scatter(early, "dp", scatter_dimension=0, tiled=True)
        proj_grad = attention_backward(
            query_low, key_low, value_low, context_grad, own_lengths, factor
        )
        grad_bias_full = jnp.sum(proj_grad[0::2], axis=1, dtype=jnp.float32)
        grad_qkv_full = jnp.einsum(
            "rd,kre->kde", tokens, proj_grad, preferred_element_type=jnp.float32
        )

        def back_project(grad, weight):
            return jnp.einsum(
                "rgj,gdj->rd",
                grad.reshape(rows, groups, shard),
                weight,
                preferred_element_type=jnp.float32,
            )

        input_part = (
            back_project(proj_grad[0], query_weight)
            + back_project(proj_grad[1], key_weight)
            + back_project(proj_grad[2], value_weight)
        )
        input_grad = (first_grad + input_part).astype(jnp.bfloat16)

        small = jnp.stack(
            [
                grad_out_bias,
                grad_norm1_gain,
                grad_norm1_shift,
                grad_down_bias,
                grad_norm2_gain,
                grad_norm2_shift,
            ]
        )
        n_small = small.shape[0]
        small_rep = jnp.tile(small.reshape(n_small, groups, shard), (1, 1, groups)).reshape(
            n_small * groups, width
        )
        up_parts = grad_up_bias.shape[0] // shard
        own_group = (jnp.arange(width) // shard == tensor_index)[None, :]
        up_rep = jnp.where(
            own_group, jnp.tile(grad_up_bias.reshape(up_parts, shard), (1, groups)), 0.0
        )
        tail = jnp.concatenate([grad_bias_full, small_rep, up_rep], axis=0)
        tail_rows = tail.shape[0]
        tail = jnp.pad(tail, ((0, -(-tail_rows // 8) * 8 - tail_rows), (0, 0)))
        late = lax.psum_scatter(
            grad_qkv_full.reshape(3 * width, width).astype(jnp.bfloat16),
            "dp",
            scatter_dimension=0,
            tiled=True,
        ).astype(jnp.float32)
        joined = jnp.concatenate([late, early, tail], axis=0)
        joined = lax.psum_scatter(
            joined.reshape(joined.shape[0], groups, shard).transpose(1, 0, 2),
            "tensor",
            scatter_dimension=0,
            tiled=True,
        )[0]
        if halved:
            ffn_grads = tuple(
                dp_double(g.astype(jnp.bfloat16), dp_size).astype(jnp.float32) for g in ffn_grads
            )
            joined, ffn_grads = lax.optimization_barrier((joined, ffn_grads))
        grad_up_weight, grad_down_weight = ffn_grads
        late_rows = late.shape[0]
        early_rows = early.shape[0]
        joined = lax.all_gather(joined, "dp", axis=0, tiled=False)
        early = joined[:, late_rows : late_rows + early_rows]
        if early_halved:
            order = bit_reversed(dp_size)
            place = [order.index(b) for b in range(dp_size)]
            early = jnp.concatenate([early[p] for p in place], axis=0)
        pieces = [
            joined[:, :late_rows].reshape(-1, shard),
            early.reshape(-1, shard),
            jnp.sum(joined[:, late_rows + early_rows :], axis=0),
        ]
        grad_qkv_weight = pieces[0].reshape(3, width, shard)
        grad_out_weight = pieces[1].T
        tail = pieces[2]
        grad_qkv_bias = tail[:2]
        small_sum = tail[2 : 2 + n_small * groups].reshape(n_small, width)
        grad_up_bias = tail[2 + n_small * groups : 2 + n_small * groups + up_parts].reshape(-1)
        (
            grad_out_bias,
            grad_norm1_gain,
            grad_norm1_shift,
            grad_down_bias,
            grad_norm2_gain,
            grad_norm2_shift,
        ) = [small_sum[i] for i in range(n_small)]
        return (
            layer_out.astype(jnp.bfloat16),
            input_grad,
            grad_qkv_weight,
            grad_qkv_bias,
            grad_out_weight,
            grad_out_bias,
            grad_norm1_gain,
            grad_norm1_shift,
            grad_up_weight,
            grad_up_bias,
            grad_down_weight,
            grad_down_bias,
            grad_norm2_gain,
            grad_norm2_shift,
        )

    return per_device


def solution(mesh):
    placed = (
        P(("dp", "tensor"), None),
        P(("dp", "tensor"), None),
        P("dp"),
        P(None, None, "tensor"),
        P(None, "tensor"),
        P("tensor", None),
        P(),
        P(),
        P(),
        P(None, "tensor"),
        P("tensor"),
        P("tensor", None),
        P(),
        P(),
        P(),
    )
    return jax.shard_map(
        make_per_device(mesh.shape["dp"]),
        mesh=mesh,
        in_specs=placed,
        out_specs=(
            P(("dp", "tensor"), None),
            P(("dp", "tensor"), None),
            P(None, None, "tensor"),
            P(None, "tensor"),
            P("tensor", None),
            P(),
            P(),
            P(),
            P(None, "tensor"),
            P("tensor"),
            P("tensor", None),
            P(),
            P(),
            P(),
        ),
        check_vma=False,
    )
```

```python
import functools

import jax
import jax.numpy as jnp
from jax import lax
from jax.experimental import pallas as pl
from jax.experimental.pallas import tpu as pltpu
from jax.sharding import PartitionSpec as P

HD = 64
LEN = 512


EPS = 1e-12
NEG = -1e30


def layer_norm(values, gain_vec, shift_vec):
    center = values - jnp.mean(values, axis=-1, keepdims=True)
    spread = jnp.mean(center * center, axis=-1, keepdims=True)
    return center * lax.rsqrt(spread + EPS) * gain_vec + shift_vec


def gelu_and_slope(values):
    cdf = 0.5 * (1.0 + lax.erf(values * (2.0 ** -0.5)))
    density = jnp.exp(-0.5 * values * values) * ((2.0 * jnp.pi) ** -0.5)
    return values * cdf, cdf + values * density


def contract(left, right, left_dim, right_dim):
    return lax.dot_general(
        left, right, (((left_dim,), (right_dim,)), ((), ())), preferred_element_type=jnp.float32
    )


def _probs(q, k, length, factor):
    scores = lax.dot_general(q, k, (((1,), (1,)), ((), ())), preferred_element_type=jnp.float32) * factor
    col = lax.broadcasted_iota(jnp.int32, scores.shape, 1)
    scores = jnp.where(col < length, scores, NEG)
    top = jnp.max(scores, axis=1, keepdims=True)
    raised = jnp.exp(scores - top)
    return raised / jnp.sum(raised, axis=1, keepdims=True)


def _fwd_kernel(len_ref, q_ref, k_ref, v_ref, out_ref, *, heads, factor):
    length = len_ref[pl.program_id(0)]
    for h in range(heads):
        cols = slice(h * HD, (h + 1) * HD)
        probs = _probs(q_ref[:, cols], k_ref[:, cols], length, factor)
        out_ref[:, cols] = jnp.dot(
            probs.astype(jnp.bfloat16), v_ref[:, cols], preferred_element_type=jnp.float32
        ).astype(out_ref.dtype)


def _bwd_kernel(len_ref, q_ref, k_ref, v_ref, grad_ref, *rest, heads, factor):
    if len(rest) == 3:
        tokens_ref, out_ref, wgrad_ref = rest
    else:
        (out_ref,), tokens_ref = rest, None
    length = len_ref[pl.program_id(0)]
    for h in range(heads):
        cols = slice(h * HD, (h + 1) * HD)
        q = q_ref[:, cols]
        k = k_ref[:, cols]
        v = v_ref[:, cols]
        g = grad_ref[:, cols]
        probs = _probs(q, k, length, factor)
        prob_grad = lax.dot_general(g, v, (((1,), (1,)), ((), ())), preferred_element_type=jnp.float32)
        row_dot = jnp.sum(prob_grad * probs, axis=1, keepdims=True)
        score_grad = (probs * (prob_grad - row_dot)).astype(jnp.bfloat16)
        out_ref[0, :, cols] = (
            jnp.dot(score_grad, k, preferred_element_type=jnp.float32) * factor
        ).astype(out_ref.dtype)
        out_ref[1, :, cols] = (
            lax.dot_general(score_grad, q, (((0,), (0,)), ((), ())), preferred_element_type=jnp.float32)
            * factor
        ).astype(out_ref.dtype)
        out_ref[2, :, cols] = lax.dot_general(
            probs.astype(jnp.bfloat16), g, (((0,), (0,)), ((), ())), preferred_element_type=jnp.float32
        ).astype(out_ref.dtype)
    if tokens_ref is not None:
        tokens = tokens_ref[...]
        for t in range(3):
            wgrad_ref[t] = lax.dot_general(
                tokens, out_ref[t], (((0,), (0,)), ((), ())), preferred_element_type=jnp.float32
            ).astype(wgrad_ref.dtype)


def attention_forward(queries, keys, values, lengths, factor, pair=2):
    rows, width = queries.shape
    block = pl.BlockSpec((LEN, pair * HD), lambda p, i, n: (p, i))
    return pl.pallas_call(
        functools.partial(_fwd_kernel, heads=pair, factor=factor),
        out_shape=jax.ShapeDtypeStruct((rows, width), jnp.bfloat16),
        grid_spec=pltpu.PrefetchScalarGridSpec(
            num_scalar_prefetch=1,
            grid=(rows // LEN, width // (pair * HD)),
            in_specs=[block] * 3,
            out_specs=block,
        ),
        cost_estimate=pl.CostEstimate(
            flops=4 * rows * LEN * width,
            transcendentals=rows * LEN * width // HD,
            bytes_accessed=4 * rows * width * 2,
        ),
    )(lengths, queries, keys, values)


def attention_backward(queries, keys, values, context_grad, lengths, factor, tokens=None, pair=2):
    rows, width = queries.shape
    block = pl.BlockSpec((LEN, pair * HD), lambda p, i, n: (p, i))
    grad_spec = pl.BlockSpec((3, LEN, pair * HD), lambda p, i, n: (0, p, i))
    grad_shape = jax.ShapeDtypeStruct((3, rows, width), jnp.bfloat16)
    operands = [lengths, queries, keys, values, context_grad]
    in_specs = [block] * 4
    out_specs, out_shape = grad_spec, grad_shape
    if tokens is not None:
        depth = tokens.shape[1]
        operands.append(tokens)
        in_specs.append(pl.BlockSpec((LEN, depth), lambda p, i, n: (p, 0)))
        out_specs = [grad_spec, pl.BlockSpec((3, depth, pair * HD), lambda p, i, n: (0, 0, i))]
        out_shape = [grad_shape, jax.ShapeDtypeStruct((3, depth, width), jnp.bfloat16)]
    return pl.pallas_call(
        functools.partial(_bwd_kernel, heads=pair, factor=factor),
        out_shape=out_shape,
        grid_spec=pltpu.PrefetchScalarGridSpec(
            num_scalar_prefetch=1,
            grid=(rows // LEN, width // (pair * HD)),
            in_specs=in_specs,
            out_specs=out_specs,
        ),
        cost_estimate=pl.CostEstimate(
            flops=16 * rows * LEN * width,
            transcendentals=rows * LEN * width // HD,
            bytes_accessed=10 * rows * width * 2,
        ),
    )(*operands)


def dp_pow2(values, dp_size):
    steps = dp_size.bit_length() - 1
    return dp_size == 1 << steps and values.shape[0] % dp_size == 0


def dp_halve(values, dp_size, sum_dtype=None):
    steps = dp_size.bit_length() - 1
    index = lax.axis_index("dp")
    link = values.dtype
    kept = values if sum_dtype is None else values.astype(sum_dtype)
    for step in range(steps):
        bit = (index >> step) & 1
        half = kept.shape[0] // 2
        keep = lax.dynamic_slice_in_dim(kept, bit * half, half)
        give = lax.dynamic_slice_in_dim(kept, (1 - bit) * half, half).astype(link)
        got = lax.ppermute(give, "dp", [(i, i ^ (1 << step)) for i in range(dp_size)])
        kept = keep + got.astype(kept.dtype)
    return kept


def bit_reversed(count):
    steps = count.bit_length() - 1
    return [int(format(i, f"0{steps}b")[::-1], 2) if steps else 0 for i in range(count)]


def dp_double(kept, dp_size):
    steps = dp_size.bit_length() - 1
    index = lax.axis_index("dp")
    for step in reversed(range(steps)):
        bit = (index >> step) & 1
        got = lax.ppermute(kept, "dp", [(i, i ^ (1 << step)) for i in range(dp_size)])
        kept = jnp.concatenate(
            [jnp.where(bit == 0, kept, got), jnp.where(bit == 0, got, kept)]
        )
    return kept


def make_per_device(dp_size):
    def per_device(
        tokens,
        out_grad,
        lengths,
        qkv_weight,
        qkv_bias,
        out_weight,
        out_bias,
        norm1_gain,
        norm1_shift,
        up_weight,
        up_bias,
        down_weight,
        down_bias,
        norm2_gain,
        norm2_shift,
    ):
        rows, width = tokens.shape
        shard = qkv_weight.shape[2]
        groups = width // shard
        passages = rows // LEN
        factor = HD ** (-0.5)

        half_rows = -(-(2 * width + 2) // 8) * 8
        first_half = jnp.pad(
            jnp.concatenate([qkv_weight[0], qkv_weight[1], qkv_bias], axis=0),
            ((0, half_rows - 2 * width - 2), (0, 0)),
        )
        second_half = jnp.pad(
            jnp.concatenate([qkv_weight[2], out_weight.T], axis=0),
            ((0, half_rows - 2 * width), (0, 0)),
        )
        dp_index = lax.axis_index("dp")
        parity = dp_index % 2
        mine = jnp.where(parity == 0, first_half, second_half)
        mine = lax.all_gather(mine, "tensor", axis=0, tiled=False)
        other = lax.ppermute(mine, "dp", [(i, i ^ 1) for i in range(dp_size)])
        first_half = jnp.where(parity == 0, mine, other)
        second_half = jnp.where(parity == 0, other, mine)
        query_weight = first_half[:, :width]
        key_weight = first_half[:, width : 2 * width]
        query_bias = first_half[:, 2 * width]
        value_bias = first_half[:, 2 * width + 1]
        value_weight = second_half[:, :width]
        proj_blocks = second_half[:, width : 2 * width]

        tensor_index = lax.axis_index("tensor")
        own_lengths = lax.dynamic_slice_in_dim(lengths, tensor_index * passages, passages)

        own_tokens = tokens.astype(jnp.float32)
        def project(weight, bias=None):
            out = jnp.einsum("rd,gdj->rgj", tokens, weight, preferred_element_type=jnp.float32)
            out = out if bias is None else out + bias
            return out.astype(jnp.bfloat16).reshape(rows, width)

        query_low = project(query_weight, query_bias)
        key_low = project(key_weight)
        value_low = project(value_weight, value_bias)
        context_low = attention_forward(query_low, key_low, value_low, own_lengths, factor)
        attn_out = jnp.einsum(
            "rgj,gcj->rc",
            context_low.reshape(rows, groups, shard),
            proj_blocks,
            preferred_element_type=jnp.float32,
        )
        middle, norm1_back = jax.vjp(
            layer_norm, own_tokens + attn_out + out_bias, norm1_gain, norm1_shift
        )
        middle_low = middle.astype(jnp.bfloat16)
        ffn_rows = lax.all_gather(middle_low, "tensor", axis=0, tiled=True)
        pre_act = jnp.dot(ffn_rows, up_weight, preferred_element_type=jnp.float32) + up_bias
        activated, gelu_slope = gelu_and_slope(pre_act)
        hidden = activated.astype(jnp.bfloat16)
        ffn_out = lax.psum_scatter(
            jnp.dot(hidden, down_weight, preferred_element_type=jnp.float32).astype(jnp.bfloat16),
            "tensor",
            scatter_dimension=0,
            tiled=True,
        ).astype(jnp.float32)
        layer_out, norm2_back = jax.vjp(
            layer_norm, middle + ffn_out + down_bias, norm2_gain, norm2_shift
        )
        second_grad, grad_norm2_gain, grad_norm2_shift = norm2_back(out_grad.astype(jnp.float32))
        branch_grad = second_grad.astype(jnp.bfloat16)
        grad_down_bias = jnp.sum(branch_grad, axis=0, dtype=jnp.float32)
        branch_rows = lax.all_gather(branch_grad, "tensor", axis=0, tiled=True)
        hidden_grad = contract(branch_rows, down_weight, 1, 1)
        grad_down_weight = contract(hidden, branch_rows, 0, 0)
        pre_grad = (hidden_grad * gelu_slope).astype(jnp.bfloat16)
        grad_up_bias = jnp.sum(pre_grad, axis=0, dtype=jnp.float32)
        grad_up_weight = contract(ffn_rows, pre_grad, 0, 0)
        ffn_grads = (grad_up_weight, grad_down_weight)
        halved = all(dp_pow2(g, dp_size) for g in ffn_grads)
        if halved:
            ffn_grads = tuple(dp_halve(g, dp_size) for g in ffn_grads)
        else:
            ffn_grads = lax.psum(ffn_grads, "dp")
        middle_part = lax.psum_scatter(
            contract(pre_grad, up_weight, 1, 1).astype(jnp.bfloat16),
            "tensor",
            scatter_dimension=0,
            tiled=True,
        ).astype(jnp.float32)
        norm1_in, ffn_grads = lax.optimization_barrier((second_grad + middle_part, ffn_grads))
        first_grad, grad_norm1_gain, grad_norm1_shift = norm1_back(norm1_in)
        attn_grad = first_grad.astype(jnp.bfloat16)
        grad_out_bias = jnp.sum(attn_grad, axis=0, dtype=jnp.float32)
        context_grad = (
            jnp.einsum("rc,gcj->rgj", attn_grad, proj_blocks, preferred_element_type=jnp.float32)
            .astype(jnp.bfloat16)
            .reshape(rows, width)
        )
        early = contract(attn_grad, context_low, 0, 0)
        early_halved = dp_pow2(early, dp_size)
        if early_halved:
            early = dp_halve(early.astype(jnp.bfloat16), dp_size, jnp.float32)
        else:
            early = lax.psum_scatter(early, "dp", scatter_dimension=0, tiled=True)
        if passages == 1:
            proj_grad, grad_qkv_low = attention_backward(
                query_low, key_low, value_low, context_grad, own_lengths, factor, tokens
            )
        else:
            proj_grad = attention_backward(
                query_low, key_low, value_low, context_grad, own_lengths, factor
            )
            grad_qkv_low = jnp.einsum(
                "rd,kre->kde", tokens, proj_grad, preferred_element_type=jnp.float32
            ).astype(jnp.bfloat16)
        grad_bias_full = jnp.sum(proj_grad[0::2], axis=1, dtype=jnp.float32)

        def back_project(grad, weight):
            return jnp.einsum(
                "rgj,gdj->rd",
                grad.reshape(rows, groups, shard),
                weight,
                preferred_element_type=jnp.float32,
            )

        input_part = (
            back_project(proj_grad[0], query_weight)
            + back_project(proj_grad[1], key_weight)
            + back_project(proj_grad[2], value_weight)
        )
        input_grad = (first_grad + input_part).astype(jnp.bfloat16)

        small = jnp.stack(
            [
                grad_out_bias,
                grad_norm1_gain,
                grad_norm1_shift,
                grad_down_bias,
                grad_norm2_gain,
                grad_norm2_shift,
            ]
        )
        n_small = small.shape[0]
        small_rep = jnp.tile(small.reshape(n_small, groups, shard), (1, 1, groups)).reshape(
            n_small * groups, width
        )
        up_parts = grad_up_bias.shape[0] // shard
        own_group = (jnp.arange(width) // shard == tensor_index)[None, :]
        up_rep = jnp.where(
            own_group, jnp.tile(grad_up_bias.reshape(up_parts, shard), (1, groups)), 0.0
        )
        tail = jnp.concatenate([grad_bias_full, small_rep, up_rep], axis=0)
        tail_rows = tail.shape[0]
        tail = jnp.pad(tail, ((0, -(-tail_rows // 8) * 8 - tail_rows), (0, 0)))
        late = lax.psum_scatter(
            grad_qkv_low.reshape(3 * width, width),
            "dp",
            scatter_dimension=0,
            tiled=True,
        ).astype(jnp.float32)
        joined = jnp.concatenate([late, early, tail], axis=0)
        joined = lax.psum_scatter(
            joined.reshape(joined.shape[0], groups, shard).transpose(1, 0, 2),
            "tensor",
            scatter_dimension=0,
            tiled=True,
        )[0]
        if halved:
            ffn_grads = tuple(
                dp_double(g.astype(jnp.bfloat16), dp_size).astype(jnp.float32) for g in ffn_grads
            )
            joined, ffn_grads = lax.optimization_barrier((joined, ffn_grads))
        grad_up_weight, grad_down_weight = ffn_grads
        late_rows = late.shape[0]
        early_rows = early.shape[0]
        joined = lax.all_gather(joined, "dp", axis=0, tiled=False)
        early = joined[:, late_rows : late_rows + early_rows]
        if early_halved:
            order = bit_reversed(dp_size)
            place = [order.index(b) for b in range(dp_size)]
            early = jnp.concatenate([early[p] for p in place], axis=0)
        pieces = [
            joined[:, :late_rows].reshape(-1, shard),
            early.reshape(-1, shard),
            jnp.sum(joined[:, late_rows + early_rows :], axis=0),
        ]
        grad_qkv_weight = pieces[0].reshape(3, width, shard)
        grad_out_weight = pieces[1].T
        tail = pieces[2]
        grad_qkv_bias = tail[:2]
        small_sum = tail[2 : 2 + n_small * groups].reshape(n_small, width)
        grad_up_bias = tail[2 + n_small * groups : 2 + n_small * groups + up_parts].reshape(-1)
        (
            grad_out_bias,
            grad_norm1_gain,
            grad_norm1_shift,
            grad_down_bias,
            grad_norm2_gain,
            grad_norm2_shift,
        ) = [small_sum[i] for i in range(n_small)]
        return (
            layer_out.astype(jnp.bfloat16),
            input_grad,
            grad_qkv_weight,
            grad_qkv_bias,
            grad_out_weight,
            grad_out_bias,
            grad_norm1_gain,
            grad_norm1_shift,
            grad_up_weight,
            grad_up_bias,
            grad_down_weight,
            grad_down_bias,
            grad_norm2_gain,
            grad_norm2_shift,
        )

    return per_device


def solution(mesh):
    placed = (
        P(("dp", "tensor"), None),
        P(("dp", "tensor"), None),
        P("dp"),
        P(None, None, "tensor"),
        P(None, "tensor"),
        P("tensor", None),
        P(),
        P(),
        P(),
        P(None, "tensor"),
        P("tensor"),
        P("tensor", None),
        P(),
        P(),
        P(),
    )
    return jax.shard_map(
        make_per_device(mesh.shape["dp"]),
        mesh=mesh,
        in_specs=placed,
        out_specs=(
            P(("dp", "tensor"), None),
            P(("dp", "tensor"), None),
            P(None, None, "tensor"),
            P(None, "tensor"),
            P("tensor", None),
            P(),
            P(),
            P(),
            P(None, "tensor"),
            P("tensor"),
            P("tensor", None),
            P(),
            P(),
            P(),
        ),
        check_vma=False,
    )
```

```python
import functools

import jax
import jax.numpy as jnp
from jax import lax
from jax.experimental import pallas as pl
from jax.experimental.pallas import tpu as pltpu
from jax.sharding import PartitionSpec as P

HD = 64
LEN = 512


EPS = 1e-12
NEG = -1e30


def layer_norm(values, gain_vec, shift_vec):
    center = values - jnp.mean(values, axis=-1, keepdims=True)
    spread = jnp.mean(center * center, axis=-1, keepdims=True)
    return center * lax.rsqrt(spread + EPS) * gain_vec + shift_vec


def gelu_and_slope(values):
    cdf = 0.5 * (1.0 + lax.erf(values * (2.0 ** -0.5)))
    density = jnp.exp(-0.5 * values * values) * ((2.0 * jnp.pi) ** -0.5)
    return values * cdf, cdf + values * density


def contract(left, right, left_dim, right_dim):
    return lax.dot_general(
        left, right, (((left_dim,), (right_dim,)), ((), ())), preferred_element_type=jnp.float32
    )


def _probs(q, k, length, factor):
    scores = lax.dot_general(q, k, (((1,), (1,)), ((), ())), preferred_element_type=jnp.float32) * factor
    col = lax.broadcasted_iota(jnp.int32, scores.shape, 1)
    scores = jnp.where(col < length, scores, NEG)
    top = jnp.max(scores, axis=1, keepdims=True)
    raised = jnp.exp(scores - top)
    return raised / jnp.sum(raised, axis=1, keepdims=True)


def _fwd_kernel(len_ref, q_ref, k_ref, v_ref, out_ref, *, heads, factor):
    length = len_ref[pl.program_id(0)]
    for h in range(heads):
        cols = slice(h * HD, (h + 1) * HD)
        probs = _probs(q_ref[:, cols], k_ref[:, cols], length, factor)
        out_ref[:, cols] = jnp.dot(
            probs.astype(jnp.bfloat16), v_ref[:, cols], preferred_element_type=jnp.float32
        ).astype(out_ref.dtype)


def _bwd_kernel(len_ref, q_ref, k_ref, v_ref, grad_ref, *rest, heads, factor):
    if len(rest) == 3:
        tokens_ref, out_ref, wgrad_ref = rest
    else:
        (out_ref,), tokens_ref = rest, None
    length = len_ref[pl.program_id(0)]
    for h in range(heads):
        cols = slice(h * HD, (h + 1) * HD)
        q = q_ref[:, cols]
        k = k_ref[:, cols]
        v = v_ref[:, cols]
        g = grad_ref[:, cols]
        probs = _probs(q, k, length, factor)
        prob_grad = lax.dot_general(g, v, (((1,), (1,)), ((), ())), preferred_element_type=jnp.float32)
        row_dot = jnp.sum(prob_grad * probs, axis=1, keepdims=True)
        score_grad = (probs * (prob_grad - row_dot)).astype(jnp.bfloat16)
        out_ref[0, :, cols] = (
            jnp.dot(score_grad, k, preferred_element_type=jnp.float32) * factor
        ).astype(out_ref.dtype)
        out_ref[1, :, cols] = (
            lax.dot_general(score_grad, q, (((0,), (0,)), ((), ())), preferred_element_type=jnp.float32)
            * factor
        ).astype(out_ref.dtype)
        out_ref[2, :, cols] = lax.dot_general(
            probs.astype(jnp.bfloat16), g, (((0,), (0,)), ((), ())), preferred_element_type=jnp.float32
        ).astype(out_ref.dtype)
    if tokens_ref is not None:
        tokens = tokens_ref[...]
        for t in range(3):
            wgrad_ref[t] = lax.dot_general(
                tokens, out_ref[t], (((0,), (0,)), ((), ())), preferred_element_type=jnp.float32
            ).astype(wgrad_ref.dtype)


def attention_forward(queries, keys, values, lengths, factor, pair=2):
    rows, width = queries.shape
    block = pl.BlockSpec((LEN, pair * HD), lambda p, i, n: (p, i))
    return pl.pallas_call(
        functools.partial(_fwd_kernel, heads=pair, factor=factor),
        out_shape=jax.ShapeDtypeStruct((rows, width), jnp.bfloat16),
        grid_spec=pltpu.PrefetchScalarGridSpec(
            num_scalar_prefetch=1,
            grid=(rows // LEN, width // (pair * HD)),
            in_specs=[block] * 3,
            out_specs=block,
        ),
        cost_estimate=pl.CostEstimate(
            flops=4 * rows * LEN * width,
            transcendentals=rows * LEN * width // HD,
            bytes_accessed=4 * rows * width * 2,
        ),
    )(lengths, queries, keys, values)


def attention_backward(queries, keys, values, context_grad, lengths, factor, tokens=None, pair=2):
    rows, width = queries.shape
    block = pl.BlockSpec((LEN, pair * HD), lambda p, i, n: (p, i))
    grad_spec = pl.BlockSpec((3, LEN, pair * HD), lambda p, i, n: (0, p, i))
    grad_shape = jax.ShapeDtypeStruct((3, rows, width), jnp.bfloat16)
    operands = [lengths, queries, keys, values, context_grad]
    in_specs = [block] * 4
    out_specs, out_shape = grad_spec, grad_shape
    if tokens is not None:
        depth = tokens.shape[1]
        operands.append(tokens)
        in_specs.append(pl.BlockSpec((LEN, depth), lambda p, i, n: (p, 0)))
        out_specs = [grad_spec, pl.BlockSpec((3, depth, pair * HD), lambda p, i, n: (0, 0, i))]
        out_shape = [grad_shape, jax.ShapeDtypeStruct((3, depth, width), jnp.bfloat16)]
    return pl.pallas_call(
        functools.partial(_bwd_kernel, heads=pair, factor=factor),
        out_shape=out_shape,
        grid_spec=pltpu.PrefetchScalarGridSpec(
            num_scalar_prefetch=1,
            grid=(rows // LEN, width // (pair * HD)),
            in_specs=in_specs,
            out_specs=out_specs,
        ),
        cost_estimate=pl.CostEstimate(
            flops=16 * rows * LEN * width,
            transcendentals=rows * LEN * width // HD,
            bytes_accessed=10 * rows * width * 2,
        ),
    )(*operands)


def _tn_kernel(left_ref, right_ref, out_ref):
    out_ref[...] = lax.dot_general(
        left_ref[...], right_ref[...], (((0,), (0,)), ((), ())), preferred_element_type=jnp.float32
    )


def tn_matmul(left, right, tile=256):
    depth, rows = left.shape
    cols = right.shape[1]
    return pl.pallas_call(
        _tn_kernel,
        out_shape=jax.ShapeDtypeStruct((rows, cols), jnp.float32),
        grid=(rows // tile, cols // tile),
        in_specs=[
            pl.BlockSpec((depth, tile), lambda i, j: (0, i)),
            pl.BlockSpec((depth, tile), lambda i, j: (0, j)),
        ],
        out_specs=pl.BlockSpec((tile, tile), lambda i, j: (i, j)),
        cost_estimate=pl.CostEstimate(
            flops=2 * depth * rows * cols,
            transcendentals=0,
            bytes_accessed=2 * depth * (rows + cols) + 4 * rows * cols,
        ),
    )(left, right)


def dp_pow2(values, dp_size):
    steps = dp_size.bit_length() - 1
    return dp_size == 1 << steps and values.shape[0] % dp_size == 0


def dp_halve(values, dp_size, sum_dtype=None):
    steps = dp_size.bit_length() - 1
    index = lax.axis_index("dp")
    link = values.dtype
    kept = values if sum_dtype is None else values.astype(sum_dtype)
    for step in range(steps):
        bit = (index >> step) & 1
        half = kept.shape[0] // 2
        keep = lax.dynamic_slice_in_dim(kept, bit * half, half)
        give = lax.dynamic_slice_in_dim(kept, (1 - bit) * half, half).astype(link)
        got = lax.ppermute(give, "dp", [(i, i ^ (1 << step)) for i in range(dp_size)])
        kept = keep + got.astype(kept.dtype)
    return kept


def bit_reversed(count):
    steps = count.bit_length() - 1
    return [int(format(i, f"0{steps}b")[::-1], 2) if steps else 0 for i in range(count)]


def dp_double(kept, dp_size):
    steps = dp_size.bit_length() - 1
    index = lax.axis_index("dp")
    for step in reversed(range(steps)):
        bit = (index >> step) & 1
        got = lax.ppermute(kept, "dp", [(i, i ^ (1 << step)) for i in range(dp_size)])
        kept = jnp.concatenate(
            [jnp.where(bit == 0, kept, got), jnp.where(bit == 0, got, kept)]
        )
    return kept


def make_per_device(dp_size):
    def per_device(
        tokens,
        out_grad,
        lengths,
        qkv_weight,
        qkv_bias,
        out_weight,
        out_bias,
        norm1_gain,
        norm1_shift,
        up_weight,
        up_bias,
        down_weight,
        down_bias,
        norm2_gain,
        norm2_shift,
    ):
        rows, width = tokens.shape
        shard = qkv_weight.shape[2]
        groups = width // shard
        passages = rows // LEN
        factor = HD ** (-0.5)

        half_rows = -(-(2 * width + 2) // 8) * 8
        first_half = jnp.pad(
            jnp.concatenate([qkv_weight[0], qkv_weight[1], qkv_bias], axis=0),
            ((0, half_rows - 2 * width - 2), (0, 0)),
        )
        second_half = jnp.pad(
            jnp.concatenate([qkv_weight[2], out_weight.T], axis=0),
            ((0, half_rows - 2 * width), (0, 0)),
        )
        dp_index = lax.axis_index("dp")
        parity = dp_index % 2
        mine = jnp.where(parity == 0, first_half, second_half)
        mine = lax.all_gather(mine, "tensor", axis=0, tiled=False)
        other = lax.ppermute(mine, "dp", [(i, i ^ 1) for i in range(dp_size)])
        first_half = jnp.where(parity == 0, mine, other)
        second_half = jnp.where(parity == 0, other, mine)
        query_weight = first_half[:, :width]
        key_weight = first_half[:, width : 2 * width]
        query_bias = first_half[:, 2 * width]
        value_bias = first_half[:, 2 * width + 1]
        value_weight = second_half[:, :width]
        proj_blocks = second_half[:, width : 2 * width]

        tensor_index = lax.axis_index("tensor")
        own_lengths = lax.dynamic_slice_in_dim(lengths, tensor_index * passages, passages)

        own_tokens = tokens.astype(jnp.float32)
        def project(weight, bias=None):
            out = jnp.einsum("rd,gdj->rgj", tokens, weight, preferred_element_type=jnp.float32)
            out = out if bias is None else out + bias
            return out.astype(jnp.bfloat16).reshape(rows, width)

        query_low = project(query_weight, query_bias)
        key_low = project(key_weight)
        value_low = project(value_weight, value_bias)
        context_low = attention_forward(query_low, key_low, value_low, own_lengths, factor)
        attn_out = jnp.einsum(
            "rgj,gcj->rc",
            context_low.reshape(rows, groups, shard),
            proj_blocks,
            preferred_element_type=jnp.float32,
        )
        middle, norm1_back = jax.vjp(
            layer_norm, own_tokens + attn_out + out_bias, norm1_gain, norm1_shift
        )
        middle_low = middle.astype(jnp.bfloat16)
        ffn_rows = lax.all_gather(middle_low, "tensor", axis=0, tiled=True)
        pre_act = jnp.dot(ffn_rows, up_weight, preferred_element_type=jnp.float32) + up_bias
        activated, gelu_slope = gelu_and_slope(pre_act)
        hidden = activated.astype(jnp.bfloat16)
        ffn_out = lax.psum_scatter(
            jnp.dot(hidden, down_weight, preferred_element_type=jnp.float32).astype(jnp.bfloat16),
            "tensor",
            scatter_dimension=0,
            tiled=True,
        ).astype(jnp.float32)
        layer_out, norm2_back = jax.vjp(
            layer_norm, middle + ffn_out + down_bias, norm2_gain, norm2_shift
        )
        second_grad, grad_norm2_gain, grad_norm2_shift = norm2_back(out_grad.astype(jnp.float32))
        branch_grad = second_grad.astype(jnp.bfloat16)
        grad_down_bias = jnp.sum(branch_grad, axis=0, dtype=jnp.float32)
        branch_rows = lax.all_gather(branch_grad, "tensor", axis=0, tiled=True)
        hidden_grad = contract(branch_rows, down_weight, 1, 1)
        grad_down_weight = tn_matmul(hidden, branch_rows)
        pre_grad = (hidden_grad * gelu_slope).astype(jnp.bfloat16)
        grad_up_bias = jnp.sum(pre_grad, axis=0, dtype=jnp.float32)
        grad_up_weight = tn_matmul(ffn_rows, pre_grad)
        ffn_grads = (grad_up_weight, grad_down_weight)
        halved = all(dp_pow2(g, dp_size) for g in ffn_grads)
        if halved:
            ffn_grads = tuple(dp_halve(g, dp_size) for g in ffn_grads)
        else:
            ffn_grads = lax.psum(ffn_grads, "dp")
        middle_part = lax.psum_scatter(
            contract(pre_grad, up_weight, 1, 1).astype(jnp.bfloat16),
            "tensor",
            scatter_dimension=0,
            tiled=True,
        ).astype(jnp.float32)
        norm1_in, ffn_grads = lax.optimization_barrier((second_grad + middle_part, ffn_grads))
        first_grad, grad_norm1_gain, grad_norm1_shift = norm1_back(norm1_in)
        attn_grad = first_grad.astype(jnp.bfloat16)
        grad_out_bias = jnp.sum(attn_grad, axis=0, dtype=jnp.float32)
        context_grad = (
            jnp.einsum("rc,gcj->rgj", attn_grad, proj_blocks, preferred_element_type=jnp.float32)
            .astype(jnp.bfloat16)
            .reshape(rows, width)
        )
        early = contract(attn_grad, context_low, 0, 0)
        early_halved = dp_pow2(early, dp_size)
        if early_halved:
            early = dp_halve(early.astype(jnp.bfloat16), dp_size, jnp.float32)
        else:
            early = lax.psum_scatter(early, "dp", scatter_dimension=0, tiled=True)
        if passages == 1:
            proj_grad, grad_qkv_low = attention_backward(
                query_low, key_low, value_low, context_grad, own_lengths, factor, tokens
            )
        else:
            proj_grad = attention_backward(
                query_low, key_low, value_low, context_grad, own_lengths, factor
            )
            grad_qkv_low = jnp.einsum(
                "rd,kre->kde", tokens, proj_grad, preferred_element_type=jnp.float32
            ).astype(jnp.bfloat16)
        grad_bias_full = jnp.sum(proj_grad[0::2], axis=1, dtype=jnp.float32)

        def back_project(grad, weight):
            return jnp.einsum(
                "rgj,gdj->rd",
                grad.reshape(rows, groups, shard),
                weight,
                preferred_element_type=jnp.float32,
            )

        input_part = (
            back_project(proj_grad[0], query_weight)
            + back_project(proj_grad[1], key_weight)
            + back_project(proj_grad[2], value_weight)
        )
        input_grad = (first_grad + input_part).astype(jnp.bfloat16)

        small = jnp.stack(
            [
                grad_out_bias,
                grad_norm1_gain,
                grad_norm1_shift,
                grad_down_bias,
                grad_norm2_gain,
                grad_norm2_shift,
            ]
        )
        n_small = small.shape[0]
        small_rep = jnp.tile(small.reshape(n_small, groups, shard), (1, 1, groups)).reshape(
            n_small * groups, width
        )
        up_parts = grad_up_bias.shape[0] // shard
        own_group = (jnp.arange(width) // shard == tensor_index)[None, :]
        up_rep = jnp.where(
            own_group, jnp.tile(grad_up_bias.reshape(up_parts, shard), (1, groups)), 0.0
        )
        tail = jnp.concatenate([grad_bias_full, small_rep, up_rep], axis=0)
        tail_rows = tail.shape[0]
        tail = jnp.pad(tail, ((0, -(-tail_rows // 8) * 8 - tail_rows), (0, 0)))
        late = lax.psum_scatter(
            grad_qkv_low.reshape(3 * width, width),
            "dp",
            scatter_dimension=0,
            tiled=True,
        ).astype(jnp.float32)
        joined = jnp.concatenate([late, early, tail], axis=0)
        joined = lax.psum_scatter(
            joined.reshape(joined.shape[0], groups, shard).transpose(1, 0, 2),
            "tensor",
            scatter_dimension=0,
            tiled=True,
        )[0]
        if halved:
            ffn_grads = tuple(
                dp_double(g.astype(jnp.bfloat16), dp_size).astype(jnp.float32) for g in ffn_grads
            )
            joined, ffn_grads = lax.optimization_barrier((joined, ffn_grads))
        grad_up_weight, grad_down_weight = ffn_grads
        late_rows = late.shape[0]
        early_rows = early.shape[0]
        joined = lax.all_gather(joined, "dp", axis=0, tiled=False)
        early = joined[:, late_rows : late_rows + early_rows]
        if early_halved:
            order = bit_reversed(dp_size)
            place = [order.index(b) for b in range(dp_size)]
            early = jnp.concatenate([early[p] for p in place], axis=0)
        pieces = [
            joined[:, :late_rows].reshape(-1, shard),
            early.reshape(-1, shard),
            jnp.sum(joined[:, late_rows + early_rows :], axis=0),
        ]
        grad_qkv_weight = pieces[0].reshape(3, width, shard)
        grad_out_weight = pieces[1].T
        tail = pieces[2]
        grad_qkv_bias = tail[:2]
        small_sum = tail[2 : 2 + n_small * groups].reshape(n_small, width)
        grad_up_bias = tail[2 + n_small * groups : 2 + n_small * groups + up_parts].reshape(-1)
        (
            grad_out_bias,
            grad_norm1_gain,
            grad_norm1_shift,
            grad_down_bias,
            grad_norm2_gain,
            grad_norm2_shift,
        ) = [small_sum[i] for i in range(n_small)]
        return (
            layer_out.astype(jnp.bfloat16),
            input_grad,
            grad_qkv_weight,
            grad_qkv_bias,
            grad_out_weight,
            grad_out_bias,
            grad_norm1_gain,
            grad_norm1_shift,
            grad_up_weight,
            grad_up_bias,
            grad_down_weight,
            grad_down_bias,
            grad_norm2_gain,
            grad_norm2_shift,
        )

    return per_device


def solution(mesh):
    placed = (
        P(("dp", "tensor"), None),
        P(("dp", "tensor"), None),
        P("dp"),
        P(None, None, "tensor"),
        P(None, "tensor"),
        P("tensor", None),
        P(),
        P(),
        P(),
        P(None, "tensor"),
        P("tensor"),
        P("tensor", None),
        P(),
        P(),
        P(),
    )
    return jax.shard_map(
        make_per_device(mesh.shape["dp"]),
        mesh=mesh,
        in_specs=placed,
        out_specs=(
            P(("dp", "tensor"), None),
            P(("dp", "tensor"), None),
            P(None, None, "tensor"),
            P(None, "tensor"),
            P("tensor", None),
            P(),
            P(),
            P(),
            P(None, "tensor"),
            P("tensor"),
            P("tensor", None),
            P(),
            P(),
            P(),
        ),
        check_vma=False,
    )
```

```python
import functools

import jax
import jax.numpy as jnp
from jax import lax
from jax.experimental import pallas as pl
from jax.experimental.pallas import tpu as pltpu
from jax.sharding import PartitionSpec as P

HD = 64
LEN = 512


EPS = 1e-12
NEG = -1e30


def layer_norm(values, gain_vec, shift_vec):
    center = values - jnp.mean(values, axis=-1, keepdims=True)
    spread = jnp.mean(center * center, axis=-1, keepdims=True)
    return center * lax.rsqrt(spread + EPS) * gain_vec + shift_vec


def gelu_and_slope(values):
    cdf = 0.5 * (1.0 + lax.erf(values * (2.0 ** -0.5)))
    density = jnp.exp(-0.5 * values * values) * ((2.0 * jnp.pi) ** -0.5)
    return values * cdf, cdf + values * density


def contract(left, right, left_dim, right_dim):
    return lax.dot_general(
        left, right, (((left_dim,), (right_dim,)), ((), ())), preferred_element_type=jnp.float32
    )


def _probs(q, k, length, factor):
    scores = lax.dot_general(q, k, (((1,), (1,)), ((), ())), preferred_element_type=jnp.float32) * factor
    col = lax.broadcasted_iota(jnp.int32, scores.shape, 1)
    scores = jnp.where(col < length, scores, NEG)
    top = jnp.max(scores, axis=1, keepdims=True)
    raised = jnp.exp(scores - top)
    return raised / jnp.sum(raised, axis=1, keepdims=True)


def _fwd_kernel(len_ref, q_ref, k_ref, v_ref, out_ref, *, heads, factor):
    length = len_ref[pl.program_id(0)]
    for h in range(heads):
        cols = slice(h * HD, (h + 1) * HD)
        probs = _probs(q_ref[:, cols], k_ref[:, cols], length, factor)
        out_ref[:, cols] = jnp.dot(
            probs.astype(jnp.bfloat16), v_ref[:, cols], preferred_element_type=jnp.float32
        ).astype(out_ref.dtype)


def _bwd_kernel(len_ref, q_ref, k_ref, v_ref, grad_ref, *rest, heads, factor):
    if len(rest) == 3:
        tokens_ref, out_ref, wgrad_ref = rest
    else:
        (out_ref,), tokens_ref = rest, None
    length = len_ref[pl.program_id(0)]
    for h in range(heads):
        cols = slice(h * HD, (h + 1) * HD)
        q = q_ref[:, cols]
        k = k_ref[:, cols]
        v = v_ref[:, cols]
        g = grad_ref[:, cols]
        probs = _probs(q, k, length, factor)
        prob_grad = lax.dot_general(g, v, (((1,), (1,)), ((), ())), preferred_element_type=jnp.float32)
        row_dot = jnp.sum(prob_grad * probs, axis=1, keepdims=True)
        score_grad = (probs * (prob_grad - row_dot)).astype(jnp.bfloat16)
        out_ref[0, :, cols] = (
            jnp.dot(score_grad, k, preferred_element_type=jnp.float32) * factor
        ).astype(out_ref.dtype)
        out_ref[1, :, cols] = (
            lax.dot_general(score_grad, q, (((0,), (0,)), ((), ())), preferred_element_type=jnp.float32)
            * factor
        ).astype(out_ref.dtype)
        out_ref[2, :, cols] = lax.dot_general(
            probs.astype(jnp.bfloat16), g, (((0,), (0,)), ((), ())), preferred_element_type=jnp.float32
        ).astype(out_ref.dtype)
    if tokens_ref is not None:
        tokens = tokens_ref[...]
        for t in range(3):
            wgrad_ref[t] = lax.dot_general(
                tokens, out_ref[t], (((0,), (0,)), ((), ())), preferred_element_type=jnp.float32
            ).astype(wgrad_ref.dtype)


def attention_forward(queries, keys, values, lengths, factor, pair=2):
    rows, width = queries.shape
    block = pl.BlockSpec((LEN, pair * HD), lambda p, i, n: (p, i))
    return pl.pallas_call(
        functools.partial(_fwd_kernel, heads=pair, factor=factor),
        out_shape=jax.ShapeDtypeStruct((rows, width), jnp.bfloat16),
        grid_spec=pltpu.PrefetchScalarGridSpec(
            num_scalar_prefetch=1,
            grid=(rows // LEN, width // (pair * HD)),
            in_specs=[block] * 3,
            out_specs=block,
        ),
        cost_estimate=pl.CostEstimate(
            flops=4 * rows * LEN * width,
            transcendentals=rows * LEN * width // HD,
            bytes_accessed=4 * rows * width * 2,
        ),
    )(lengths, queries, keys, values)


def attention_backward(queries, keys, values, context_grad, lengths, factor, tokens=None, pair=2):
    rows, width = queries.shape
    block = pl.BlockSpec((LEN, pair * HD), lambda p, i, n: (p, i))
    grad_spec = pl.BlockSpec((3, LEN, pair * HD), lambda p, i, n: (0, p, i))
    grad_shape = jax.ShapeDtypeStruct((3, rows, width), jnp.bfloat16)
    operands = [lengths, queries, keys, values, context_grad]
    in_specs = [block] * 4
    out_specs, out_shape = grad_spec, grad_shape
    if tokens is not None:
        depth = tokens.shape[1]
        operands.append(tokens)
        in_specs.append(pl.BlockSpec((LEN, depth), lambda p, i, n: (p, 0)))
        out_specs = [grad_spec, pl.BlockSpec((3, depth, pair * HD), lambda p, i, n: (0, 0, i))]
        out_shape = [grad_shape, jax.ShapeDtypeStruct((3, depth, width), jnp.bfloat16)]
    return pl.pallas_call(
        functools.partial(_bwd_kernel, heads=pair, factor=factor),
        out_shape=out_shape,
        grid_spec=pltpu.PrefetchScalarGridSpec(
            num_scalar_prefetch=1,
            grid=(rows // LEN, width // (pair * HD)),
            in_specs=in_specs,
            out_specs=out_specs,
        ),
        cost_estimate=pl.CostEstimate(
            flops=16 * rows * LEN * width,
            transcendentals=rows * LEN * width // HD,
            bytes_accessed=10 * rows * width * 2,
        ),
    )(*operands)


def _tn_kernel(left_ref, right_ref, out_ref):
    out_ref[...] = lax.dot_general(
        left_ref[...], right_ref[...], (((0,), (0,)), ((), ())), preferred_element_type=jnp.float32
    )


def tn_matmul(left, right, tile=256):
    depth, rows = left.shape
    cols = right.shape[1]
    return pl.pallas_call(
        _tn_kernel,
        out_shape=jax.ShapeDtypeStruct((rows, cols), jnp.float32),
        grid=(rows // tile,),
        in_specs=[
            pl.BlockSpec((depth, tile), lambda i: (0, i)),
            pl.BlockSpec((depth, cols), lambda i: (0, 0)),
        ],
        out_specs=pl.BlockSpec((tile, cols), lambda i: (i, 0)),
        cost_estimate=pl.CostEstimate(
            flops=2 * depth * rows * cols,
            transcendentals=0,
            bytes_accessed=2 * depth * (rows + cols) + 4 * rows * cols,
        ),
    )(left, right)


def dp_pow2(values, dp_size):
    steps = dp_size.bit_length() - 1
    return dp_size == 1 << steps and values.shape[0] % dp_size == 0


def dp_halve(values, dp_size, sum_dtype=None):
    steps = dp_size.bit_length() - 1
    index = lax.axis_index("dp")
    link = values.dtype
    kept = values if sum_dtype is None else values.astype(sum_dtype)
    for step in range(steps):
        bit = (index >> step) & 1
        half = kept.shape[0] // 2
        keep = lax.dynamic_slice_in_dim(kept, bit * half, half)
        give = lax.dynamic_slice_in_dim(kept, (1 - bit) * half, half).astype(link)
        got = lax.ppermute(give, "dp", [(i, i ^ (1 << step)) for i in range(dp_size)])
        kept = keep + got.astype(kept.dtype)
    return kept


def bit_reversed(count):
    steps = count.bit_length() - 1
    return [int(format(i, f"0{steps}b")[::-1], 2) if steps else 0 for i in range(count)]


def dp_double(kept, dp_size):
    steps = dp_size.bit_length() - 1
    index = lax.axis_index("dp")
    for step in reversed(range(steps)):
        bit = (index >> step) & 1
        got = lax.ppermute(kept, "dp", [(i, i ^ (1 << step)) for i in range(dp_size)])
        kept = jnp.concatenate(
            [jnp.where(bit == 0, kept, got), jnp.where(bit == 0, got, kept)]
        )
    return kept


def make_per_device(dp_size):
    def per_device(
        tokens,
        out_grad,
        lengths,
        qkv_weight,
        qkv_bias,
        out_weight,
        out_bias,
        norm1_gain,
        norm1_shift,
        up_weight,
        up_bias,
        down_weight,
        down_bias,
        norm2_gain,
        norm2_shift,
    ):
        rows, width = tokens.shape
        shard = qkv_weight.shape[2]
        groups = width // shard
        passages = rows // LEN
        factor = HD ** (-0.5)

        half_rows = -(-(2 * width + 2) // 8) * 8
        first_half = jnp.pad(
            jnp.concatenate([qkv_weight[0], qkv_weight[1], qkv_bias], axis=0),
            ((0, half_rows - 2 * width - 2), (0, 0)),
        )
        second_half = jnp.pad(
            jnp.concatenate([qkv_weight[2], out_weight.T], axis=0),
            ((0, half_rows - 2 * width), (0, 0)),
        )
        dp_index = lax.axis_index("dp")
        parity = dp_index % 2
        mine = jnp.where(parity == 0, first_half, second_half)
        mine = lax.all_gather(mine, "tensor", axis=0, tiled=False)
        other = lax.ppermute(mine, "dp", [(i, i ^ 1) for i in range(dp_size)])
        first_half = jnp.where(parity == 0, mine, other)
        second_half = jnp.where(parity == 0, other, mine)
        query_weight = first_half[:, :width]
        key_weight = first_half[:, width : 2 * width]
        query_bias = first_half[:, 2 * width]
        value_bias = first_half[:, 2 * width + 1]
        value_weight = second_half[:, :width]
        proj_blocks = second_half[:, width : 2 * width]

        tensor_index = lax.axis_index("tensor")
        own_lengths = lax.dynamic_slice_in_dim(lengths, tensor_index * passages, passages)

        own_tokens = tokens.astype(jnp.float32)
        def project(weight, bias=None):
            out = jnp.einsum("rd,gdj->rgj", tokens, weight, preferred_element_type=jnp.float32)
            out = out if bias is None else out + bias
            return out.astype(jnp.bfloat16).reshape(rows, width)

        query_low = project(query_weight, query_bias)
        key_low = project(key_weight)
        value_low = project(value_weight, value_bias)
        context_low = attention_forward(query_low, key_low, value_low, own_lengths, factor)
        attn_out = jnp.einsum(
            "rgj,gcj->rc",
            context_low.reshape(rows, groups, shard),
            proj_blocks,
            preferred_element_type=jnp.float32,
        )
        middle, norm1_back = jax.vjp(
            layer_norm, own_tokens + attn_out + out_bias, norm1_gain, norm1_shift
        )
        middle_low = middle.astype(jnp.bfloat16)
        ffn_rows = lax.all_gather(middle_low, "tensor", axis=0, tiled=True)
        pre_act = jnp.dot(ffn_rows, up_weight, preferred_element_type=jnp.float32) + up_bias
        activated, gelu_slope = gelu_and_slope(pre_act)
        hidden = activated.astype(jnp.bfloat16)
        ffn_out = lax.psum_scatter(
            jnp.dot(hidden, down_weight, preferred_element_type=jnp.float32).astype(jnp.bfloat16),
            "tensor",
            scatter_dimension=0,
            tiled=True,
        ).astype(jnp.float32)
        layer_out, norm2_back = jax.vjp(
            layer_norm, middle + ffn_out + down_bias, norm2_gain, norm2_shift
        )
        second_grad, grad_norm2_gain, grad_norm2_shift = norm2_back(out_grad.astype(jnp.float32))
        branch_grad = second_grad.astype(jnp.bfloat16)
        grad_down_bias = jnp.sum(branch_grad, axis=0, dtype=jnp.float32)
        branch_rows = lax.all_gather(branch_grad, "tensor", axis=0, tiled=True)
        hidden_grad = contract(branch_rows, down_weight, 1, 1)
        grad_down_weight = tn_matmul(hidden, branch_rows)
        pre_grad = (hidden_grad * gelu_slope).astype(jnp.bfloat16)
        grad_up_bias = jnp.sum(pre_grad, axis=0, dtype=jnp.float32)
        grad_up_weight = tn_matmul(ffn_rows, pre_grad)
        ffn_grads = (grad_up_weight, grad_down_weight)
        halved = all(dp_pow2(g, dp_size) for g in ffn_grads)
        if halved:
            ffn_grads = tuple(dp_halve(g, dp_size) for g in ffn_grads)
        else:
            ffn_grads = lax.psum(ffn_grads, "dp")
        middle_part = lax.psum_scatter(
            contract(pre_grad, up_weight, 1, 1).astype(jnp.bfloat16),
            "tensor",
            scatter_dimension=0,
            tiled=True,
        ).astype(jnp.float32)
        first_grad, grad_norm1_gain, grad_norm1_shift = norm1_back(second_grad + middle_part)
        attn_grad = first_grad.astype(jnp.bfloat16)
        grad_out_bias = jnp.sum(attn_grad, axis=0, dtype=jnp.float32)
        context_grad = (
            jnp.einsum("rc,gcj->rgj", attn_grad, proj_blocks, preferred_element_type=jnp.float32)
            .astype(jnp.bfloat16)
            .reshape(rows, width)
        )
        early = contract(attn_grad, context_low, 0, 0)
        early_halved = dp_pow2(early, dp_size)
        if early_halved:
            early = dp_halve(early.astype(jnp.bfloat16), dp_size, jnp.float32)
        else:
            early = lax.psum_scatter(early, "dp", scatter_dimension=0, tiled=True)
        if passages == 1:
            proj_grad, grad_qkv_low = attention_backward(
                query_low, key_low, value_low, context_grad, own_lengths, factor, tokens
            )
            grad_qkv_low, ffn_grads = lax.optimization_barrier((grad_qkv_low, ffn_grads))
        else:
            proj_grad = attention_backward(
                query_low, key_low, value_low, context_grad, own_lengths, factor
            )
            grad_qkv_low = jnp.einsum(
                "rd,kre->kde", tokens, proj_grad, preferred_element_type=jnp.float32
            ).astype(jnp.bfloat16)
        grad_bias_full = jnp.sum(proj_grad[0::2], axis=1, dtype=jnp.float32)

        def back_project(grad, weight):
            return jnp.einsum(
                "rgj,gdj->rd",
                grad.reshape(rows, groups, shard),
                weight,
                preferred_element_type=jnp.float32,
            )

        input_part = (
            back_project(proj_grad[0], query_weight)
            + back_project(proj_grad[1], key_weight)
            + back_project(proj_grad[2], value_weight)
        )
        input_grad = (first_grad + input_part).astype(jnp.bfloat16)

        small = jnp.stack(
            [
                grad_out_bias,
                grad_norm1_gain,
                grad_norm1_shift,
                grad_down_bias,
                grad_norm2_gain,
                grad_norm2_shift,
            ]
        )
        n_small = small.shape[0]
        small_rep = jnp.tile(small.reshape(n_small, groups, shard), (1, 1, groups)).reshape(
            n_small * groups, width
        )
        up_parts = grad_up_bias.shape[0] // shard
        own_group = (jnp.arange(width) // shard == tensor_index)[None, :]
        up_rep = jnp.where(
            own_group, jnp.tile(grad_up_bias.reshape(up_parts, shard), (1, groups)), 0.0
        )
        tail = jnp.concatenate([grad_bias_full, small_rep, up_rep], axis=0)
        tail_rows = tail.shape[0]
        tail = jnp.pad(tail, ((0, -(-tail_rows // 8) * 8 - tail_rows), (0, 0)))
        late = lax.psum_scatter(
            grad_qkv_low.reshape(3 * width, width),
            "dp",
            scatter_dimension=0,
            tiled=True,
        ).astype(jnp.float32)
        joined = jnp.concatenate([late, early, tail], axis=0)
        joined = lax.psum_scatter(
            joined.reshape(joined.shape[0], groups, shard).transpose(1, 0, 2),
            "tensor",
            scatter_dimension=0,
            tiled=True,
        )[0]
        if halved:
            ffn_grads = tuple(
                dp_double(g.astype(jnp.bfloat16), dp_size).astype(jnp.float32) for g in ffn_grads
            )
            joined, ffn_grads = lax.optimization_barrier((joined, ffn_grads))
        grad_up_weight, grad_down_weight = ffn_grads
        late_rows = late.shape[0]
        early_rows = early.shape[0]
        joined = lax.all_gather(joined, "dp", axis=0, tiled=False)
        early = joined[:, late_rows : late_rows + early_rows]
        if early_halved:
            order = bit_reversed(dp_size)
            place = [order.index(b) for b in range(dp_size)]
            early = jnp.concatenate([early[p] for p in place], axis=0)
        pieces = [
            joined[:, :late_rows].reshape(-1, shard),
            early.reshape(-1, shard),
            jnp.sum(joined[:, late_rows + early_rows :], axis=0),
        ]
        grad_qkv_weight = pieces[0].reshape(3, width, shard)
        grad_out_weight = pieces[1].T
        tail = pieces[2]
        grad_qkv_bias = tail[:2]
        small_sum = tail[2 : 2 + n_small * groups].reshape(n_small, width)
        grad_up_bias = tail[2 + n_small * groups : 2 + n_small * groups + up_parts].reshape(-1)
        (
            grad_out_bias,
            grad_norm1_gain,
            grad_norm1_shift,
            grad_down_bias,
            grad_norm2_gain,
            grad_norm2_shift,
        ) = [small_sum[i] for i in range(n_small)]
        return (
            layer_out.astype(jnp.bfloat16),
            input_grad,
            grad_qkv_weight,
            grad_qkv_bias,
            grad_out_weight,
            grad_out_bias,
            grad_norm1_gain,
            grad_norm1_shift,
            grad_up_weight,
            grad_up_bias,
            grad_down_weight,
            grad_down_bias,
            grad_norm2_gain,
            grad_norm2_shift,
        )

    return per_device


def solution(mesh):
    placed = (
        P(("dp", "tensor"), None),
        P(("dp", "tensor"), None),
        P("dp"),
        P(None, None, "tensor"),
        P(None, "tensor"),
        P("tensor", None),
        P(),
        P(),
        P(),
        P(None, "tensor"),
        P("tensor"),
        P("tensor", None),
        P(),
        P(),
        P(),
    )
    return jax.shard_map(
        make_per_device(mesh.shape["dp"]),
        mesh=mesh,
        in_specs=placed,
        out_specs=(
            P(("dp", "tensor"), None),
            P(("dp", "tensor"), None),
            P(None, None, "tensor"),
            P(None, "tensor"),
            P("tensor", None),
            P(),
            P(),
            P(),
            P(None, "tensor"),
            P("tensor"),
            P("tensor", None),
            P(),
            P(),
            P(),
        ),
        check_vma=False,
    )
```

```python
import functools

import jax
import jax.numpy as jnp
from jax import lax
from jax.experimental import pallas as pl
from jax.experimental.pallas import tpu as pltpu
from jax.sharding import PartitionSpec as P

HD = 64
LEN = 512


EPS = 1e-12
NEG = -1e30


def layer_norm(values, gain_vec, shift_vec):
    center = values - jnp.mean(values, axis=-1, keepdims=True)
    spread = jnp.mean(center * center, axis=-1, keepdims=True)
    return center * lax.rsqrt(spread + EPS) * gain_vec + shift_vec


def gelu_and_slope(values):
    cdf = 0.5 * (1.0 + lax.erf(values * (2.0 ** -0.5)))
    density = jnp.exp(-0.5 * values * values) * ((2.0 * jnp.pi) ** -0.5)
    return values * cdf, cdf + values * density


def contract(left, right, left_dim, right_dim):
    return lax.dot_general(
        left, right, (((left_dim,), (right_dim,)), ((), ())), preferred_element_type=jnp.float32
    )


def _probs(q, k, length, factor):
    scores = lax.dot_general(q, k, (((1,), (1,)), ((), ())), preferred_element_type=jnp.float32) * factor
    col = lax.broadcasted_iota(jnp.int32, scores.shape, 1)
    scores = jnp.where(col < length, scores, NEG)
    top = jnp.max(scores, axis=1, keepdims=True)
    raised = jnp.exp(scores - top)
    return raised / jnp.sum(raised, axis=1, keepdims=True)


def _fwd_kernel(len_ref, q_ref, k_ref, v_ref, out_ref, *, heads, factor):
    length = len_ref[pl.program_id(0)]
    for h in range(heads):
        cols = slice(h * HD, (h + 1) * HD)
        probs = _probs(q_ref[:, cols], k_ref[:, cols], length, factor)
        out_ref[:, cols] = jnp.dot(
            probs.astype(jnp.bfloat16), v_ref[:, cols], preferred_element_type=jnp.float32
        ).astype(out_ref.dtype)


def _bwd_kernel(len_ref, q_ref, k_ref, v_ref, grad_ref, *rest, heads, factor):
    if len(rest) == 3:
        tokens_ref, out_ref, wgrad_ref = rest
    else:
        (out_ref,), tokens_ref = rest, None
    length = len_ref[pl.program_id(0)]
    for h in range(heads):
        cols = slice(h * HD, (h + 1) * HD)
        q = q_ref[:, cols]
        k = k_ref[:, cols]
        v = v_ref[:, cols]
        g = grad_ref[:, cols]
        probs = _probs(q, k, length, factor)
        prob_grad = lax.dot_general(g, v, (((1,), (1,)), ((), ())), preferred_element_type=jnp.float32)
        row_dot = jnp.sum(prob_grad * probs, axis=1, keepdims=True)
        score_grad = (probs * (prob_grad - row_dot)).astype(jnp.bfloat16)
        out_ref[0, :, cols] = (
            jnp.dot(score_grad, k, preferred_element_type=jnp.float32) * factor
        ).astype(out_ref.dtype)
        out_ref[1, :, cols] = (
            lax.dot_general(score_grad, q, (((0,), (0,)), ((), ())), preferred_element_type=jnp.float32)
            * factor
        ).astype(out_ref.dtype)
        out_ref[2, :, cols] = lax.dot_general(
            probs.astype(jnp.bfloat16), g, (((0,), (0,)), ((), ())), preferred_element_type=jnp.float32
        ).astype(out_ref.dtype)
    if tokens_ref is not None:
        tokens = tokens_ref[...]
        for t in range(3):
            wgrad_ref[t] = lax.dot_general(
                tokens, out_ref[t], (((0,), (0,)), ((), ())), preferred_element_type=jnp.float32
            ).astype(wgrad_ref.dtype)


def attention_forward(queries, keys, values, lengths, factor, pair=2):
    rows, width = queries.shape
    block = pl.BlockSpec((LEN, pair * HD), lambda p, i, n: (p, i))
    return pl.pallas_call(
        functools.partial(_fwd_kernel, heads=pair, factor=factor),
        out_shape=jax.ShapeDtypeStruct((rows, width), jnp.bfloat16),
        grid_spec=pltpu.PrefetchScalarGridSpec(
            num_scalar_prefetch=1,
            grid=(rows // LEN, width // (pair * HD)),
            in_specs=[block] * 3,
            out_specs=block,
        ),
        cost_estimate=pl.CostEstimate(
            flops=4 * rows * LEN * width,
            transcendentals=rows * LEN * width // HD,
            bytes_accessed=4 * rows * width * 2,
        ),
    )(lengths, queries, keys, values)


def attention_backward(queries, keys, values, context_grad, lengths, factor, tokens=None, pair=2):
    rows, width = queries.shape
    block = pl.BlockSpec((LEN, pair * HD), lambda p, i, n: (p, i))
    grad_spec = pl.BlockSpec((3, LEN, pair * HD), lambda p, i, n: (0, p, i))
    grad_shape = jax.ShapeDtypeStruct((3, rows, width), jnp.bfloat16)
    operands = [lengths, queries, keys, values, context_grad]
    in_specs = [block] * 4
    out_specs, out_shape = grad_spec, grad_shape
    if tokens is not None:
        depth = tokens.shape[1]
        operands.append(tokens)
        in_specs.append(pl.BlockSpec((LEN, depth), lambda p, i, n: (p, 0)))
        out_specs = [grad_spec, pl.BlockSpec((3, depth, pair * HD), lambda p, i, n: (0, 0, i))]
        out_shape = [grad_shape, jax.ShapeDtypeStruct((3, depth, width), jnp.bfloat16)]
    return pl.pallas_call(
        functools.partial(_bwd_kernel, heads=pair, factor=factor),
        out_shape=out_shape,
        grid_spec=pltpu.PrefetchScalarGridSpec(
            num_scalar_prefetch=1,
            grid=(rows // LEN, width // (pair * HD)),
            in_specs=in_specs,
            out_specs=out_specs,
        ),
        cost_estimate=pl.CostEstimate(
            flops=16 * rows * LEN * width,
            transcendentals=rows * LEN * width // HD,
            bytes_accessed=10 * rows * width * 2,
        ),
    )(*operands)


def _tn_kernel(left_ref, right_ref, out_ref):
    out_ref[...] = lax.dot_general(
        left_ref[...], right_ref[...], (((0,), (0,)), ((), ())), preferred_element_type=jnp.float32
    )


def tn_matmul(left, right, tile=256):
    depth, rows = left.shape
    cols = right.shape[1]
    return pl.pallas_call(
        _tn_kernel,
        out_shape=jax.ShapeDtypeStruct((rows, cols), jnp.float32),
        grid=(rows // tile,),
        in_specs=[
            pl.BlockSpec((depth, tile), lambda i: (0, i)),
            pl.BlockSpec((depth, cols), lambda i: (0, 0)),
        ],
        out_specs=pl.BlockSpec((tile, cols), lambda i: (i, 0)),
        cost_estimate=pl.CostEstimate(
            flops=2 * depth * rows * cols,
            transcendentals=0,
            bytes_accessed=2 * depth * (rows + cols) + 4 * rows * cols,
        ),
    )(left, right)


def dp_pow2(values, dp_size):
    steps = dp_size.bit_length() - 1
    return dp_size == 1 << steps and values.shape[0] % dp_size == 0


def dp_halve(values, dp_size, sum_dtype=None, high_first=False):
    steps = dp_size.bit_length() - 1
    index = lax.axis_index("dp")
    link = values.dtype
    kept = values if sum_dtype is None else values.astype(sum_dtype)
    for step in reversed(range(steps)) if high_first else range(steps):
        bit = (index >> step) & 1
        half = kept.shape[0] // 2
        keep = lax.dynamic_slice_in_dim(kept, bit * half, half)
        give = lax.dynamic_slice_in_dim(kept, (1 - bit) * half, half).astype(link)
        got = lax.ppermute(give, "dp", [(i, i ^ (1 << step)) for i in range(dp_size)])
        kept = keep + got.astype(kept.dtype)
    return kept


def dp_double(kept, dp_size):
    steps = dp_size.bit_length() - 1
    index = lax.axis_index("dp")
    for step in reversed(range(steps)):
        bit = (index >> step) & 1
        got = lax.ppermute(kept, "dp", [(i, i ^ (1 << step)) for i in range(dp_size)])
        kept = jnp.concatenate(
            [jnp.where(bit == 0, kept, got), jnp.where(bit == 0, got, kept)]
        )
    return kept


def make_per_device(dp_size):
    def per_device(
        tokens,
        out_grad,
        lengths,
        qkv_weight,
        qkv_bias,
        out_weight,
        out_bias,
        norm1_gain,
        norm1_shift,
        up_weight,
        up_bias,
        down_weight,
        down_bias,
        norm2_gain,
        norm2_shift,
    ):
        rows, width = tokens.shape
        shard = qkv_weight.shape[2]
        groups = width // shard
        passages = rows // LEN
        factor = HD ** (-0.5)

        half_rows = -(-(2 * width + 2) // 8) * 8
        first_half = jnp.pad(
            jnp.concatenate([qkv_weight[0], qkv_weight[1], qkv_bias], axis=0),
            ((0, half_rows - 2 * width - 2), (0, 0)),
        )
        second_half = jnp.pad(
            jnp.concatenate([qkv_weight[2], out_weight.T], axis=0),
            ((0, half_rows - 2 * width), (0, 0)),
        )
        dp_index = lax.axis_index("dp")
        parity = dp_index % 2
        mine = jnp.where(parity == 0, first_half, second_half)
        mine = lax.all_gather(mine, "tensor", axis=0, tiled=False)
        other = lax.ppermute(mine, "dp", [(i, i ^ 1) for i in range(dp_size)])
        first_half = jnp.where(parity == 0, mine, other)
        second_half = jnp.where(parity == 0, other, mine)
        query_weight = first_half[:, :width]
        key_weight = first_half[:, width : 2 * width]
        query_bias = first_half[:, 2 * width]
        value_bias = first_half[:, 2 * width + 1]
        value_weight = second_half[:, :width]
        proj_blocks = second_half[:, width : 2 * width]

        tensor_index = lax.axis_index("tensor")
        own_lengths = lax.dynamic_slice_in_dim(lengths, tensor_index * passages, passages)

        own_tokens = tokens.astype(jnp.float32)
        def project(weight, bias=None):
            out = jnp.einsum("rd,gdj->rgj", tokens, weight, preferred_element_type=jnp.float32)
            out = out if bias is None else out + bias
            return out.astype(jnp.bfloat16).reshape(rows, width)

        query_low = project(query_weight, query_bias)
        key_low = project(key_weight)
        value_low = project(value_weight, value_bias)
        context_low = attention_forward(query_low, key_low, value_low, own_lengths, factor)
        attn_out = jnp.einsum(
            "rgj,gcj->rc",
            context_low.reshape(rows, groups, shard),
            proj_blocks,
            preferred_element_type=jnp.float32,
        )
        middle, norm1_back = jax.vjp(
            layer_norm, own_tokens + attn_out + out_bias, norm1_gain, norm1_shift
        )
        middle_low = middle.astype(jnp.bfloat16)
        ffn_rows = lax.all_gather(middle_low, "tensor", axis=0, tiled=True)
        pre_act = jnp.dot(ffn_rows, up_weight, preferred_element_type=jnp.float32) + up_bias
        activated, gelu_slope = gelu_and_slope(pre_act)
        hidden = activated.astype(jnp.bfloat16)
        ffn_out = lax.psum_scatter(
            jnp.dot(hidden, down_weight, preferred_element_type=jnp.float32).astype(jnp.bfloat16),
            "tensor",
            scatter_dimension=0,
            tiled=True,
        ).astype(jnp.float32)
        layer_out, norm2_back = jax.vjp(
            layer_norm, middle + ffn_out + down_bias, norm2_gain, norm2_shift
        )
        second_grad, grad_norm2_gain, grad_norm2_shift = norm2_back(out_grad.astype(jnp.float32))
        branch_grad = second_grad.astype(jnp.bfloat16)
        grad_down_bias = jnp.sum(branch_grad, axis=0, dtype=jnp.float32)
        branch_rows = lax.all_gather(branch_grad, "tensor", axis=0, tiled=True)
        hidden_grad = contract(branch_rows, down_weight, 1, 1)
        grad_down_weight = tn_matmul(hidden, branch_rows)
        pre_grad = (hidden_grad * gelu_slope).astype(jnp.bfloat16)
        grad_up_bias = jnp.sum(pre_grad, axis=0, dtype=jnp.float32)
        grad_up_weight = tn_matmul(ffn_rows, pre_grad)
        ffn_grads = (grad_up_weight, grad_down_weight)
        halved = all(dp_pow2(g, dp_size) for g in ffn_grads)
        if halved:
            ffn_grads = tuple(dp_halve(g, dp_size) for g in ffn_grads)
        else:
            ffn_grads = lax.psum(ffn_grads, "dp")
        middle_part = lax.psum_scatter(
            contract(pre_grad, up_weight, 1, 1).astype(jnp.bfloat16),
            "tensor",
            scatter_dimension=0,
            tiled=True,
        ).astype(jnp.float32)
        first_grad, grad_norm1_gain, grad_norm1_shift = norm1_back(second_grad + middle_part)
        attn_grad = first_grad.astype(jnp.bfloat16)
        grad_out_bias = jnp.sum(attn_grad, axis=0, dtype=jnp.float32)
        context_grad = (
            jnp.einsum("rc,gcj->rgj", attn_grad, proj_blocks, preferred_element_type=jnp.float32)
            .astype(jnp.bfloat16)
            .reshape(rows, width)
        )
        early = contract(attn_grad, context_low, 0, 0)
        early_halved = dp_pow2(early, dp_size)
        if early_halved:
            early = dp_halve(early.astype(jnp.bfloat16), dp_size, jnp.float32, high_first=True)
        else:
            early = lax.psum_scatter(early, "dp", scatter_dimension=0, tiled=True)
        if passages == 1:
            proj_grad, grad_qkv_low = attention_backward(
                query_low, key_low, value_low, context_grad, own_lengths, factor, tokens
            )
            grad_qkv_low, ffn_grads = lax.optimization_barrier((grad_qkv_low, ffn_grads))
        else:
            proj_grad = attention_backward(
                query_low, key_low, value_low, context_grad, own_lengths, factor
            )
            grad_qkv_low = jnp.einsum(
                "rd,kre->kde", tokens, proj_grad, preferred_element_type=jnp.float32
            ).astype(jnp.bfloat16)
        grad_bias_full = jnp.sum(proj_grad[0::2], axis=1, dtype=jnp.float32)

        def back_project(grad, weight):
            return jnp.einsum(
                "rgj,gdj->rd",
                grad.reshape(rows, groups, shard),
                weight,
                preferred_element_type=jnp.float32,
            )

        input_part = (
            back_project(proj_grad[0], query_weight)
            + back_project(proj_grad[1], key_weight)
            + back_project(proj_grad[2], value_weight)
        )
        input_grad = (first_grad + input_part).astype(jnp.bfloat16)

        small = jnp.stack(
            [
                grad_out_bias,
                grad_norm1_gain,
                grad_norm1_shift,
                grad_down_bias,
                grad_norm2_gain,
                grad_norm2_shift,
            ]
        )
        n_small = small.shape[0]
        small_rep = jnp.tile(small.reshape(n_small, groups, shard), (1, 1, groups)).reshape(
            n_small * groups, width
        )
        up_parts = grad_up_bias.shape[0] // shard
        own_group = (jnp.arange(width) // shard == tensor_index)[None, :]
        up_rep = jnp.where(
            own_group, jnp.tile(grad_up_bias.reshape(up_parts, shard), (1, groups)), 0.0
        )
        tail = jnp.concatenate([grad_bias_full, small_rep, up_rep], axis=0)
        tail_rows = tail.shape[0]
        tail = jnp.pad(tail, ((0, -(-tail_rows // 8) * 8 - tail_rows), (0, 0)))
        late = lax.psum_scatter(
            grad_qkv_low.reshape(3 * width, width),
            "dp",
            scatter_dimension=0,
            tiled=True,
        ).astype(jnp.float32)
        joined = jnp.concatenate([late, early, tail], axis=0)
        joined = lax.psum_scatter(
            joined.reshape(joined.shape[0], groups, shard).transpose(1, 0, 2),
            "tensor",
            scatter_dimension=0,
            tiled=True,
        )[0]
        if halved:
            ffn_grads = tuple(
                dp_double(g.astype(jnp.bfloat16), dp_size).astype(jnp.float32) for g in ffn_grads
            )
            joined, ffn_grads = lax.optimization_barrier((joined, ffn_grads))
        grad_up_weight, grad_down_weight = ffn_grads
        late_rows = late.shape[0]
        early_rows = early.shape[0]
        joined = lax.all_gather(joined, "dp", axis=0, tiled=False)
        early = joined[:, late_rows : late_rows + early_rows]
        pieces = [
            joined[:, :late_rows].reshape(-1, shard),
            early.reshape(-1, shard),
            jnp.sum(joined[:, late_rows + early_rows :], axis=0),
        ]
        grad_qkv_weight = pieces[0].reshape(3, width, shard)
        grad_out_weight = pieces[1].T
        tail = pieces[2]
        grad_qkv_bias = tail[:2]
        small_sum = tail[2 : 2 + n_small * groups].reshape(n_small, width)
        grad_up_bias = tail[2 + n_small * groups : 2 + n_small * groups + up_parts].reshape(-1)
        (
            grad_out_bias,
            grad_norm1_gain,
            grad_norm1_shift,
            grad_down_bias,
            grad_norm2_gain,
            grad_norm2_shift,
        ) = [small_sum[i] for i in range(n_small)]
        return (
            layer_out.astype(jnp.bfloat16),
            input_grad,
            grad_qkv_weight,
            grad_qkv_bias,
            grad_out_weight,
            grad_out_bias,
            grad_norm1_gain,
            grad_norm1_shift,
            grad_up_weight,
            grad_up_bias,
            grad_down_weight,
            grad_down_bias,
            grad_norm2_gain,
            grad_norm2_shift,
        )

    return per_device


def solution(mesh):
    placed = (
        P(("dp", "tensor"), None),
        P(("dp", "tensor"), None),
        P("dp"),
        P(None, None, "tensor"),
        P(None, "tensor"),
        P("tensor", None),
        P(),
        P(),
        P(),
        P(None, "tensor"),
        P("tensor"),
        P("tensor", None),
        P(),
        P(),
        P(),
    )
    return jax.shard_map(
        make_per_device(mesh.shape["dp"]),
        mesh=mesh,
        in_specs=placed,
        out_specs=(
            P(("dp", "tensor"), None),
            P(("dp", "tensor"), None),
            P(None, None, "tensor"),
            P(None, "tensor"),
            P("tensor", None),
            P(),
            P(),
            P(),
            P(None, "tensor"),
            P("tensor"),
            P("tensor", None),
            P(),
            P(),
            P(),
        ),
        check_vma=False,
    )
```

```python
import functools

import jax
import jax.numpy as jnp
from jax import lax
from jax.experimental import pallas as pl
from jax.experimental.pallas import tpu as pltpu
from jax.sharding import PartitionSpec as P

HD = 64
LEN = 512


EPS = 1e-12
NEG = -1e30


def layer_norm(values, gain_vec, shift_vec):
    center = values - jnp.mean(values, axis=-1, keepdims=True)
    spread = jnp.mean(center * center, axis=-1, keepdims=True)
    return center * lax.rsqrt(spread + EPS) * gain_vec + shift_vec


def gelu_and_slope(values):
    cdf = 0.5 * (1.0 + lax.erf(values * (2.0 ** -0.5)))
    density = jnp.exp(-0.5 * values * values) * ((2.0 * jnp.pi) ** -0.5)
    return values * cdf, cdf + values * density


def contract(left, right, left_dim, right_dim):
    return lax.dot_general(
        left, right, (((left_dim,), (right_dim,)), ((), ())), preferred_element_type=jnp.float32
    )


def _probs(q, k, length, factor):
    scores = lax.dot_general(q, k, (((1,), (1,)), ((), ())), preferred_element_type=jnp.float32) * factor
    col = lax.broadcasted_iota(jnp.int32, scores.shape, 1)
    scores = jnp.where(col < length, scores, NEG)
    top = jnp.max(scores, axis=1, keepdims=True)
    raised = jnp.exp(scores - top)
    return raised / jnp.sum(raised, axis=1, keepdims=True)


def _fwd_kernel(len_ref, q_ref, k_ref, v_ref, out_ref, *, heads, factor):
    length = len_ref[pl.program_id(0)]
    for h in range(heads):
        cols = slice(h * HD, (h + 1) * HD)
        probs = _probs(q_ref[:, cols], k_ref[:, cols], length, factor)
        out_ref[:, cols] = jnp.dot(
            probs.astype(jnp.bfloat16), v_ref[:, cols], preferred_element_type=jnp.float32
        ).astype(out_ref.dtype)


def _bwd_kernel(len_ref, q_ref, k_ref, v_ref, grad_ref, *rest, heads, factor):
    if len(rest) == 3:
        tokens_ref, out_ref, wgrad_ref = rest
    else:
        (out_ref,), tokens_ref = rest, None
    length = len_ref[pl.program_id(0)]
    for h in range(heads):
        cols = slice(h * HD, (h + 1) * HD)
        q = q_ref[:, cols]
        k = k_ref[:, cols]
        v = v_ref[:, cols]
        g = grad_ref[:, cols]
        probs = _probs(q, k, length, factor)
        prob_grad = lax.dot_general(g, v, (((1,), (1,)), ((), ())), preferred_element_type=jnp.float32)
        row_dot = jnp.sum(prob_grad * probs, axis=1, keepdims=True)
        score_grad = (probs * (prob_grad - row_dot)).astype(jnp.bfloat16)
        out_ref[0, :, cols] = (
            jnp.dot(score_grad, k, preferred_element_type=jnp.float32) * factor
        ).astype(out_ref.dtype)
        out_ref[1, :, cols] = (
            lax.dot_general(score_grad, q, (((0,), (0,)), ((), ())), preferred_element_type=jnp.float32)
            * factor
        ).astype(out_ref.dtype)
        out_ref[2, :, cols] = lax.dot_general(
            probs.astype(jnp.bfloat16), g, (((0,), (0,)), ((), ())), preferred_element_type=jnp.float32
        ).astype(out_ref.dtype)
    if tokens_ref is not None:
        tokens = tokens_ref[...]
        for t in range(3):
            wgrad_ref[t] = lax.dot_general(
                tokens, out_ref[t], (((0,), (0,)), ((), ())), preferred_element_type=jnp.float32
            ).astype(wgrad_ref.dtype)


def attention_forward(queries, keys, values, lengths, factor, pair=2):
    rows, width = queries.shape
    block = pl.BlockSpec((LEN, pair * HD), lambda p, i, n: (p, i))
    return pl.pallas_call(
        functools.partial(_fwd_kernel, heads=pair, factor=factor),
        out_shape=jax.ShapeDtypeStruct((rows, width), jnp.bfloat16),
        grid_spec=pltpu.PrefetchScalarGridSpec(
            num_scalar_prefetch=1,
            grid=(rows // LEN, width // (pair * HD)),
            in_specs=[block] * 3,
            out_specs=block,
        ),
        cost_estimate=pl.CostEstimate(
            flops=4 * rows * LEN * width,
            transcendentals=rows * LEN * width // HD,
            bytes_accessed=4 * rows * width * 2,
        ),
    )(lengths, queries, keys, values)


def attention_backward(queries, keys, values, context_grad, lengths, factor, tokens=None, pair=2):
    rows, width = queries.shape
    block = pl.BlockSpec((LEN, pair * HD), lambda p, i, n: (p, i))
    grad_spec = pl.BlockSpec((3, LEN, pair * HD), lambda p, i, n: (0, p, i))
    grad_shape = jax.ShapeDtypeStruct((3, rows, width), jnp.bfloat16)
    operands = [lengths, queries, keys, values, context_grad]
    in_specs = [block] * 4
    out_specs, out_shape = grad_spec, grad_shape
    if tokens is not None:
        depth = tokens.shape[1]
        operands.append(tokens)
        in_specs.append(pl.BlockSpec((LEN, depth), lambda p, i, n: (p, 0)))
        out_specs = [grad_spec, pl.BlockSpec((3, depth, pair * HD), lambda p, i, n: (0, 0, i))]
        out_shape = [grad_shape, jax.ShapeDtypeStruct((3, depth, width), jnp.bfloat16)]
    return pl.pallas_call(
        functools.partial(_bwd_kernel, heads=pair, factor=factor),
        out_shape=out_shape,
        grid_spec=pltpu.PrefetchScalarGridSpec(
            num_scalar_prefetch=1,
            grid=(rows // LEN, width // (pair * HD)),
            in_specs=in_specs,
            out_specs=out_specs,
        ),
        cost_estimate=pl.CostEstimate(
            flops=16 * rows * LEN * width,
            transcendentals=rows * LEN * width // HD,
            bytes_accessed=10 * rows * width * 2,
        ),
    )(*operands)


def _tn_kernel(left_ref, right_ref, out_ref):
    out_ref[...] = lax.dot_general(
        left_ref[...], right_ref[...], (((0,), (0,)), ((), ())), preferred_element_type=jnp.float32
    )


def tn_matmul(left, right, tile=256):
    depth, rows = left.shape
    cols = right.shape[1]
    return pl.pallas_call(
        _tn_kernel,
        out_shape=jax.ShapeDtypeStruct((rows, cols), jnp.float32),
        grid=(rows // tile,),
        in_specs=[
            pl.BlockSpec((depth, tile), lambda i: (0, i)),
            pl.BlockSpec((depth, cols), lambda i: (0, 0)),
        ],
        out_specs=pl.BlockSpec((tile, cols), lambda i: (i, 0)),
        cost_estimate=pl.CostEstimate(
            flops=2 * depth * rows * cols,
            transcendentals=0,
            bytes_accessed=2 * depth * (rows + cols) + 4 * rows * cols,
        ),
    )(left, right)


def dp_pow2(values, dp_size):
    steps = dp_size.bit_length() - 1
    return dp_size == 1 << steps and values.shape[0] % dp_size == 0


def dp_halve(values, dp_size, sum_dtype=None):
    steps = dp_size.bit_length() - 1
    index = lax.axis_index("dp")
    link = values.dtype
    kept = values if sum_dtype is None else values.astype(sum_dtype)
    for step in range(steps):
        bit = (index >> step) & 1
        half = kept.shape[0] // 2
        keep = lax.dynamic_slice_in_dim(kept, bit * half, half)
        give = lax.dynamic_slice_in_dim(kept, (1 - bit) * half, half).astype(link)
        got = lax.ppermute(give, "dp", [(i, i ^ (1 << step)) for i in range(dp_size)])
        kept = keep + got.astype(kept.dtype)
    return kept


def bit_reversed(count):
    steps = count.bit_length() - 1
    return [int(format(i, f"0{steps}b")[::-1], 2) if steps else 0 for i in range(count)]


def dp_double(kept, dp_size):
    steps = dp_size.bit_length() - 1
    index = lax.axis_index("dp")
    for step in reversed(range(steps)):
        bit = (index >> step) & 1
        got = lax.ppermute(kept, "dp", [(i, i ^ (1 << step)) for i in range(dp_size)])
        kept = jnp.concatenate(
            [jnp.where(bit == 0, kept, got), jnp.where(bit == 0, got, kept)]
        )
    return kept


def make_per_device(dp_size):
    def per_device(
        tokens,
        out_grad,
        lengths,
        qkv_weight,
        qkv_bias,
        out_weight,
        out_bias,
        norm1_gain,
        norm1_shift,
        up_weight,
        up_bias,
        down_weight,
        down_bias,
        norm2_gain,
        norm2_shift,
    ):
        rows, width = tokens.shape
        shard = qkv_weight.shape[2]
        groups = width // shard
        passages = rows // LEN
        factor = HD ** (-0.5)

        half_rows = -(-(2 * width + 2) // 8) * 8
        first_half = jnp.pad(
            jnp.concatenate([qkv_weight[0], qkv_weight[1], qkv_bias], axis=0),
            ((0, half_rows - 2 * width - 2), (0, 0)),
        )
        second_half = jnp.pad(
            jnp.concatenate([qkv_weight[2], out_weight.T], axis=0),
            ((0, half_rows - 2 * width), (0, 0)),
        )
        dp_index = lax.axis_index("dp")
        parity = dp_index % 2
        mine = jnp.where(parity == 0, first_half, second_half)
        mine = lax.all_gather(mine, "tensor", axis=0, tiled=False)
        other = lax.ppermute(mine, "dp", [(i, i ^ 1) for i in range(dp_size)])
        first_half = jnp.where(parity == 0, mine, other)
        second_half = jnp.where(parity == 0, other, mine)
        query_weight = first_half[:, :width]
        key_weight = first_half[:, width : 2 * width]
        query_bias = first_half[:, 2 * width]
        value_bias = first_half[:, 2 * width + 1]
        value_weight = second_half[:, :width]
        proj_blocks = second_half[:, width : 2 * width]

        tensor_index = lax.axis_index("tensor")
        own_lengths = lax.dynamic_slice_in_dim(lengths, tensor_index * passages, passages)

        own_tokens = tokens.astype(jnp.float32)
        def project(weight, bias=None):
            out = jnp.einsum("rd,gdj->rgj", tokens, weight, preferred_element_type=jnp.float32)
            out = out if bias is None else out + bias
            return out.astype(jnp.bfloat16).reshape(rows, width)

        query_low = project(query_weight, query_bias)
        key_low = project(key_weight)
        value_low = project(value_weight, value_bias)
        context_low = attention_forward(query_low, key_low, value_low, own_lengths, factor)
        attn_out = jnp.einsum(
            "rgj,gcj->rc",
            context_low.reshape(rows, groups, shard),
            proj_blocks,
            preferred_element_type=jnp.float32,
        )
        middle, norm1_back = jax.vjp(
            layer_norm, own_tokens + attn_out + out_bias, norm1_gain, norm1_shift
        )
        middle_low = middle.astype(jnp.bfloat16)
        ffn_rows = lax.all_gather(middle_low, "tensor", axis=0, tiled=True)
        pre_act = jnp.dot(ffn_rows, up_weight, preferred_element_type=jnp.float32) + up_bias
        activated, gelu_slope = gelu_and_slope(pre_act)
        hidden = activated.astype(jnp.bfloat16)
        ffn_out = lax.psum_scatter(
            jnp.dot(hidden, down_weight, preferred_element_type=jnp.float32).astype(jnp.bfloat16),
            "tensor",
            scatter_dimension=0,
            tiled=True,
        ).astype(jnp.float32)
        layer_out, norm2_back = jax.vjp(
            layer_norm, middle + ffn_out + down_bias, norm2_gain, norm2_shift
        )
        second_grad, grad_norm2_gain, grad_norm2_shift = norm2_back(out_grad.astype(jnp.float32))
        branch_grad = second_grad.astype(jnp.bfloat16)
        grad_down_bias = jnp.sum(branch_grad, axis=0, dtype=jnp.float32)
        branch_rows = lax.all_gather(branch_grad, "tensor", axis=0, tiled=True)
        hidden_grad = contract(branch_rows, down_weight, 1, 1)
        grad_down_weight = tn_matmul(hidden, branch_rows)
        pre_grad = (hidden_grad * gelu_slope).astype(jnp.bfloat16)
        grad_up_bias = jnp.sum(pre_grad, axis=0, dtype=jnp.float32)
        grad_up_weight = tn_matmul(ffn_rows, pre_grad)
        ffn_grads = (grad_up_weight, grad_down_weight)
        halved = all(dp_pow2(g, dp_size) for g in ffn_grads)
        if halved:
            ffn_grads = tuple(dp_halve(g, dp_size) for g in ffn_grads)
        else:
            ffn_grads = lax.psum(ffn_grads, "dp")
        middle_part = lax.psum_scatter(
            contract(pre_grad, up_weight, 1, 1).astype(jnp.bfloat16),
            "tensor",
            scatter_dimension=0,
            tiled=True,
        ).astype(jnp.float32)
        first_grad, grad_norm1_gain, grad_norm1_shift = norm1_back(second_grad + middle_part)
        attn_grad = first_grad.astype(jnp.bfloat16)
        grad_out_bias = jnp.sum(attn_grad, axis=0, dtype=jnp.float32)
        context_grad = (
            jnp.einsum("rc,gcj->rgj", attn_grad, proj_blocks, preferred_element_type=jnp.float32)
            .astype(jnp.bfloat16)
            .reshape(rows, width)
        )
        early = contract(attn_grad, context_low, 0, 0)
        early_halved = dp_pow2(early, dp_size)
        if early_halved:
            early = dp_halve(early.astype(jnp.bfloat16), dp_size, jnp.float32)
        else:
            early = lax.psum_scatter(early, "dp", scatter_dimension=0, tiled=True)
        if passages == 1:
            proj_grad, grad_qkv_low = attention_backward(
                query_low, key_low, value_low, context_grad, own_lengths, factor, tokens
            )
            grad_qkv_low, ffn_grads = lax.optimization_barrier((grad_qkv_low, ffn_grads))
        else:
            proj_grad = attention_backward(
                query_low, key_low, value_low, context_grad, own_lengths, factor
            )
            grad_qkv_low = jnp.einsum(
                "rd,kre->kde", tokens, proj_grad, preferred_element_type=jnp.float32
            ).astype(jnp.bfloat16)
        grad_bias_full = jnp.sum(proj_grad[0::2], axis=1, dtype=jnp.float32)

        def back_project(grad, weight):
            return jnp.einsum(
                "rgj,gdj->rd",
                grad.reshape(rows, groups, shard),
                weight,
                preferred_element_type=jnp.float32,
            )

        input_part = (
            back_project(proj_grad[0], query_weight)
            + back_project(proj_grad[1], key_weight)
            + back_project(proj_grad[2], value_weight)
        )
        input_grad = (first_grad + input_part).astype(jnp.bfloat16)

        small = jnp.stack(
            [
                grad_out_bias,
                grad_norm1_gain,
                grad_norm1_shift,
                grad_down_bias,
                grad_norm2_gain,
                grad_norm2_shift,
            ]
        )
        n_small = small.shape[0]
        small_rep = jnp.tile(small.reshape(n_small, groups, shard), (1, 1, groups)).reshape(
            n_small * groups, width
        )
        up_parts = grad_up_bias.shape[0] // shard
        own_group = (jnp.arange(width) // shard == tensor_index)[None, :]
        up_rep = jnp.where(
            own_group, jnp.tile(grad_up_bias.reshape(up_parts, shard), (1, groups)), 0.0
        )
        tail = jnp.concatenate([grad_bias_full, small_rep, up_rep], axis=0)
        tail_rows = tail.shape[0]
        tail = jnp.pad(tail, ((0, -(-tail_rows // 8) * 8 - tail_rows), (0, 0)))
        late = lax.psum_scatter(
            grad_qkv_low.reshape(3 * width, width),
            "dp",
            scatter_dimension=0,
            tiled=True,
        ).astype(jnp.float32)
        joined = jnp.concatenate([late, early, tail], axis=0)
        joined = lax.psum_scatter(
            joined.reshape(joined.shape[0], groups, shard).transpose(1, 0, 2).astype(jnp.bfloat16),
            "tensor",
            scatter_dimension=0,
            tiled=True,
        )[0]
        if halved:
            ffn_grads = tuple(
                dp_double(g.astype(jnp.bfloat16), dp_size).astype(jnp.float32) for g in ffn_grads
            )
            joined, ffn_grads = lax.optimization_barrier((joined, ffn_grads))
        grad_up_weight, grad_down_weight = ffn_grads
        late_rows = late.shape[0]
        early_rows = early.shape[0]
        joined = lax.all_gather(joined, "dp", axis=0, tiled=False).astype(jnp.float32)
        early = joined[:, late_rows : late_rows + early_rows]
        if early_halved:
            order = bit_reversed(dp_size)
            place = [order.index(b) for b in range(dp_size)]
            early = jnp.concatenate([early[p] for p in place], axis=0)
        pieces = [
            joined[:, :late_rows].reshape(-1, shard),
            early.reshape(-1, shard),
            jnp.sum(joined[:, late_rows + early_rows :], axis=0),
        ]
        grad_qkv_weight = pieces[0].reshape(3, width, shard)
        grad_out_weight = pieces[1].T
        tail = pieces[2]
        grad_qkv_bias = tail[:2]
        small_sum = tail[2 : 2 + n_small * groups].reshape(n_small, width)
        grad_up_bias = tail[2 + n_small * groups : 2 + n_small * groups + up_parts].reshape(-1)
        (
            grad_out_bias,
            grad_norm1_gain,
            grad_norm1_shift,
            grad_down_bias,
            grad_norm2_gain,
            grad_norm2_shift,
        ) = [small_sum[i] for i in range(n_small)]
        return (
            layer_out.astype(jnp.bfloat16),
            input_grad,
            grad_qkv_weight,
            grad_qkv_bias,
            grad_out_weight,
            grad_out_bias,
            grad_norm1_gain,
            grad_norm1_shift,
            grad_up_weight,
            grad_up_bias,
            grad_down_weight,
            grad_down_bias,
            grad_norm2_gain,
            grad_norm2_shift,
        )

    return per_device


def solution(mesh):
    placed = (
        P(("dp", "tensor"), None),
        P(("dp", "tensor"), None),
        P("dp"),
        P(None, None, "tensor"),
        P(None, "tensor"),
        P("tensor", None),
        P(),
        P(),
        P(),
        P(None, "tensor"),
        P("tensor"),
        P("tensor", None),
        P(),
        P(),
        P(),
    )
    return jax.shard_map(
        make_per_device(mesh.shape["dp"]),
        mesh=mesh,
        in_specs=placed,
        out_specs=(
            P(("dp", "tensor"), None),
            P(("dp", "tensor"), None),
            P(None, None, "tensor"),
            P(None, "tensor"),
            P("tensor", None),
            P(),
            P(),
            P(),
            P(None, "tensor"),
            P("tensor"),
            P("tensor", None),
            P(),
            P(),
            P(),
        ),
        check_vma=False,
    )
```

```python
import functools

import jax
import jax.numpy as jnp
from jax import lax
from jax.experimental import pallas as pl
from jax.experimental.pallas import tpu as pltpu
from jax.sharding import PartitionSpec as P

HD = 64
LEN = 512


EPS = 1e-12
NEG = -1e30


def layer_norm(values, gain_vec, shift_vec):
    center = values - jnp.mean(values, axis=-1, keepdims=True)
    spread = jnp.mean(center * center, axis=-1, keepdims=True)
    return center * lax.rsqrt(spread + EPS) * gain_vec + shift_vec


def gelu_and_slope(values):
    cdf = 0.5 * (1.0 + lax.erf(values * (2.0 ** -0.5)))
    density = jnp.exp(-0.5 * values * values) * ((2.0 * jnp.pi) ** -0.5)
    return values * cdf, cdf + values * density


def contract(left, right, left_dim, right_dim):
    return lax.dot_general(
        left, right, (((left_dim,), (right_dim,)), ((), ())), preferred_element_type=jnp.float32
    )


def _probs(q, k, length, factor):
    scores = lax.dot_general(q, k, (((1,), (1,)), ((), ())), preferred_element_type=jnp.float32) * factor
    col = lax.broadcasted_iota(jnp.int32, scores.shape, 1)
    scores = jnp.where(col < length, scores, NEG)
    top = jnp.max(scores, axis=1, keepdims=True)
    raised = jnp.exp(scores - top)
    return raised / jnp.sum(raised, axis=1, keepdims=True)


def _fwd_kernel(len_ref, q_ref, k_ref, v_ref, out_ref, *, heads, factor):
    length = len_ref[pl.program_id(0)]
    for h in range(heads):
        cols = slice(h * HD, (h + 1) * HD)
        probs = _probs(q_ref[:, cols], k_ref[:, cols], length, factor)
        out_ref[:, cols] = jnp.dot(
            probs.astype(jnp.bfloat16), v_ref[:, cols], preferred_element_type=jnp.float32
        ).astype(out_ref.dtype)


def _bwd_kernel(len_ref, q_ref, k_ref, v_ref, grad_ref, *rest, heads, factor):
    if len(rest) == 3:
        tokens_ref, out_ref, wgrad_ref = rest
    else:
        (out_ref,), tokens_ref = rest, None
    length = len_ref[pl.program_id(0)]
    for h in range(heads):
        cols = slice(h * HD, (h + 1) * HD)
        q = q_ref[:, cols]
        k = k_ref[:, cols]
        v = v_ref[:, cols]
        g = grad_ref[:, cols]
        probs = _probs(q, k, length, factor)
        prob_grad = lax.dot_general(g, v, (((1,), (1,)), ((), ())), preferred_element_type=jnp.float32)
        row_dot = jnp.sum(prob_grad * probs, axis=1, keepdims=True)
        score_grad = (probs * (prob_grad - row_dot)).astype(jnp.bfloat16)
        out_ref[0, :, cols] = (
            jnp.dot(score_grad, k, preferred_element_type=jnp.float32) * factor
        ).astype(out_ref.dtype)
        out_ref[1, :, cols] = (
            lax.dot_general(score_grad, q, (((0,), (0,)), ((), ())), preferred_element_type=jnp.float32)
            * factor
        ).astype(out_ref.dtype)
        out_ref[2, :, cols] = lax.dot_general(
            probs.astype(jnp.bfloat16), g, (((0,), (0,)), ((), ())), preferred_element_type=jnp.float32
        ).astype(out_ref.dtype)
    if tokens_ref is not None:
        tokens = tokens_ref[...]
        for t in range(3):
            wgrad_ref[t] = lax.dot_general(
                tokens, out_ref[t], (((0,), (0,)), ((), ())), preferred_element_type=jnp.float32
            ).astype(wgrad_ref.dtype)


def attention_forward(queries, keys, values, lengths, factor, pair=2):
    rows, width = queries.shape
    block = pl.BlockSpec((LEN, pair * HD), lambda p, i, n: (p, i))
    return pl.pallas_call(
        functools.partial(_fwd_kernel, heads=pair, factor=factor),
        out_shape=jax.ShapeDtypeStruct((rows, width), jnp.bfloat16),
        grid_spec=pltpu.PrefetchScalarGridSpec(
            num_scalar_prefetch=1,
            grid=(rows // LEN, width // (pair * HD)),
            in_specs=[block] * 3,
            out_specs=block,
        ),
        cost_estimate=pl.CostEstimate(
            flops=4 * rows * LEN * width,
            transcendentals=rows * LEN * width // HD,
            bytes_accessed=4 * rows * width * 2,
        ),
    )(lengths, queries, keys, values)


def attention_backward(queries, keys, values, context_grad, lengths, factor, tokens=None, pair=2):
    rows, width = queries.shape
    block = pl.BlockSpec((LEN, pair * HD), lambda p, i, n: (p, i))
    grad_spec = pl.BlockSpec((3, LEN, pair * HD), lambda p, i, n: (0, p, i))
    grad_shape = jax.ShapeDtypeStruct((3, rows, width), jnp.bfloat16)
    operands = [lengths, queries, keys, values, context_grad]
    in_specs = [block] * 4
    out_specs, out_shape = grad_spec, grad_shape
    if tokens is not None:
        depth = tokens.shape[1]
        operands.append(tokens)
        in_specs.append(pl.BlockSpec((LEN, depth), lambda p, i, n: (p, 0)))
        out_specs = [grad_spec, pl.BlockSpec((3, depth, pair * HD), lambda p, i, n: (0, 0, i))]
        out_shape = [grad_shape, jax.ShapeDtypeStruct((3, depth, width), jnp.bfloat16)]
    return pl.pallas_call(
        functools.partial(_bwd_kernel, heads=pair, factor=factor),
        out_shape=out_shape,
        grid_spec=pltpu.PrefetchScalarGridSpec(
            num_scalar_prefetch=1,
            grid=(rows // LEN, width // (pair * HD)),
            in_specs=in_specs,
            out_specs=out_specs,
        ),
        cost_estimate=pl.CostEstimate(
            flops=16 * rows * LEN * width,
            transcendentals=rows * LEN * width // HD,
            bytes_accessed=10 * rows * width * 2,
        ),
    )(*operands)


def _tn_kernel(left_ref, right_ref, out_ref):
    out_ref[...] = lax.dot_general(
        left_ref[...], right_ref[...], (((0,), (0,)), ((), ())), preferred_element_type=jnp.float32
    )


def tn_matmul(left, right, tile=256):
    depth, rows = left.shape
    cols = right.shape[1]
    return pl.pallas_call(
        _tn_kernel,
        out_shape=jax.ShapeDtypeStruct((rows, cols), jnp.float32),
        grid=(rows // tile,),
        in_specs=[
            pl.BlockSpec((depth, tile), lambda i: (0, i)),
            pl.BlockSpec((depth, cols), lambda i: (0, 0)),
        ],
        out_specs=pl.BlockSpec((tile, cols), lambda i: (i, 0)),
        cost_estimate=pl.CostEstimate(
            flops=2 * depth * rows * cols,
            transcendentals=0,
            bytes_accessed=2 * depth * (rows + cols) + 4 * rows * cols,
        ),
    )(left, right)


def dp_pow2(values, dp_size):
    steps = dp_size.bit_length() - 1
    return dp_size == 1 << steps and values.shape[0] % dp_size == 0


def dp_halve(values, dp_size, sum_dtype=None):
    steps = dp_size.bit_length() - 1
    index = lax.axis_index("dp")
    link = values.dtype
    kept = values if sum_dtype is None else values.astype(sum_dtype)
    for step in range(steps):
        bit = (index >> step) & 1
        half = kept.shape[0] // 2
        keep = lax.dynamic_slice_in_dim(kept, bit * half, half)
        give = lax.dynamic_slice_in_dim(kept, (1 - bit) * half, half).astype(link)
        got = lax.ppermute(give, "dp", [(i, i ^ (1 << step)) for i in range(dp_size)])
        kept = keep + got.astype(kept.dtype)
    return kept


def bit_reversed(count):
    steps = count.bit_length() - 1
    return [int(format(i, f"0{steps}b")[::-1], 2) if steps else 0 for i in range(count)]


def dp_double(kept, dp_size):
    steps = dp_size.bit_length() - 1
    index = lax.axis_index("dp")
    for step in reversed(range(steps)):
        bit = (index >> step) & 1
        got = lax.ppermute(kept, "dp", [(i, i ^ (1 << step)) for i in range(dp_size)])
        kept = jnp.concatenate(
            [jnp.where(bit == 0, kept, got), jnp.where(bit == 0, got, kept)]
        )
    return kept


def make_per_device(dp_size):
    def per_device(
        tokens,
        out_grad,
        lengths,
        qkv_weight,
        qkv_bias,
        out_weight,
        out_bias,
        norm1_gain,
        norm1_shift,
        up_weight,
        up_bias,
        down_weight,
        down_bias,
        norm2_gain,
        norm2_shift,
    ):
        rows, width = tokens.shape
        shard = qkv_weight.shape[2]
        groups = width // shard
        passages = rows // LEN
        factor = HD ** (-0.5)

        half_rows = -(-(2 * width + 2) // 8) * 8
        first_half = jnp.pad(
            jnp.concatenate([qkv_weight[0], qkv_weight[1], qkv_bias], axis=0),
            ((0, half_rows - 2 * width - 2), (0, 0)),
        )
        second_half = jnp.pad(
            jnp.concatenate([qkv_weight[2], out_weight.T], axis=0),
            ((0, half_rows - 2 * width), (0, 0)),
        )
        dp_index = lax.axis_index("dp")
        parity = dp_index % 2
        mine = jnp.where(parity == 0, first_half, second_half)
        mine = lax.all_gather(mine, "tensor", axis=0, tiled=False)
        other = lax.ppermute(mine, "dp", [(i, i ^ 1) for i in range(dp_size)])
        first_half = jnp.where(parity == 0, mine, other)
        second_half = jnp.where(parity == 0, other, mine)
        query_weight = first_half[:, :width]
        key_weight = first_half[:, width : 2 * width]
        query_bias = first_half[:, 2 * width]
        value_bias = first_half[:, 2 * width + 1]
        value_weight = second_half[:, :width]
        proj_blocks = second_half[:, width : 2 * width]

        tensor_index = lax.axis_index("tensor")
        own_lengths = lax.dynamic_slice_in_dim(lengths, tensor_index * passages, passages)

        own_tokens = tokens.astype(jnp.float32)
        def project(weight, bias=None):
            out = jnp.einsum("rd,gdj->rgj", tokens, weight, preferred_element_type=jnp.float32)
            out = out if bias is None else out + bias
            return out.astype(jnp.bfloat16).reshape(rows, width)

        query_low = project(query_weight, query_bias)
        key_low = project(key_weight)
        value_low = project(value_weight, value_bias)
        context_low = attention_forward(query_low, key_low, value_low, own_lengths, factor)
        attn_out = jnp.einsum(
            "rgj,gcj->rc",
            context_low.reshape(rows, groups, shard),
            proj_blocks,
            preferred_element_type=jnp.float32,
        )
        middle, norm1_back = jax.vjp(
            layer_norm, own_tokens + attn_out + out_bias, norm1_gain, norm1_shift
        )
        middle_low = middle.astype(jnp.bfloat16)
        ffn_rows = lax.all_gather(middle_low, "tensor", axis=0, tiled=True)
        pre_act = jnp.dot(ffn_rows, up_weight, preferred_element_type=jnp.float32) + up_bias
        activated, gelu_slope = gelu_and_slope(pre_act)
        hidden = activated.astype(jnp.bfloat16)
        ffn_out = lax.psum_scatter(
            jnp.dot(hidden, down_weight, preferred_element_type=jnp.float32).astype(jnp.bfloat16),
            "tensor",
            scatter_dimension=0,
            tiled=True,
        ).astype(jnp.float32)
        layer_out, norm2_back = jax.vjp(
            layer_norm, middle + ffn_out + down_bias, norm2_gain, norm2_shift
        )
        second_grad, grad_norm2_gain, grad_norm2_shift = norm2_back(out_grad.astype(jnp.float32))
        branch_grad = second_grad.astype(jnp.bfloat16)
        grad_down_bias = jnp.sum(branch_grad, axis=0, dtype=jnp.float32)
        branch_rows = lax.all_gather(branch_grad, "tensor", axis=0, tiled=True)
        hidden_grad = contract(branch_rows, down_weight, 1, 1)
        grad_down_weight = tn_matmul(hidden, branch_rows)
        pre_grad = (hidden_grad * gelu_slope).astype(jnp.bfloat16)
        grad_up_bias = jnp.sum(pre_grad, axis=0, dtype=jnp.float32)
        grad_up_weight = tn_matmul(ffn_rows, pre_grad)
        ffn_grads = (grad_up_weight, grad_down_weight)
        halved = all(dp_pow2(g, dp_size) for g in ffn_grads)
        if halved:
            ffn_grads = tuple(
                dp_halve(g.astype(jnp.bfloat16), dp_size, jnp.float32) for g in ffn_grads
            )
        else:
            ffn_grads = lax.psum(ffn_grads, "dp")
        middle_part = lax.psum_scatter(
            contract(pre_grad, up_weight, 1, 1).astype(jnp.bfloat16),
            "tensor",
            scatter_dimension=0,
            tiled=True,
        ).astype(jnp.float32)
        first_grad, grad_norm1_gain, grad_norm1_shift = norm1_back(second_grad + middle_part)
        attn_grad = first_grad.astype(jnp.bfloat16)
        grad_out_bias = jnp.sum(attn_grad, axis=0, dtype=jnp.float32)
        context_grad = (
            jnp.einsum("rc,gcj->rgj", attn_grad, proj_blocks, preferred_element_type=jnp.float32)
            .astype(jnp.bfloat16)
            .reshape(rows, width)
        )
        early = contract(attn_grad, context_low, 0, 0)
        early_halved = dp_pow2(early, dp_size)
        if early_halved:
            early = dp_halve(early.astype(jnp.bfloat16), dp_size, jnp.float32)
        else:
            early = lax.psum_scatter(early, "dp", scatter_dimension=0, tiled=True)
        if passages == 1:
            proj_grad, grad_qkv_low = attention_backward(
                query_low, key_low, value_low, context_grad, own_lengths, factor, tokens
            )
            grad_qkv_low, ffn_grads = lax.optimization_barrier((grad_qkv_low, ffn_grads))
        else:
            proj_grad = attention_backward(
                query_low, key_low, value_low, context_grad, own_lengths, factor
            )
            grad_qkv_low = jnp.einsum(
                "rd,kre->kde", tokens, proj_grad, preferred_element_type=jnp.float32
            ).astype(jnp.bfloat16)
        grad_bias_full = jnp.sum(proj_grad[0::2], axis=1, dtype=jnp.float32)

        def back_project(grad, weight):
            return jnp.einsum(
                "rgj,gdj->rd",
                grad.reshape(rows, groups, shard),
                weight,
                preferred_element_type=jnp.float32,
            )

        input_part = (
            back_project(proj_grad[0], query_weight)
            + back_project(proj_grad[1], key_weight)
            + back_project(proj_grad[2], value_weight)
        )
        input_grad = (first_grad + input_part).astype(jnp.bfloat16)

        small = jnp.stack(
            [
                grad_out_bias,
                grad_norm1_gain,
                grad_norm1_shift,
                grad_down_bias,
                grad_norm2_gain,
                grad_norm2_shift,
            ]
        )
        n_small = small.shape[0]
        small_rep = jnp.tile(small.reshape(n_small, groups, shard), (1, 1, groups)).reshape(
            n_small * groups, width
        )
        up_parts = grad_up_bias.shape[0] // shard
        own_group = (jnp.arange(width) // shard == tensor_index)[None, :]
        up_rep = jnp.where(
            own_group, jnp.tile(grad_up_bias.reshape(up_parts, shard), (1, groups)), 0.0
        )
        tail = jnp.concatenate([grad_bias_full, small_rep, up_rep], axis=0)
        tail_rows = tail.shape[0]
        tail = jnp.pad(tail, ((0, -(-tail_rows // 8) * 8 - tail_rows), (0, 0)))
        late = lax.psum_scatter(
            grad_qkv_low.reshape(3 * width, width),
            "dp",
            scatter_dimension=0,
            tiled=True,
        ).astype(jnp.float32)
        joined = jnp.concatenate([late, early, tail], axis=0)
        joined = lax.psum_scatter(
            joined.reshape(joined.shape[0], groups, shard).transpose(1, 0, 2).astype(jnp.bfloat16),
            "tensor",
            scatter_dimension=0,
            tiled=True,
        )[0]
        if halved:
            ffn_grads = tuple(
                dp_double(g.astype(jnp.bfloat16), dp_size).astype(jnp.float32) for g in ffn_grads
            )
            joined, ffn_grads = lax.optimization_barrier((joined, ffn_grads))
        grad_up_weight, grad_down_weight = ffn_grads
        late_rows = late.shape[0]
        early_rows = early.shape[0]
        joined = lax.all_gather(joined, "dp", axis=0, tiled=False).astype(jnp.float32)
        early = joined[:, late_rows : late_rows + early_rows]
        if early_halved:
            order = bit_reversed(dp_size)
            place = [order.index(b) for b in range(dp_size)]
            early = jnp.concatenate([early[p] for p in place], axis=0)
        pieces = [
            joined[:, :late_rows].reshape(-1, shard),
            early.reshape(-1, shard),
            jnp.sum(joined[:, late_rows + early_rows :], axis=0),
        ]
        grad_qkv_weight = pieces[0].reshape(3, width, shard)
        grad_out_weight = pieces[1].T
        tail = pieces[2]
        grad_qkv_bias = tail[:2]
        small_sum = tail[2 : 2 + n_small * groups].reshape(n_small, width)
        grad_up_bias = tail[2 + n_small * groups : 2 + n_small * groups + up_parts].reshape(-1)
        (
            grad_out_bias,
            grad_norm1_gain,
            grad_norm1_shift,
            grad_down_bias,
            grad_norm2_gain,
            grad_norm2_shift,
        ) = [small_sum[i] for i in range(n_small)]
        return (
            layer_out.astype(jnp.bfloat16),
            input_grad,
            grad_qkv_weight,
            grad_qkv_bias,
            grad_out_weight,
            grad_out_bias,
            grad_norm1_gain,
            grad_norm1_shift,
            grad_up_weight,
            grad_up_bias,
            grad_down_weight,
            grad_down_bias,
            grad_norm2_gain,
            grad_norm2_shift,
        )

    return per_device


def solution(mesh):
    placed = (
        P(("dp", "tensor"), None),
        P(("dp", "tensor"), None),
        P("dp"),
        P(None, None, "tensor"),
        P(None, "tensor"),
        P("tensor", None),
        P(),
        P(),
        P(),
        P(None, "tensor"),
        P("tensor"),
        P("tensor", None),
        P(),
        P(),
        P(),
    )
    return jax.shard_map(
        make_per_device(mesh.shape["dp"]),
        mesh=mesh,
        in_specs=placed,
        out_specs=(
            P(("dp", "tensor"), None),
            P(("dp", "tensor"), None),
            P(None, None, "tensor"),
            P(None, "tensor"),
            P("tensor", None),
            P(),
            P(),
            P(),
            P(None, "tensor"),
            P("tensor"),
            P("tensor", None),
            P(),
            P(),
            P(),
        ),
        check_vma=False,
    )
```

```python
import functools

import jax
import jax.numpy as jnp
from jax import lax
from jax.experimental import pallas as pl
from jax.experimental.pallas import tpu as pltpu
from jax.sharding import PartitionSpec as P

HD = 64
LEN = 512


EPS = 1e-12
NEG = -1e30


def layer_norm(values, gain_vec, shift_vec):
    center = values - jnp.mean(values, axis=-1, keepdims=True)
    spread = jnp.mean(center * center, axis=-1, keepdims=True)
    return center * lax.rsqrt(spread + EPS) * gain_vec + shift_vec


def gelu_and_slope(values):
    cdf = 0.5 * (1.0 + lax.erf(values * (2.0 ** -0.5)))
    density = jnp.exp(-0.5 * values * values) * ((2.0 * jnp.pi) ** -0.5)
    return values * cdf, cdf + values * density


def contract(left, right, left_dim, right_dim):
    return lax.dot_general(
        left, right, (((left_dim,), (right_dim,)), ((), ())), preferred_element_type=jnp.float32
    )


def _probs(q, k, length, factor):
    scores = lax.dot_general(q, k, (((1,), (1,)), ((), ())), preferred_element_type=jnp.float32) * factor
    col = lax.broadcasted_iota(jnp.int32, scores.shape, 1)
    scores = jnp.where(col < length, scores, NEG)
    top = jnp.max(scores, axis=1, keepdims=True)
    raised = jnp.exp(scores - top)
    return raised * (1.0 / jnp.sum(raised, axis=1, keepdims=True))


def _fwd_kernel(len_ref, q_ref, k_ref, v_ref, out_ref, *, heads, factor):
    length = len_ref[pl.program_id(0)]
    for h in range(heads):
        cols = slice(h * HD, (h + 1) * HD)
        probs = _probs(q_ref[:, cols], k_ref[:, cols], length, factor)
        out_ref[:, cols] = jnp.dot(
            probs.astype(jnp.bfloat16), v_ref[:, cols], preferred_element_type=jnp.float32
        ).astype(out_ref.dtype)


def _bwd_kernel(len_ref, q_ref, k_ref, v_ref, grad_ref, *rest, heads, factor):
    if len(rest) == 3:
        tokens_ref, out_ref, wgrad_ref = rest
    else:
        (out_ref,), tokens_ref = rest, None
    length = len_ref[pl.program_id(0)]
    for h in range(heads):
        cols = slice(h * HD, (h + 1) * HD)
        q = q_ref[:, cols]
        k = k_ref[:, cols]
        v = v_ref[:, cols]
        g = grad_ref[:, cols]
        probs = _probs(q, k, length, factor)
        prob_grad = lax.dot_general(g, v, (((1,), (1,)), ((), ())), preferred_element_type=jnp.float32)
        row_dot = jnp.sum(prob_grad * probs, axis=1, keepdims=True)
        score_grad = (probs * (prob_grad - row_dot)).astype(jnp.bfloat16)
        out_ref[0, :, cols] = (
            jnp.dot(score_grad, k, preferred_element_type=jnp.float32) * factor
        ).astype(out_ref.dtype)
        out_ref[1, :, cols] = (
            lax.dot_general(score_grad, q, (((0,), (0,)), ((), ())), preferred_element_type=jnp.float32)
            * factor
        ).astype(out_ref.dtype)
        out_ref[2, :, cols] = lax.dot_general(
            probs.astype(jnp.bfloat16), g, (((0,), (0,)), ((), ())), preferred_element_type=jnp.float32
        ).astype(out_ref.dtype)
    if tokens_ref is not None:
        tokens = tokens_ref[...]
        for t in range(3):
            wgrad_ref[t] = lax.dot_general(
                tokens, out_ref[t], (((0,), (0,)), ((), ())), preferred_element_type=jnp.float32
            ).astype(wgrad_ref.dtype)


def attention_forward(queries, keys, values, lengths, factor, pair=2):
    rows, width = queries.shape
    block = pl.BlockSpec((LEN, pair * HD), lambda p, i, n: (p, i))
    return pl.pallas_call(
        functools.partial(_fwd_kernel, heads=pair, factor=factor),
        out_shape=jax.ShapeDtypeStruct((rows, width), jnp.bfloat16),
        grid_spec=pltpu.PrefetchScalarGridSpec(
            num_scalar_prefetch=1,
            grid=(rows // LEN, width // (pair * HD)),
            in_specs=[block] * 3,
            out_specs=block,
        ),
        cost_estimate=pl.CostEstimate(
            flops=4 * rows * LEN * width,
            transcendentals=rows * LEN * width // HD,
            bytes_accessed=4 * rows * width * 2,
        ),
    )(lengths, queries, keys, values)


def attention_backward(queries, keys, values, context_grad, lengths, factor, tokens=None, pair=2):
    rows, width = queries.shape
    block = pl.BlockSpec((LEN, pair * HD), lambda p, i, n: (p, i))
    grad_spec = pl.BlockSpec((3, LEN, pair * HD), lambda p, i, n: (0, p, i))
    grad_shape = jax.ShapeDtypeStruct((3, rows, width), jnp.bfloat16)
    operands = [lengths, queries, keys, values, context_grad]
    in_specs = [block] * 4
    out_specs, out_shape = grad_spec, grad_shape
    if tokens is not None:
        depth = tokens.shape[1]
        operands.append(tokens)
        in_specs.append(pl.BlockSpec((LEN, depth), lambda p, i, n: (p, 0)))
        out_specs = [grad_spec, pl.BlockSpec((3, depth, pair * HD), lambda p, i, n: (0, 0, i))]
        out_shape = [grad_shape, jax.ShapeDtypeStruct((3, depth, width), jnp.bfloat16)]
    return pl.pallas_call(
        functools.partial(_bwd_kernel, heads=pair, factor=factor),
        out_shape=out_shape,
        grid_spec=pltpu.PrefetchScalarGridSpec(
            num_scalar_prefetch=1,
            grid=(rows // LEN, width // (pair * HD)),
            in_specs=in_specs,
            out_specs=out_specs,
        ),
        cost_estimate=pl.CostEstimate(
            flops=16 * rows * LEN * width,
            transcendentals=rows * LEN * width // HD,
            bytes_accessed=10 * rows * width * 2,
        ),
    )(*operands)


def _tn_kernel(left_ref, right_ref, out_ref):
    out_ref[...] = lax.dot_general(
        left_ref[...], right_ref[...], (((0,), (0,)), ((), ())), preferred_element_type=jnp.float32
    )


def tn_matmul(left, right, tile=256):
    depth, rows = left.shape
    cols = right.shape[1]
    return pl.pallas_call(
        _tn_kernel,
        out_shape=jax.ShapeDtypeStruct((rows, cols), jnp.float32),
        grid=(rows // tile,),
        in_specs=[
            pl.BlockSpec((depth, tile), lambda i: (0, i)),
            pl.BlockSpec((depth, cols), lambda i: (0, 0)),
        ],
        out_specs=pl.BlockSpec((tile, cols), lambda i: (i, 0)),
        cost_estimate=pl.CostEstimate(
            flops=2 * depth * rows * cols,
            transcendentals=0,
            bytes_accessed=2 * depth * (rows + cols) + 4 * rows * cols,
        ),
    )(left, right)


def dp_pow2(values, dp_size):
    steps = dp_size.bit_length() - 1
    return dp_size == 1 << steps and values.shape[0] % dp_size == 0


def dp_halve(values, dp_size, sum_dtype=None):
    steps = dp_size.bit_length() - 1
    index = lax.axis_index("dp")
    link = values.dtype
    kept = values if sum_dtype is None else values.astype(sum_dtype)
    for step in range(steps):
        bit = (index >> step) & 1
        half = kept.shape[0] // 2
        keep = lax.dynamic_slice_in_dim(kept, bit * half, half)
        give = lax.dynamic_slice_in_dim(kept, (1 - bit) * half, half).astype(link)
        got = lax.ppermute(give, "dp", [(i, i ^ (1 << step)) for i in range(dp_size)])
        kept = keep + got.astype(kept.dtype)
    return kept


def bit_reversed(count):
    steps = count.bit_length() - 1
    return [int(format(i, f"0{steps}b")[::-1], 2) if steps else 0 for i in range(count)]


def dp_double(kept, dp_size):
    steps = dp_size.bit_length() - 1
    index = lax.axis_index("dp")
    for step in reversed(range(steps)):
        bit = (index >> step) & 1
        got = lax.ppermute(kept, "dp", [(i, i ^ (1 << step)) for i in range(dp_size)])
        kept = jnp.concatenate(
            [jnp.where(bit == 0, kept, got), jnp.where(bit == 0, got, kept)]
        )
    return kept


def make_per_device(dp_size):
    def per_device(
        tokens,
        out_grad,
        lengths,
        qkv_weight,
        qkv_bias,
        out_weight,
        out_bias,
        norm1_gain,
        norm1_shift,
        up_weight,
        up_bias,
        down_weight,
        down_bias,
        norm2_gain,
        norm2_shift,
    ):
        rows, width = tokens.shape
        shard = qkv_weight.shape[2]
        groups = width // shard
        passages = rows // LEN
        factor = HD ** (-0.5)

        half_rows = -(-(2 * width + 2) // 8) * 8
        first_half = jnp.pad(
            jnp.concatenate([qkv_weight[0], qkv_weight[1], qkv_bias], axis=0),
            ((0, half_rows - 2 * width - 2), (0, 0)),
        )
        second_half = jnp.pad(
            jnp.concatenate([qkv_weight[2], out_weight.T], axis=0),
            ((0, half_rows - 2 * width), (0, 0)),
        )
        dp_index = lax.axis_index("dp")
        parity = dp_index % 2
        mine = jnp.where(parity == 0, first_half, second_half)
        mine = lax.all_gather(mine, "tensor", axis=0, tiled=False)
        other = lax.ppermute(mine, "dp", [(i, i ^ 1) for i in range(dp_size)])
        first_half = jnp.where(parity == 0, mine, other)
        second_half = jnp.where(parity == 0, other, mine)
        query_weight = first_half[:, :width]
        key_weight = first_half[:, width : 2 * width]
        query_bias = first_half[:, 2 * width]
        value_bias = first_half[:, 2 * width + 1]
        value_weight = second_half[:, :width]
        proj_blocks = second_half[:, width : 2 * width]

        tensor_index = lax.axis_index("tensor")
        own_lengths = lax.dynamic_slice_in_dim(lengths, tensor_index * passages, passages)

        own_tokens = tokens.astype(jnp.float32)
        def project(weight, bias=None):
            out = jnp.einsum("rd,gdj->rgj", tokens, weight, preferred_element_type=jnp.float32)
            out = out if bias is None else out + bias
            return out.astype(jnp.bfloat16).reshape(rows, width)

        query_low = project(query_weight, query_bias)
        key_low = project(key_weight)
        value_low = project(value_weight, value_bias)
        context_low = attention_forward(query_low, key_low, value_low, own_lengths, factor)
        attn_out = jnp.einsum(
            "rgj,gcj->rc",
            context_low.reshape(rows, groups, shard),
            proj_blocks,
            preferred_element_type=jnp.float32,
        )
        middle, norm1_back = jax.vjp(
            layer_norm, own_tokens + attn_out + out_bias, norm1_gain, norm1_shift
        )
        middle_low = middle.astype(jnp.bfloat16)
        ffn_rows = lax.all_gather(middle_low, "tensor", axis=0, tiled=True)
        pre_act = jnp.dot(ffn_rows, up_weight, preferred_element_type=jnp.float32) + up_bias
        activated, gelu_slope = gelu_and_slope(pre_act)
        hidden = activated.astype(jnp.bfloat16)
        ffn_out = lax.psum_scatter(
            jnp.dot(hidden, down_weight, preferred_element_type=jnp.float32).astype(jnp.bfloat16),
            "tensor",
            scatter_dimension=0,
            tiled=True,
        ).astype(jnp.float32)
        layer_out, norm2_back = jax.vjp(
            layer_norm, middle + ffn_out + down_bias, norm2_gain, norm2_shift
        )
        second_grad, grad_norm2_gain, grad_norm2_shift = norm2_back(out_grad.astype(jnp.float32))
        branch_grad = second_grad.astype(jnp.bfloat16)
        grad_down_bias = jnp.sum(branch_grad, axis=0, dtype=jnp.float32)
        branch_rows = lax.all_gather(branch_grad, "tensor", axis=0, tiled=True)
        hidden_grad = contract(branch_rows, down_weight, 1, 1)
        grad_down_weight = tn_matmul(hidden, branch_rows)
        pre_grad = (hidden_grad * gelu_slope).astype(jnp.bfloat16)
        grad_up_bias = jnp.sum(pre_grad, axis=0, dtype=jnp.float32)
        grad_up_weight = tn_matmul(ffn_rows, pre_grad)
        ffn_grads = (grad_up_weight, grad_down_weight)
        halved = all(dp_pow2(g, dp_size) for g in ffn_grads)
        if halved:
            ffn_grads = tuple(
                dp_halve(g.astype(jnp.bfloat16), dp_size, jnp.float32) for g in ffn_grads
            )
        else:
            ffn_grads = lax.psum(ffn_grads, "dp")
        middle_part = lax.psum_scatter(
            contract(pre_grad, up_weight, 1, 1).astype(jnp.bfloat16),
            "tensor",
            scatter_dimension=0,
            tiled=True,
        ).astype(jnp.float32)
        first_grad, grad_norm1_gain, grad_norm1_shift = norm1_back(second_grad + middle_part)
        attn_grad = first_grad.astype(jnp.bfloat16)
        grad_out_bias = jnp.sum(attn_grad, axis=0, dtype=jnp.float32)
        context_grad = (
            jnp.einsum("rc,gcj->rgj", attn_grad, proj_blocks, preferred_element_type=jnp.float32)
            .astype(jnp.bfloat16)
            .reshape(rows, width)
        )
        early = contract(attn_grad, context_low, 0, 0)
        early_halved = dp_pow2(early, dp_size)
        if early_halved:
            early = dp_halve(early.astype(jnp.bfloat16), dp_size, jnp.float32)
        else:
            early = lax.psum_scatter(early, "dp", scatter_dimension=0, tiled=True)
        if passages == 1:
            proj_grad, grad_qkv_low = attention_backward(
                query_low, key_low, value_low, context_grad, own_lengths, factor, tokens
            )
            grad_qkv_low, ffn_grads = lax.optimization_barrier((grad_qkv_low, ffn_grads))
        else:
            proj_grad = attention_backward(
                query_low, key_low, value_low, context_grad, own_lengths, factor
            )
            grad_qkv_low = jnp.einsum(
                "rd,kre->kde", tokens, proj_grad, preferred_element_type=jnp.float32
            ).astype(jnp.bfloat16)
        grad_bias_full = jnp.sum(proj_grad[0::2], axis=1, dtype=jnp.float32)

        def back_project(grad, weight):
            return jnp.einsum(
                "rgj,gdj->rd",
                grad.reshape(rows, groups, shard),
                weight,
                preferred_element_type=jnp.float32,
            )

        input_part = (
            back_project(proj_grad[0], query_weight)
            + back_project(proj_grad[1], key_weight)
            + back_project(proj_grad[2], value_weight)
        )
        input_grad = (first_grad + input_part).astype(jnp.bfloat16)

        small = jnp.stack(
            [
                grad_out_bias,
                grad_norm1_gain,
                grad_norm1_shift,
                grad_down_bias,
                grad_norm2_gain,
                grad_norm2_shift,
            ]
        )
        n_small = small.shape[0]
        small_rep = jnp.tile(small.reshape(n_small, groups, shard), (1, 1, groups)).reshape(
            n_small * groups, width
        )
        up_parts = grad_up_bias.shape[0] // shard
        own_group = (jnp.arange(width) // shard == tensor_index)[None, :]
        up_rep = jnp.where(
            own_group, jnp.tile(grad_up_bias.reshape(up_parts, shard), (1, groups)), 0.0
        )
        tail = jnp.concatenate([grad_bias_full, small_rep, up_rep], axis=0)
        tail_rows = tail.shape[0]
        tail = jnp.pad(tail, ((0, -(-tail_rows // 8) * 8 - tail_rows), (0, 0)))
        late = lax.psum_scatter(
            grad_qkv_low.reshape(3 * width, width),
            "dp",
            scatter_dimension=0,
            tiled=True,
        ).astype(jnp.float32)
        joined = jnp.concatenate([late, early, tail], axis=0)
        joined = lax.psum_scatter(
            joined.reshape(joined.shape[0], groups, shard).transpose(1, 0, 2).astype(jnp.bfloat16),
            "tensor",
            scatter_dimension=0,
            tiled=True,
        )[0]
        if halved:
            ffn_grads = tuple(
                dp_double(g.astype(jnp.bfloat16), dp_size).astype(jnp.float32) for g in ffn_grads
            )
            joined, ffn_grads = lax.optimization_barrier((joined, ffn_grads))
        grad_up_weight, grad_down_weight = ffn_grads
        late_rows = late.shape[0]
        early_rows = early.shape[0]
        joined = lax.all_gather(joined, "dp", axis=0, tiled=False).astype(jnp.float32)
        early = joined[:, late_rows : late_rows + early_rows]
        if early_halved:
            order = bit_reversed(dp_size)
            place = [order.index(b) for b in range(dp_size)]
            early = jnp.concatenate([early[p] for p in place], axis=0)
        pieces = [
            joined[:, :late_rows].reshape(-1, shard),
            early.reshape(-1, shard),
            jnp.sum(joined[:, late_rows + early_rows :], axis=0),
        ]
        grad_qkv_weight = pieces[0].reshape(3, width, shard)
        grad_out_weight = pieces[1].T
        tail = pieces[2]
        grad_qkv_bias = tail[:2]
        small_sum = tail[2 : 2 + n_small * groups].reshape(n_small, width)
        grad_up_bias = tail[2 + n_small * groups : 2 + n_small * groups + up_parts].reshape(-1)
        (
            grad_out_bias,
            grad_norm1_gain,
            grad_norm1_shift,
            grad_down_bias,
            grad_norm2_gain,
            grad_norm2_shift,
        ) = [small_sum[i] for i in range(n_small)]
        return (
            layer_out.astype(jnp.bfloat16),
            input_grad,
            grad_qkv_weight,
            grad_qkv_bias,
            grad_out_weight,
            grad_out_bias,
            grad_norm1_gain,
            grad_norm1_shift,
            grad_up_weight,
            grad_up_bias,
            grad_down_weight,
            grad_down_bias,
            grad_norm2_gain,
            grad_norm2_shift,
        )

    return per_device


def solution(mesh):
    placed = (
        P(("dp", "tensor"), None),
        P(("dp", "tensor"), None),
        P("dp"),
        P(None, None, "tensor"),
        P(None, "tensor"),
        P("tensor", None),
        P(),
        P(),
        P(),
        P(None, "tensor"),
        P("tensor"),
        P("tensor", None),
        P(),
        P(),
        P(),
    )
    return jax.shard_map(
        make_per_device(mesh.shape["dp"]),
        mesh=mesh,
        in_specs=placed,
        out_specs=(
            P(("dp", "tensor"), None),
            P(("dp", "tensor"), None),
            P(None, None, "tensor"),
            P(None, "tensor"),
            P("tensor", None),
            P(),
            P(),
            P(),
            P(None, "tensor"),
            P("tensor"),
            P("tensor", None),
            P(),
            P(),
            P(),
        ),
        check_vma=False,
    )
```
